256 devices in a mesh: dp: 2 (over y_hi), ctx: 64 (over y_lo, x, z), head: 2 (over core).
Axes of the slice: x: 4, y: 4 (y_hi: 2, y_lo: 2; y = y_hi * 2 + y_lo), z: 8, core: 2. Of those that a mesh axis runs over, the one named last changes fastest.
Arguments:
- hidden_in: bfloat16 [2, 8192, 4096], P('dp', 'ctx'), may hold values from -16 to 16
- proj_weight: bfloat16 [4096, 2, 256], P(('dp', 'ctx'), None, 'head'), may hold values from -0.0029296875 to 0.0029296875
- values_in: bfloat16 [2, 8192, 4096], P('dp', 'ctx', 'head'), may hold values from -6 to 6
- gate_in: bfloat16 [2, 8192, 4096], P('dp', 'ctx', 'head'), may hold values from -6 to 6
- log_decay: float32 [2, 64, 8192], P('dp', 'head', 'ctx'), may hold values from -1 to 0, as said below
- skip_gain: float32 [64], P('head'), may hold values from 0.5 to 2
- grad_out: bfloat16 [2, 8192, 4096], P('dp', 'ctx', 'head'), may hold values from -6 to 6
Outputs:
- grad_input: bfloat16 [2, 8192, 4096], P('dp', 'ctx', 'head')
- grad_values: bfloat16 [2, 8192, 4096], P('dp', 'ctx', 'head')
- grad_gate: bfloat16 [2, 8192, 4096], P('dp', 'ctx', 'head')
- grad_proj: float32 [4096, 2, 256], P(('dp', 'ctx'), None, 'head')
The draws below stay inside these ranges and needn't reach their ends.
Inputs may be any that keep to these rules, and one draw needn't show every extreme that they name: `log_decay`: logarithms of the per-token decay of each head's state; all values are at most zero.
All inputs are finite; a program needn't handle non-finite values.
Results may differ from the reference program's by a relative error of at most 0.011.
Values may be sent and summed in bfloat16 or wider, within the bound.
No kernel may reach another device: no remote copies, remote signals or barrier semaphores. Data moves between devices by JAX's collectives and lax.ppermute only.
A program may use at most 192 MiB of HBM per device.

```python
import math
import jax
import jax.numpy as jnp
from jax import lax

WIDTH = 4096
SHARD_MIXERS = 64
HEAD_DIM = 64
STATE = 64
GROUPS = 4
SPAN = 128
BATCH_SIZE = 2
CONTEXT_SPAN = 8192


def draw_log_decay(key, part):
    sampler_seeds = jax.random.split(key, 12)
    shape_heads = (BATCH_SIZE, SHARD_MIXERS, 1)
    shape_full = (BATCH_SIZE, SHARD_MIXERS, CONTEXT_SPAN)
    fast_rate = jnp.exp(jax.random.uniform(sampler_seeds[0], shape_heads, jnp.float32, math.log(0.02), math.log(0.034)))
    slow_rate = jax.random.uniform(sampler_seeds[1], shape_heads, jnp.float32, 0.1, 0.5) / CONTEXT_SPAN
    steady_rate = jax.random.uniform(sampler_seeds[8], shape_heads, jnp.float32, 0.0015, 0.0024)
    sparse_rate = jax.random.uniform(sampler_seeds[9], shape_heads, jnp.float32, 0.5, 2.0) * 1e-05
    edge_fast = 0.15
    edge_steady = 0.3
    edge_sparse = 0.5
    kind_draw = jax.random.uniform(sampler_seeds[2], shape_heads, jnp.float32)
    discretize_deltas = jnp.where(kind_draw < edge_fast, fast_rate, jnp.where(kind_draw < edge_steady, steady_rate, jnp.where(kind_draw < edge_sparse, sparse_rate, slow_rate)))
    sparse_heads = jnp.logical_and(kind_draw >= edge_steady, kind_draw < edge_sparse)
    uneven_spread = jnp.exp(jax.random.uniform(sampler_seeds[3], shape_full, jnp.float32, -0.7, 0.7))
    segment_bounds = jnp.exp(jax.random.uniform(sampler_seeds[4], (BATCH_SIZE, SHARD_MIXERS, CONTEXT_SPAN // SPAN, 1), jnp.float32, -0.7, 0.7))
    segment_bounds = jnp.broadcast_to(segment_bounds, (BATCH_SIZE, SHARD_MIXERS, CONTEXT_SPAN // SPAN, SPAN)).reshape(shape_full)
    cluster_partition = jax.random.uniform(sampler_seeds[5], shape_full, jnp.float32) < 3.0 / CONTEXT_SPAN
    objective_scores = jnp.log(jax.random.uniform(sampler_seeds[6], shape_full, jnp.float32, 0.5, 0.8))
    positions = jnp.arange(CONTEXT_SPAN, dtype=jnp.int32)[None, None, :]
    third_len = CONTEXT_SPAN // 3
    run_starts = jax.random.randint(sampler_seeds[10], (BATCH_SIZE, SHARD_MIXERS, 3), 0, third_len - 9, dtype=jnp.int32) + jnp.arange(3, dtype=jnp.int32)[None, None, :] * third_len
    in_runs = jnp.zeros(shape_full, dtype=bool)
    for run_index in range(3):
        run_first = run_starts[:, :, run_index:run_index + 1]
        in_runs = jnp.logical_or(in_runs, jnp.logical_and(positions >= run_first, positions < run_first + 9))
    run_logs = jnp.log(jax.random.uniform(sampler_seeds[11], shape_full, jnp.float32, 0.38, 0.42))
    smooth_part = -discretize_deltas * uneven_spread * segment_bounds + jnp.where(cluster_partition, objective_scores, 0.0)
    mixed_logs = jnp.where(jnp.logical_and(sparse_heads, in_runs), run_logs, smooth_part)
    return jnp.maximum(mixed_logs, -1.0)


def spiked(values, stream_key, source, target, blocks, factor):
    owner, partner = [(jnp.arange(values.shape[dim]) // (values.shape[dim] // blocks)).reshape([-1 if axis == dim else 1 for axis in range(values.ndim)]) for dim in (source, target)]
    chosen = jax.random.permutation(stream_key, blocks)[partner]
    strong = (owner == chosen) | (owner == (partner + blocks // 2) % blocks)
    return jnp.where(strong, factor * values, values)


def levels(own_key, extent, pieces, smallest, high):
    gain, own = 1.0, jax.random.fold_in(own_key, 6)
    for position, parts in pieces:
        steps = jnp.exp(jax.random.uniform(jax.random.fold_in(own, position), (parts,), jnp.float32, smallest / len(pieces), high / len(pieces)))
        gain = gain * jnp.repeat(steps, extent[position] // parts).reshape([-1 if axis == position else 1 for axis in range(len(extent))])
    return gain


def scatter_about(stream_key, shape, width, most, cuts=(), kind=jnp.bfloat16):
    array = jax.random.normal(stream_key, shape, jnp.float32) * width
    if len(cuts) > 0:
        array = levels(stream_key, shape, cuts, -0.22, 0.18) * array
    return jnp.clip(array, min=-most, max=most).astype(kind)


def gaussian_with(own_key, extent, width, most, shards, heavy, held_as=jnp.bfloat16):
    array = width * jax.random.normal(own_key, extent, jnp.float32)
    if shards:
        array = array * levels(own_key, extent, shards, -0.22, 0.18)
    return jnp.clip(spiked(array, jax.random.fold_in(own_key, 3), *heavy), -most, most).astype(held_as)


def setup_inputs(seed: int = 0) -> dict:
    keys = jax.random.split(jax.random.key(seed), 8)
    return {
        "hidden_in": gaussian_with(keys[0], (BATCH_SIZE, CONTEXT_SPAN, WIDTH), 1.0, 16.0, ((0, 2), (1, 64)), (1, 2, 64, 4.0)),
        "proj_weight": scatter_about(keys[1], (WIDTH, 2, GROUPS * STATE), (WIDTH * 1024) ** -0.5, 0.0029296875, ((0, 128), (2, 2))),
        "values_in": scatter_about(keys[2], (BATCH_SIZE, CONTEXT_SPAN, SHARD_MIXERS * HEAD_DIM), 1.0, 6.0, ((0, 2), (1, 64), (2, 2))),
        "gate_in": scatter_about(keys[3], (BATCH_SIZE, CONTEXT_SPAN, SHARD_MIXERS * HEAD_DIM), 1.0, 6.0, ((0, 2), (1, 64), (2, 2))),
        "log_decay": draw_log_decay(jax.random.fold_in(keys[7], 71), 0),
        "skip_gain": jnp.clip(0.5 + 1.5 * jax.random.uniform(keys[5], (SHARD_MIXERS,), jnp.float32) ** levels(keys[5], (SHARD_MIXERS,), ((0, 2),), -0.2, 0.2), 0.5, 2.0),
        "grad_out": scatter_about(keys[6], (BATCH_SIZE, CONTEXT_SPAN, SHARD_MIXERS * HEAD_DIM), 1.0, 6.0, ((0, 2), (1, 64), (2, 2))),
    }


def span_summary(b_vals, c_vals, x_vals, dy_round, rate_vals):
    block_len = x_vals.shape[0]
    head_count = x_vals.shape[1]
    group_count = b_vals.shape[1]
    per_group = head_count // group_count
    cumlog = jnp.cumsum(rate_vals, axis=1)
    final_log = cumlog[:, -1]
    to_end = jnp.exp(final_log[:, None] - cumlog)
    from_start = jnp.exp(cumlog)
    b_wide = b_vals.astype(jnp.float32)
    c_wide = c_vals.astype(jnp.float32)
    x_scaled = (x_vals.astype(jnp.float32) * to_end.T[:, :, None]).reshape(block_len, group_count, per_group, HEAD_DIM)
    dy_scaled = (dy_round.astype(jnp.float32) * from_start.T[:, :, None]).reshape(block_len, group_count, per_group, HEAD_DIM)
    state_part = jnp.einsum('qgn,qgkp->ngkp', b_wide, x_scaled, precision=lax.Precision.HIGHEST)
    adjoint_part = jnp.einsum('qgn,qgkp->ngkp', c_wide, dy_scaled, precision=lax.Precision.HIGHEST)
    return jnp.exp(final_log), state_part.reshape(STATE, -1), adjoint_part.reshape(STATE, -1)


def span_full(b_vals, c_vals, x_vals, dy_round, rate_vals, skip_vals, state_in, adjoint_out, dout_vals, gate_vals):
    block_len = x_vals.shape[0]
    head_count = x_vals.shape[1]
    group_count = b_vals.shape[1]
    per_group = head_count // group_count
    cumlog = jnp.cumsum(rate_vals, axis=1)
    final_log = cumlog[:, -1]
    to_end = jnp.exp(final_log[:, None] - cumlog)
    from_start = jnp.exp(cumlog)
    causal = jnp.arange(block_len)[:, None] >= jnp.arange(block_len)[None, :]
    log_gaps = cumlog[:, :, None] - cumlog[:, None, :]
    decays = jnp.where(causal[None], jnp.exp(jnp.where(causal[None], log_gaps, 0.0)), 0.0)
    b_wide = b_vals.astype(jnp.float32)
    c_wide = c_vals.astype(jnp.float32)
    x_wide = x_vals.astype(jnp.float32)
    dy_wide = dy_round.astype(jnp.float32)
    cb_dots = jnp.einsum('tgn,sgn->gts', c_wide, b_wide)
    mixer_bf = (decays * jnp.repeat(cb_dots, per_group, axis=0)).astype(jnp.bfloat16)
    mixer_wide = mixer_bf.astype(jnp.float32)
    state_four = state_in.reshape(STATE, group_count, per_group, HEAD_DIM)
    adjoint_four = adjoint_out.reshape(STATE, group_count, per_group, HEAD_DIM)
    y_intra = jnp.einsum('hts,shp->thp', mixer_wide, x_wide)
    y_inter = jnp.einsum('tgn,ngkp->tgkp', c_wide, state_four, precision=lax.Precision.HIGHEST).reshape(block_len, head_count, HEAD_DIM)
    output_pre = y_intra + y_inter * from_start.T[:, :, None] + skip_vals[None, :, None] * x_wide
    gate_wide = gate_vals.astype(jnp.float32)
    gate_sig = jax.nn.sigmoid(gate_wide)
    grad_gate = (dout_vals.astype(jnp.float32) * output_pre * gate_sig * (1.0 + gate_wide * (1.0 - gate_sig))).astype(jnp.bfloat16)
    x_inter = jnp.einsum('sgn,ngkp->sgkp', b_wide, adjoint_four, precision=lax.Precision.HIGHEST).reshape(block_len, head_count, HEAD_DIM)
    grad_vals = jnp.einsum('hts,thp->shp', mixer_wide, dy_wide) + x_inter * to_end.T[:, :, None] + skip_vals[None, :, None] * dy_wide
    mix_grad = jnp.einsum('thp,shp->hts', dy_wide, x_wide) * decays
    dots_grad = mix_grad.reshape(group_count, per_group, block_len, block_len).sum(axis=1).astype(jnp.bfloat16).astype(jnp.float32)
    dy_scaled = (dy_wide * from_start.T[:, :, None]).reshape(block_len, group_count, per_group, HEAD_DIM)
    x_scaled = (x_wide * to_end.T[:, :, None]).reshape(block_len, group_count, per_group, HEAD_DIM)
    c_grad = jnp.einsum('gts,sgn->tgn', dots_grad, b_wide) + jnp.einsum('tgkp,ngkp->tgn', dy_scaled, state_four, precision=lax.Precision.HIGHEST)
    b_grad = jnp.einsum('gts,tgn->sgn', dots_grad, c_wide) + jnp.einsum('sgkp,ngkp->sgn', x_scaled, adjoint_four, precision=lax.Precision.HIGHEST)
    return grad_vals.astype(jnp.bfloat16), grad_gate, jnp.stack([b_grad, c_grad], axis=1)


def carry_step(running, packed):
    decay_vals, part_vals = packed
    return running * jnp.repeat(decay_vals, HEAD_DIM)[None, :] + part_vals, running


def reference(hidden_in, proj_weight, values_in, gate_in, log_decay, skip_gain, grad_out):
    weight_flat = proj_weight.reshape(WIDTH, 2 * GROUPS * STATE)
    nblocks = CONTEXT_SPAN // SPAN
    grad_inputs = []
    grad_values = []
    grad_gates = []
    proj_sum = jnp.zeros((WIDTH, 2 * GROUPS * STATE), jnp.float32)
    for seq_index in range(BATCH_SIZE):
        tokens = hidden_in[seq_index]
        bc_vals = jnp.dot(tokens, weight_flat, preferred_element_type=jnp.float32).astype(jnp.bfloat16)
        bc_vals = bc_vals.reshape(nblocks, SPAN, 2, GROUPS, STATE)
        b_vals = bc_vals[:, :, 0]
        c_vals = bc_vals[:, :, 1]
        x_vals = values_in[seq_index].reshape(nblocks, SPAN, SHARD_MIXERS, HEAD_DIM)
        gate_vals = gate_in[seq_index].reshape(nblocks, SPAN, SHARD_MIXERS, HEAD_DIM)
        dout_vals = grad_out[seq_index].reshape(nblocks, SPAN, SHARD_MIXERS, HEAD_DIM)
        dy_round = (dout_vals.astype(jnp.float32) * jax.nn.silu(gate_vals.astype(jnp.float32))).astype(jnp.bfloat16)
        rate_vals = log_decay[seq_index].reshape(SHARD_MIXERS, nblocks, SPAN).transpose(1, 0, 2)

        def summary_of(packed):
            return span_summary(packed[0], packed[1], packed[2], packed[3], packed[4])

        decays_all, state_parts, adjoint_parts = lax.map(summary_of, (b_vals, c_vals, x_vals, dy_round, rate_vals))
        zero_state = jnp.zeros((STATE, SHARD_MIXERS * HEAD_DIM), jnp.float32)
        final_state, states_in = lax.scan(carry_step, zero_state, (decays_all, state_parts))
        first_adjoint, adjoints_out = lax.scan(carry_step, zero_state, (decays_all, adjoint_parts), reverse=True)

        def full_of(packed):
            return span_full(packed[0], packed[1], packed[2], packed[3], packed[4], skip_gain, packed[5], packed[6], packed[7], packed[8])

        grad_vals, grad_gate, grad_bc = lax.map(full_of, (b_vals, c_vals, x_vals, dy_round, rate_vals, states_in, adjoints_out, dout_vals, gate_vals))
        grad_flat = grad_bc.reshape(CONTEXT_SPAN, 2 * GROUPS * STATE).astype(jnp.bfloat16)
        grad_inputs.append(jnp.dot(grad_flat, weight_flat.T, preferred_element_type=jnp.float32).astype(jnp.bfloat16))
        grad_values.append(grad_vals.reshape(CONTEXT_SPAN, SHARD_MIXERS * HEAD_DIM))
        grad_gates.append(grad_gate.reshape(CONTEXT_SPAN, SHARD_MIXERS * HEAD_DIM))
        proj_sum = proj_sum + jnp.dot(tokens.T, grad_flat, preferred_element_type=jnp.float32)
    grad_proj = (proj_sum / (BATCH_SIZE * CONTEXT_SPAN)).reshape(WIDTH, 2, GROUPS * STATE)
    return jnp.stack(grad_inputs), jnp.stack(grad_values), jnp.stack(grad_gates), grad_proj
```

```python
import jax
import jax.numpy as jnp
from jax import lax
from jax.sharding import PartitionSpec as P

HEAD_DIM = 64
STATE = 64
SPAN = 128


def carried_in(part, axis, combine, identity, reverse):
    count = lax.axis_size(axis)
    place = lax.axis_index(axis)

    def shifted(tree, offset):
        if reverse:
            pairs = [(i + offset, i) for i in range(count - offset)]
        else:
            pairs = [(i, i + offset) for i in range(count - offset)]
        return jax.tree.map(lambda a: lax.ppermute(a, axis, pairs), tree)

    ahead = count - 1 - place if reverse else place
    state = jax.tree.map(
        lambda a, e: jnp.where(ahead >= 1, a, jnp.asarray(e, a.dtype)),
        shifted(part, 1),
        identity,
    )
    offset = 1
    while offset < count:
        earlier = shifted(state, offset)
        merged = combine(earlier, state)
        state = jax.tree.map(lambda m, s: jnp.where(ahead >= offset, m, s), merged, state)
        offset *= 2
    return state


def span_summary(b_vals, c_vals, x_vals, dy_round, rate_vals):
    block_len = x_vals.shape[0]
    head_count = x_vals.shape[1]
    group_count = b_vals.shape[1]
    per_group = head_count // group_count
    cumlog = jnp.cumsum(rate_vals, axis=1)
    final_log = cumlog[:, -1]
    to_end = jnp.exp(final_log[:, None] - cumlog)
    from_start = jnp.exp(cumlog)
    b_wide = b_vals.astype(jnp.float32)
    c_wide = c_vals.astype(jnp.float32)
    x_scaled = (x_vals.astype(jnp.float32) * to_end.T[:, :, None]).reshape(
        block_len, group_count, per_group, HEAD_DIM
    )
    dy_scaled = (dy_round.astype(jnp.float32) * from_start.T[:, :, None]).reshape(
        block_len, group_count, per_group, HEAD_DIM
    )
    state_part = jnp.einsum("qgn,qgkp->ngkp", b_wide, x_scaled, precision=lax.Precision.HIGHEST)
    adjoint_part = jnp.einsum("qgn,qgkp->ngkp", c_wide, dy_scaled, precision=lax.Precision.HIGHEST)
    return (jnp.exp(final_log), state_part.reshape(STATE, -1), adjoint_part.reshape(STATE, -1))


def span_full(
    b_vals,
    c_vals,
    x_vals,
    dy_round,
    rate_vals,
    skip_vals,
    state_in,
    adjoint_out,
    dout_vals,
    gate_vals,
):
    block_len = x_vals.shape[0]
    head_count = x_vals.shape[1]
    group_count = b_vals.shape[1]
    per_group = head_count // group_count
    cumlog = jnp.cumsum(rate_vals, axis=1)
    final_log = cumlog[:, -1]
    to_end = jnp.exp(final_log[:, None] - cumlog)
    from_start = jnp.exp(cumlog)
    causal = jnp.arange(block_len)[:, None] >= jnp.arange(block_len)[None, :]
    log_gaps = cumlog[:, :, None] - cumlog[:, None, :]
    decays = jnp.where(causal[None], jnp.exp(jnp.where(causal[None], log_gaps, 0.0)), 0.0)
    b_wide = b_vals.astype(jnp.float32)
    c_wide = c_vals.astype(jnp.float32)
    cb_dots = jnp.einsum("tgn,sgn->gts", c_vals, b_vals, preferred_element_type=jnp.float32)
    mixer_bf = (decays * jnp.repeat(cb_dots, per_group, axis=0)).astype(jnp.bfloat16)
    state_four = state_in.reshape(STATE, group_count, per_group, HEAD_DIM)
    adjoint_four = adjoint_out.reshape(STATE, group_count, per_group, HEAD_DIM)
    y_intra = jnp.einsum("hts,shp->thp", mixer_bf, x_vals, preferred_element_type=jnp.float32)
    y_inter = jnp.einsum(
        "tgn,ngkp->tgkp", c_wide, state_four, precision=lax.Precision.HIGHEST
    ).reshape(block_len, head_count, HEAD_DIM)
    x_wide = x_vals.astype(jnp.float32)
    output_pre = y_intra + y_inter * from_start.T[:, :, None] + skip_vals[None, :, None] * x_wide
    gate_wide = gate_vals.astype(jnp.float32)
    gate_sig = jax.nn.sigmoid(gate_wide)
    grad_gate = (
        dout_vals.astype(jnp.float32) * output_pre * gate_sig * (1.0 + gate_wide * (1.0 - gate_sig))
    ).astype(jnp.bfloat16)
    dy_wide = dy_round.astype(jnp.float32)
    x_inter = jnp.einsum(
        "sgn,ngkp->sgkp", b_wide, adjoint_four, precision=lax.Precision.HIGHEST
    ).reshape(block_len, head_count, HEAD_DIM)
    grad_vals = (
        jnp.einsum("hts,thp->shp", mixer_bf, dy_round, preferred_element_type=jnp.float32)
        + x_inter * to_end.T[:, :, None]
        + skip_vals[None, :, None] * dy_wide
    )
    mix_grad = (
        jnp.einsum("thp,shp->hts", dy_round, x_vals, preferred_element_type=jnp.float32) * decays
    )
    dots_grad = (
        mix_grad.reshape(group_count, per_group, block_len, block_len)
        .sum(axis=1)
        .astype(jnp.bfloat16)
    )
    dy_scaled = (dy_wide * from_start.T[:, :, None]).reshape(
        block_len, group_count, per_group, HEAD_DIM
    )
    x_scaled = (x_wide * to_end.T[:, :, None]).reshape(block_len, group_count, per_group, HEAD_DIM)
    c_grad = jnp.einsum(
        "gts,sgn->tgn", dots_grad, b_vals, preferred_element_type=jnp.float32
    ) + jnp.einsum("tgkp,ngkp->tgn", dy_scaled, state_four, precision=lax.Precision.HIGHEST)
    b_grad = jnp.einsum(
        "gts,tgn->sgn", dots_grad, c_vals, preferred_element_type=jnp.float32
    ) + jnp.einsum("sgkp,ngkp->sgn", x_scaled, adjoint_four, precision=lax.Precision.HIGHEST)
    return (grad_vals.astype(jnp.bfloat16), grad_gate, jnp.stack([b_grad, c_grad], axis=1))


def chain(earlier, later):
    return (earlier[0] * later[0], earlier[1] * jnp.repeat(later[0], HEAD_DIM)[None, :] + later[1])


def body(hidden_in, proj_weight, values_in, gate_in, log_decay, skip_gain, grad_out):
    tokens = hidden_in[0]
    tok_rows = tokens.shape[0]
    weight_local = proj_weight.reshape(proj_weight.shape[0], -1)
    col_count = weight_local.shape[1]
    weight_full = lax.all_gather(weight_local, ("dp", "ctx"), axis=0, tiled=True)
    bc_sums = jnp.dot(tokens, weight_full, preferred_element_type=jnp.float32)
    group_count = col_count // (2 * STATE)
    head_count = values_in.shape[2] // HEAD_DIM
    nblocks = tok_rows // SPAN
    bc_vals = bc_sums.astype(jnp.bfloat16).reshape(nblocks, SPAN, 2, group_count, STATE)
    x_vals = values_in[0].reshape(nblocks, SPAN, head_count, HEAD_DIM)
    gate_vals = gate_in[0].reshape(nblocks, SPAN, head_count, HEAD_DIM)
    dout_vals = grad_out[0].reshape(nblocks, SPAN, head_count, HEAD_DIM)
    dy_round = (dout_vals.astype(jnp.float32) * jax.nn.silu(gate_vals.astype(jnp.float32))).astype(
        jnp.bfloat16
    )
    rate_vals = log_decay[0].reshape(head_count, nblocks, SPAN)
    summaries = [
        span_summary(bc_vals[0, :, 0], bc_vals[0, :, 1], x_vals[0], dy_round[0], rate_vals[:, 0])
    ]
    dev_decay = jnp.ones((head_count,), jnp.float32)
    dev_state = jnp.zeros((STATE, head_count * HEAD_DIM), jnp.float32)
    dev_adjoint = jnp.zeros((STATE, head_count * HEAD_DIM), jnp.float32)
    block_id = 0
    dev_state = (
        dev_state * jnp.repeat(summaries[block_id][0], HEAD_DIM)[None, :] + summaries[block_id][1]
    )
    dev_decay = dev_decay * summaries[block_id][0]
    for block_id in reversed(range(nblocks)):
        dev_adjoint = (
            dev_adjoint * jnp.repeat(summaries[block_id][0], HEAD_DIM)[None, :]
            + summaries[block_id][2]
        )
    identity = (
        jnp.ones((head_count,), jnp.float32),
        jnp.zeros((STATE, head_count * HEAD_DIM), jnp.float32),
    )
    state_start = carried_in((dev_decay, dev_state), "ctx", chain, identity, False)[1]
    adjoint_end = carried_in((dev_decay, dev_adjoint), "ctx", chain, identity, True)[1]
    running = state_start
    block_id = 0
    states_in = running
    adjoints_out = [None] * nblocks
    running = adjoint_end
    for block_id in reversed(range(nblocks)):
        adjoints_out[block_id] = running
        running = (
            running * jnp.repeat(summaries[block_id][0], HEAD_DIM)[None, :] + summaries[block_id][2]
        )
    results = [
        span_full(
            bc_vals[0, :, 0],
            bc_vals[0, :, 1],
            x_vals[0],
            dy_round[0],
            rate_vals[:, 0],
            skip_gain,
            states_in,
            adjoints_out[0],
            dout_vals[0],
            gate_vals[0],
        )
    ]
    grad_values = jnp.concatenate([entry[0] for entry in results], axis=0).reshape(
        1, tok_rows, head_count * HEAD_DIM
    )
    grad_gate = jnp.concatenate([entry[1] for entry in results], axis=0).reshape(
        1, tok_rows, head_count * HEAD_DIM
    )
    grad_flat = (
        jnp.concatenate([entry[2] for entry in results], axis=0)
        .reshape(tok_rows, col_count)
        .astype(jnp.bfloat16)
    )
    input_terms = jnp.einsum(
        "tc,dc->td", grad_flat, weight_full, preferred_element_type=jnp.float32
    )
    grad_input = lax.psum_scatter(
        input_terms.astype(jnp.bfloat16), "head", scatter_dimension=1, tiled=True
    )[None]
    scale = 1.0 / (lax.axis_size("dp") * lax.axis_size("ctx") * tok_rows)
    proj_terms = jnp.einsum("td,tc->dc", tokens, grad_flat, preferred_element_type=jnp.float32)
    shard_count = lax.axis_size(("dp", "ctx"))
    proj_parts = lax.all_to_all(
        proj_terms.reshape(shard_count, -1, col_count),
        ("dp", "ctx"),
        0,
        0,
        tiled=True,
    )
    grad_proj = proj_parts.sum(axis=0) * scale
    grad_proj = grad_proj.reshape(-1, 2, col_count // 2)
    return (grad_input, grad_values, grad_gate, grad_proj)


def solution(mesh):
    return jax.shard_map(
        body,
        mesh=mesh,
        in_specs=(
            P("dp", "ctx", None),
            P(("dp", "ctx"), None, "head"),
            P("dp", "ctx", "head"),
            P("dp", "ctx", "head"),
            P("dp", "head", "ctx"),
            P("head"),
            P("dp", "ctx", "head"),
        ),
        out_specs=(
            P("dp", "ctx", "head"),
            P("dp", "ctx", "head"),
            P("dp", "ctx", "head"),
            P(("dp", "ctx"), None, "head"),
        ),
        check_vma=False,
    )
```

```python
import jax
import jax.numpy as jnp
from jax import lax
from jax.sharding import PartitionSpec as P

HEAD_DIM = 64
STATE = 64
SPAN = 128


def carried_in(part, axis, combine, identity, reverse):
    count = lax.axis_size(axis)

    def shifted(tree, offset):
        if reverse:
            pairs = [(i + offset, i) for i in range(count - offset)]
        else:
            pairs = [(i, i + offset) for i in range(count - offset)]
        return jax.tree.map(lambda a: lax.ppermute(a, axis, pairs), tree)

    window = jax.tree.map(lambda a, e: jnp.zeros_like(a) + jnp.asarray(e, a.dtype), part, identity)
    whole = part
    offset = 1
    while offset < count:
        window = combine(shifted(whole, offset), window)
        whole = combine(window, part)
        offset *= 2
    return window


def span_summary(b_vals, c_vals, x_vals, dy_round, rate_vals):
    block_len = x_vals.shape[0]
    head_count = x_vals.shape[1]
    group_count = b_vals.shape[1]
    per_group = head_count // group_count
    cumlog = jnp.cumsum(rate_vals, axis=1)
    final_log = cumlog[:, -1]
    to_end = jnp.exp(final_log[:, None] - cumlog)
    from_start = jnp.exp(cumlog)
    b_wide = b_vals.astype(jnp.float32)
    c_wide = c_vals.astype(jnp.float32)
    x_scaled = (x_vals.astype(jnp.float32) * to_end.T[:, :, None]).reshape(
        block_len, group_count, per_group, HEAD_DIM
    )
    dy_scaled = (dy_round.astype(jnp.float32) * from_start.T[:, :, None]).reshape(
        block_len, group_count, per_group, HEAD_DIM
    )
    state_part = jnp.einsum("qgn,qgkp->ngkp", b_wide, x_scaled, precision=lax.Precision.HIGHEST)
    adjoint_part = jnp.einsum("qgn,qgkp->ngkp", c_wide, dy_scaled, precision=lax.Precision.HIGHEST)
    return (jnp.exp(final_log), state_part.reshape(STATE, -1), adjoint_part.reshape(STATE, -1))


def span_full(
    b_vals,
    c_vals,
    x_vals,
    dy_round,
    rate_vals,
    skip_vals,
    state_in,
    adjoint_out,
    dout_vals,
    gate_vals,
):
    block_len = x_vals.shape[0]
    head_count = x_vals.shape[1]
    group_count = b_vals.shape[1]
    per_group = head_count // group_count
    cumlog = jnp.cumsum(rate_vals, axis=1)
    final_log = cumlog[:, -1]
    to_end = jnp.exp(final_log[:, None] - cumlog)
    from_start = jnp.exp(cumlog)
    causal = jnp.arange(block_len)[:, None] >= jnp.arange(block_len)[None, :]
    log_gaps = cumlog[:, :, None] - cumlog[:, None, :]
    decays = jnp.where(causal[None], jnp.exp(jnp.where(causal[None], log_gaps, 0.0)), 0.0)
    b_wide = b_vals.astype(jnp.float32)
    c_wide = c_vals.astype(jnp.float32)
    cb_dots = jnp.einsum("tgn,sgn->gts", c_vals, b_vals, preferred_element_type=jnp.float32)
    mixer_bf = (decays * jnp.repeat(cb_dots, per_group, axis=0)).astype(jnp.bfloat16)
    state_four = state_in.reshape(STATE, group_count, per_group, HEAD_DIM)
    adjoint_four = adjoint_out.reshape(STATE, group_count, per_group, HEAD_DIM)
    y_intra = jnp.einsum("hts,shp->thp", mixer_bf, x_vals, preferred_element_type=jnp.float32)
    y_inter = jnp.einsum(
        "tgn,ngkp->tgkp", c_wide, state_four, precision=lax.Precision.HIGHEST
    ).reshape(block_len, head_count, HEAD_DIM)
    x_wide = x_vals.astype(jnp.float32)
    output_pre = y_intra + y_inter * from_start.T[:, :, None] + skip_vals[None, :, None] * x_wide
    gate_wide = gate_vals.astype(jnp.float32)
    gate_sig = jax.nn.sigmoid(gate_wide)
    grad_gate = (
        dout_vals.astype(jnp.float32) * output_pre * gate_sig * (1.0 + gate_wide * (1.0 - gate_sig))
    ).astype(jnp.bfloat16)
    dy_wide = dy_round.astype(jnp.float32)
    x_inter = jnp.einsum(
        "sgn,ngkp->sgkp", b_wide, adjoint_four, precision=lax.Precision.HIGHEST
    ).reshape(block_len, head_count, HEAD_DIM)
    grad_vals = (
        jnp.einsum("hts,thp->shp", mixer_bf, dy_round, preferred_element_type=jnp.float32)
        + x_inter * to_end.T[:, :, None]
        + skip_vals[None, :, None] * dy_wide
    )
    mix_grad = (
        jnp.einsum("thp,shp->hts", dy_round, x_vals, preferred_element_type=jnp.float32) * decays
    )
    dots_grad = (
        mix_grad.reshape(group_count, per_group, block_len, block_len)
        .sum(axis=1)
        .astype(jnp.bfloat16)
    )
    dy_scaled = (dy_wide * from_start.T[:, :, None]).reshape(
        block_len, group_count, per_group, HEAD_DIM
    )
    x_scaled = (x_wide * to_end.T[:, :, None]).reshape(block_len, group_count, per_group, HEAD_DIM)
    c_grad = jnp.einsum(
        "gts,sgn->tgn", dots_grad, b_vals, preferred_element_type=jnp.float32
    ) + jnp.einsum("tgkp,ngkp->tgn", dy_scaled, state_four, precision=lax.Precision.HIGHEST)
    b_grad = jnp.einsum(
        "gts,tgn->sgn", dots_grad, c_vals, preferred_element_type=jnp.float32
    ) + jnp.einsum("sgkp,ngkp->sgn", x_scaled, adjoint_four, precision=lax.Precision.HIGHEST)
    return (grad_vals.astype(jnp.bfloat16), grad_gate, jnp.stack([b_grad, c_grad], axis=1))


def chain(earlier, later):
    return (earlier[0] * later[0], earlier[1] * jnp.repeat(later[0], HEAD_DIM)[None, :] + later[1])


def body(hidden_in, proj_weight, values_in, gate_in, log_decay, skip_gain, grad_out):
    tokens = hidden_in[0]
    tok_rows = tokens.shape[0]
    weight_local = proj_weight.reshape(proj_weight.shape[0], -1)
    col_count = weight_local.shape[1]
    shard_count = lax.axis_size(("dp", "ctx"))
    weight_full = lax.all_to_all(
        jnp.broadcast_to(weight_local[None], (shard_count,) + weight_local.shape),
        ("dp", "ctx"),
        0,
        0,
        tiled=True,
    ).reshape(-1, col_count)
    bc_sums = jnp.dot(tokens, weight_full, preferred_element_type=jnp.float32)
    group_count = col_count // (2 * STATE)
    head_count = values_in.shape[2] // HEAD_DIM
    nblocks = tok_rows // SPAN
    bc_vals = bc_sums.astype(jnp.bfloat16).reshape(nblocks, SPAN, 2, group_count, STATE)
    x_vals = values_in[0].reshape(nblocks, SPAN, head_count, HEAD_DIM)
    gate_vals = gate_in[0].reshape(nblocks, SPAN, head_count, HEAD_DIM)
    dout_vals = grad_out[0].reshape(nblocks, SPAN, head_count, HEAD_DIM)
    dy_round = (dout_vals.astype(jnp.float32) * jax.nn.silu(gate_vals.astype(jnp.float32))).astype(
        jnp.bfloat16
    )
    rate_vals = log_decay[0].reshape(head_count, nblocks, SPAN)
    summaries = [
        span_summary(bc_vals[0, :, 0], bc_vals[0, :, 1], x_vals[0], dy_round[0], rate_vals[:, 0])
    ]
    dev_decay = jnp.ones((head_count,), jnp.float32)
    dev_state = jnp.zeros((STATE, head_count * HEAD_DIM), jnp.float32)
    dev_adjoint = jnp.zeros((STATE, head_count * HEAD_DIM), jnp.float32)
    block_id = 0
    dev_state = (
        dev_state * jnp.repeat(summaries[block_id][0], HEAD_DIM)[None, :] + summaries[block_id][1]
    )
    dev_decay = dev_decay * summaries[block_id][0]
    for block_id in reversed(range(nblocks)):
        dev_adjoint = (
            dev_adjoint * jnp.repeat(summaries[block_id][0], HEAD_DIM)[None, :]
            + summaries[block_id][2]
        )
    identity = (
        jnp.ones((head_count,), jnp.float32),
        jnp.zeros((STATE, head_count * HEAD_DIM), jnp.float32),
    )
    state_start = carried_in((dev_decay, dev_state), "ctx", chain, identity, False)[1]
    adjoint_end = carried_in((dev_decay, dev_adjoint), "ctx", chain, identity, True)[1]
    running = state_start
    block_id = 0
    states_in = running
    adjoints_out = [None] * nblocks
    running = adjoint_end
    for block_id in reversed(range(nblocks)):
        adjoints_out[block_id] = running
        running = (
            running * jnp.repeat(summaries[block_id][0], HEAD_DIM)[None, :] + summaries[block_id][2]
        )
    results = [
        span_full(
            bc_vals[0, :, 0],
            bc_vals[0, :, 1],
            x_vals[0],
            dy_round[0],
            rate_vals[:, 0],
            skip_gain,
            states_in,
            adjoints_out[0],
            dout_vals[0],
            gate_vals[0],
        )
    ]
    grad_values = jnp.concatenate([entry[0] for entry in results], axis=0).reshape(
        1, tok_rows, head_count * HEAD_DIM
    )
    grad_gate = jnp.concatenate([entry[1] for entry in results], axis=0).reshape(
        1, tok_rows, head_count * HEAD_DIM
    )
    grad_flat = (
        jnp.concatenate([entry[2] for entry in results], axis=0)
        .reshape(tok_rows, col_count)
        .astype(jnp.bfloat16)
    )
    input_terms = jnp.einsum(
        "tc,dc->td", grad_flat, weight_full, preferred_element_type=jnp.float32
    )
    grad_input = lax.psum_scatter(
        input_terms.astype(jnp.bfloat16), "head", scatter_dimension=1, tiled=True
    )[None]
    scale = 1.0 / (lax.axis_size("dp") * lax.axis_size("ctx") * tok_rows)
    proj_terms = jnp.einsum("td,tc->dc", tokens, grad_flat, preferred_element_type=jnp.float32)
    proj_parts = lax.all_to_all(
        proj_terms.reshape(shard_count, -1, col_count),
        ("dp", "ctx"),
        0,
        0,
        tiled=True,
    )
    grad_proj = proj_parts.sum(axis=0) * scale
    grad_proj = grad_proj.reshape(-1, 2, col_count // 2)
    return (grad_input, grad_values, grad_gate, grad_proj)


def solution(mesh):
    return jax.shard_map(
        body,
        mesh=mesh,
        in_specs=(
            P("dp", "ctx", None),
            P(("dp", "ctx"), None, "head"),
            P("dp", "ctx", "head"),
            P("dp", "ctx", "head"),
            P("dp", "head", "ctx"),
            P("head"),
            P("dp", "ctx", "head"),
        ),
        out_specs=(
            P("dp", "ctx", "head"),
            P("dp", "ctx", "head"),
            P("dp", "ctx", "head"),
            P(("dp", "ctx"), None, "head"),
        ),
        check_vma=False,
    )
```

```python
import jax
import jax.numpy as jnp
from jax import lax
from jax.sharding import PartitionSpec as P

HEAD_DIM = 64
STATE = 64
SPAN = 128


def carried_both(decay, state, adjoint, axis):
    count = lax.axis_size(axis)
    rows, cols = state.shape
    chunk = cols // count
    decay_row = jnp.repeat(decay, cols // decay.shape[0])[None, :]
    packed = jnp.stack(
        [jnp.concatenate([state, decay_row], 0), jnp.concatenate([adjoint, decay_row], 0)]
    )
    packed = packed.reshape(2, rows + 1, count, chunk).transpose(2, 0, 1, 3)
    got = lax.all_to_all(packed, axis, 0, 0, tiled=True)
    decays = got[:, :, rows:, :]
    parts = got[:, :, :rows, :]

    def chain_cols(earlier, later):
        return (earlier[0] * later[0], earlier[1] * later[0] + later[1])

    decays = jnp.stack([decays[:, 0], decays[::-1, 1]], 1)
    parts = jnp.stack([parts[:, 0], parts[::-1, 1]], 1)

    def moved(a, offset):
        return jnp.concatenate([jnp.zeros_like(a[:offset]), a[:-offset]], 0)

    win_decay, win_part = jnp.ones_like(decays), jnp.zeros_like(parts)
    whole = (decays, parts)
    offset = 1
    while offset < count:
        win_decay, win_part = chain_cols(
            (moved(whole[0], offset), moved(whole[1], offset)), (win_decay, win_part)
        )
        whole = chain_cols((win_decay, win_part), (decays, parts))
        offset *= 2
    scanned = jnp.stack([win_part[:, 0], win_part[::-1, 1]], 1)
    back = lax.all_to_all(scanned, axis, 0, 0, tiled=True)
    back = back.transpose(1, 2, 0, 3).reshape(2, rows, cols)
    return back[0], back[1]


def span_summary(b_vals, c_vals, x_vals, dy_round, rate_vals):
    block_len = x_vals.shape[0]
    head_count = x_vals.shape[1]
    group_count = b_vals.shape[1]
    per_group = head_count // group_count
    cumlog = jnp.cumsum(rate_vals, axis=1)
    final_log = cumlog[:, -1]
    to_end = jnp.exp(final_log[:, None] - cumlog)
    from_start = jnp.exp(cumlog)
    b_wide = b_vals.astype(jnp.float32)
    c_wide = c_vals.astype(jnp.float32)
    x_scaled = (x_vals.astype(jnp.float32) * to_end.T[:, :, None]).reshape(
        block_len, group_count, per_group, HEAD_DIM
    )
    dy_scaled = (dy_round.astype(jnp.float32) * from_start.T[:, :, None]).reshape(
        block_len, group_count, per_group, HEAD_DIM
    )
    state_part = jnp.einsum("qgn,qgkp->ngkp", b_wide, x_scaled, precision=lax.Precision.HIGHEST)
    adjoint_part = jnp.einsum("qgn,qgkp->ngkp", c_wide, dy_scaled, precision=lax.Precision.HIGHEST)
    return (jnp.exp(final_log), state_part.reshape(STATE, -1), adjoint_part.reshape(STATE, -1))


def span_full(
    b_vals,
    c_vals,
    x_vals,
    dy_round,
    rate_vals,
    skip_vals,
    state_in,
    adjoint_out,
    dout_vals,
    gate_vals,
):
    block_len = x_vals.shape[0]
    head_count = x_vals.shape[1]
    group_count = b_vals.shape[1]
    per_group = head_count // group_count
    cumlog = jnp.cumsum(rate_vals, axis=1)
    final_log = cumlog[:, -1]
    to_end = jnp.exp(final_log[:, None] - cumlog)
    from_start = jnp.exp(cumlog)
    causal = jnp.arange(block_len)[:, None] >= jnp.arange(block_len)[None, :]
    log_gaps = cumlog[:, :, None] - cumlog[:, None, :]
    decays = jnp.where(causal[None], jnp.exp(jnp.where(causal[None], log_gaps, 0.0)), 0.0)
    b_wide = b_vals.astype(jnp.float32)
    c_wide = c_vals.astype(jnp.float32)
    cb_dots = jnp.einsum("tgn,sgn->gts", c_vals, b_vals, preferred_element_type=jnp.float32)
    mixer_bf = (decays * jnp.repeat(cb_dots, per_group, axis=0)).astype(jnp.bfloat16)
    state_four = state_in.reshape(STATE, group_count, per_group, HEAD_DIM)
    adjoint_four = adjoint_out.reshape(STATE, group_count, per_group, HEAD_DIM)
    y_intra = jnp.einsum("hts,shp->thp", mixer_bf, x_vals, preferred_element_type=jnp.float32)
    y_inter = jnp.einsum(
        "tgn,ngkp->tgkp", c_wide, state_four, precision=lax.Precision.HIGHEST
    ).reshape(block_len, head_count, HEAD_DIM)
    x_wide = x_vals.astype(jnp.float32)
    output_pre = y_intra + y_inter * from_start.T[:, :, None] + skip_vals[None, :, None] * x_wide
    gate_wide = gate_vals.astype(jnp.float32)
    gate_sig = jax.nn.sigmoid(gate_wide)
    grad_gate = (
        dout_vals.astype(jnp.float32) * output_pre * gate_sig * (1.0 + gate_wide * (1.0 - gate_sig))
    ).astype(jnp.bfloat16)
    dy_wide = dy_round.astype(jnp.float32)
    x_inter = jnp.einsum(
        "sgn,ngkp->sgkp", b_wide, adjoint_four, precision=lax.Precision.HIGHEST
    ).reshape(block_len, head_count, HEAD_DIM)
    grad_vals = (
        jnp.einsum("hts,thp->shp", mixer_bf, dy_round, preferred_element_type=jnp.float32)
        + x_inter * to_end.T[:, :, None]
        + skip_vals[None, :, None] * dy_wide
    )
    mix_grad = (
        jnp.einsum("thp,shp->hts", dy_round, x_vals, preferred_element_type=jnp.float32) * decays
    )
    dots_grad = (
        mix_grad.reshape(group_count, per_group, block_len, block_len)
        .sum(axis=1)
        .astype(jnp.bfloat16)
    )
    dy_scaled = (dy_wide * from_start.T[:, :, None]).reshape(
        block_len, group_count, per_group, HEAD_DIM
    )
    x_scaled = (x_wide * to_end.T[:, :, None]).reshape(block_len, group_count, per_group, HEAD_DIM)
    c_grad = jnp.einsum(
        "gts,sgn->tgn", dots_grad, b_vals, preferred_element_type=jnp.float32
    ) + jnp.einsum("tgkp,ngkp->tgn", dy_scaled, state_four, precision=lax.Precision.HIGHEST)
    b_grad = jnp.einsum(
        "gts,tgn->sgn", dots_grad, c_vals, preferred_element_type=jnp.float32
    ) + jnp.einsum("sgkp,ngkp->sgn", x_scaled, adjoint_four, precision=lax.Precision.HIGHEST)
    return (grad_vals.astype(jnp.bfloat16), grad_gate, jnp.stack([b_grad, c_grad], axis=1))


def chain(earlier, later):
    return (earlier[0] * later[0], earlier[1] * jnp.repeat(later[0], HEAD_DIM)[None, :] + later[1])


def body(hidden_in, proj_weight, values_in, gate_in, log_decay, skip_gain, grad_out):
    tokens = hidden_in[0]
    tok_rows = tokens.shape[0]
    weight_local = proj_weight.reshape(proj_weight.shape[0], -1)
    col_count = weight_local.shape[1]
    shard_count = lax.axis_size(("dp", "ctx"))
    weight_full = lax.all_to_all(
        jnp.broadcast_to(weight_local[None], (shard_count,) + weight_local.shape),
        ("dp", "ctx"),
        0,
        0,
        tiled=True,
    ).reshape(-1, col_count)
    bc_sums = jnp.dot(tokens, weight_full, preferred_element_type=jnp.float32)
    group_count = col_count // (2 * STATE)
    head_count = values_in.shape[2] // HEAD_DIM
    nblocks = tok_rows // SPAN
    bc_vals = bc_sums.astype(jnp.bfloat16).reshape(nblocks, SPAN, 2, group_count, STATE)
    x_vals = values_in[0].reshape(nblocks, SPAN, head_count, HEAD_DIM)
    gate_vals = gate_in[0].reshape(nblocks, SPAN, head_count, HEAD_DIM)
    dout_vals = grad_out[0].reshape(nblocks, SPAN, head_count, HEAD_DIM)
    dy_round = (dout_vals.astype(jnp.float32) * jax.nn.silu(gate_vals.astype(jnp.float32))).astype(
        jnp.bfloat16
    )
    rate_vals = log_decay[0].reshape(head_count, nblocks, SPAN)
    summaries = [
        span_summary(bc_vals[0, :, 0], bc_vals[0, :, 1], x_vals[0], dy_round[0], rate_vals[:, 0])
    ]
    dev_decay = jnp.ones((head_count,), jnp.float32)
    dev_state = jnp.zeros((STATE, head_count * HEAD_DIM), jnp.float32)
    dev_adjoint = jnp.zeros((STATE, head_count * HEAD_DIM), jnp.float32)
    block_id = 0
    dev_state = (
        dev_state * jnp.repeat(summaries[block_id][0], HEAD_DIM)[None, :] + summaries[block_id][1]
    )
    dev_decay = dev_decay * summaries[block_id][0]
    for block_id in reversed(range(nblocks)):
        dev_adjoint = (
            dev_adjoint * jnp.repeat(summaries[block_id][0], HEAD_DIM)[None, :]
            + summaries[block_id][2]
        )
    state_start, adjoint_end = carried_both(dev_decay, dev_state, dev_adjoint, "ctx")
    running = state_start
    block_id = 0
    states_in = running
    adjoints_out = [None] * nblocks
    running = adjoint_end
    for block_id in reversed(range(nblocks)):
        adjoints_out[block_id] = running
        running = (
            running * jnp.repeat(summaries[block_id][0], HEAD_DIM)[None, :] + summaries[block_id][2]
        )
    results = [
        span_full(
            bc_vals[0, :, 0],
            bc_vals[0, :, 1],
            x_vals[0],
            dy_round[0],
            rate_vals[:, 0],
            skip_gain,
            states_in,
            adjoints_out[0],
            dout_vals[0],
            gate_vals[0],
        )
    ]
    grad_values = jnp.concatenate([entry[0] for entry in results], axis=0).reshape(
        1, tok_rows, head_count * HEAD_DIM
    )
    grad_gate = jnp.concatenate([entry[1] for entry in results], axis=0).reshape(
        1, tok_rows, head_count * HEAD_DIM
    )
    grad_flat = (
        jnp.concatenate([entry[2] for entry in results], axis=0)
        .reshape(tok_rows, col_count)
        .astype(jnp.bfloat16)
    )
    input_terms = jnp.einsum(
        "tc,dc->td", grad_flat, weight_full, preferred_element_type=jnp.float32
    )
    grad_input = lax.psum_scatter(
        input_terms.astype(jnp.bfloat16), "head", scatter_dimension=1, tiled=True
    )[None]
    scale = 1.0 / (lax.axis_size("dp") * lax.axis_size("ctx") * tok_rows)
    proj_terms = jnp.einsum("td,tc->dc", tokens, grad_flat, preferred_element_type=jnp.float32)
    proj_parts = lax.all_to_all(
        proj_terms.reshape(shard_count, -1, col_count),
        ("dp", "ctx"),
        0,
        0,
        tiled=True,
    )
    grad_proj = proj_parts.sum(axis=0) * scale
    grad_proj = grad_proj.reshape(-1, 2, col_count // 2)
    return (grad_input, grad_values, grad_gate, grad_proj)


def solution(mesh):
    return jax.shard_map(
        body,
        mesh=mesh,
        in_specs=(
            P("dp", "ctx", None),
            P(("dp", "ctx"), None, "head"),
            P("dp", "ctx", "head"),
            P("dp", "ctx", "head"),
            P("dp", "head", "ctx"),
            P("head"),
            P("dp", "ctx", "head"),
        ),
        out_specs=(
            P("dp", "ctx", "head"),
            P("dp", "ctx", "head"),
            P("dp", "ctx", "head"),
            P(("dp", "ctx"), None, "head"),
        ),
        check_vma=False,
    )
```

```python
import jax
import jax.numpy as jnp
from jax import lax
from jax.sharding import PartitionSpec as P

HEAD_DIM = 64
STATE = 64
SPAN = 128
CTX_PARTS = (("ylo", 2), ("x", 4), ("z", 8))
CTX = tuple(name for name, _ in CTX_PARTS)
ROWS = ("dp",) + CTX
OUTER = ROWS[:-1]
INNER = ROWS[-1]


def carried_both(log_total, state, adjoint, axis):
    count = lax.axis_size(axis)
    rows, cols = state.shape
    chunk = cols // count
    assert HEAD_DIM % chunk == 0
    log_row = jnp.repeat(log_total, cols // log_total.shape[0])[None, :]
    packed = jnp.concatenate(
        [jnp.concatenate([state, log_row], 0)[None], jnp.pad(adjoint, ((0, 1), (0, 0)))[None]], 0
    )
    packed = packed.reshape(2, rows + 1, count, chunk).transpose(2, 0, 1, 3)
    got = lax.all_to_all(packed, axis, 0, 0, tiled=True)
    logs = got[:, 0, rows, 0]
    place = jnp.arange(count)
    inside = (place[None, :, None] < place[None, None, :]) & (
        place[None, None, :] < place[:, None, None]
    )
    gaps = jnp.sum(jnp.where(inside, logs[None, None, :], 0.0), axis=-1)
    before = place[None, :] < place[:, None]
    carry = jnp.where(before, jnp.exp(jnp.where(before, gaps, 0.0)), 0.0)
    fwd = jnp.einsum(
        "ik,knc->inc", carry, got[:, 0, :rows], precision=lax.Precision.HIGHEST
    )
    bwd = jnp.einsum(
        "ki,knc->inc", carry, got[:, 1, :rows], precision=lax.Precision.HIGHEST
    )
    back = lax.all_to_all(jnp.stack([fwd, bwd], 1), axis, 0, 0, tiled=True)
    back = back.transpose(1, 2, 0, 3).reshape(2, rows, cols)
    return back[0], back[1]


def span_summary(b_vals, c_vals, x_vals, dy_round, rate_vals):
    block_len = x_vals.shape[0]
    head_count = x_vals.shape[1]
    group_count = b_vals.shape[1]
    per_group = head_count // group_count
    cumlog = jnp.cumsum(rate_vals, axis=1)
    final_log = cumlog[:, -1]
    to_end = jnp.exp(final_log[:, None] - cumlog)
    from_start = jnp.exp(cumlog)
    b_wide = b_vals.astype(jnp.float32)
    c_wide = c_vals.astype(jnp.float32)
    x_scaled = (x_vals.astype(jnp.float32) * to_end.T[:, :, None]).reshape(
        block_len, group_count, per_group, HEAD_DIM
    )
    dy_scaled = (dy_round.astype(jnp.float32) * from_start.T[:, :, None]).reshape(
        block_len, group_count, per_group, HEAD_DIM
    )
    state_part = jnp.einsum("qgn,qgkp->ngkp", b_wide, x_scaled, precision=lax.Precision.HIGHEST)
    adjoint_part = jnp.einsum("qgn,qgkp->ngkp", c_wide, dy_scaled, precision=lax.Precision.HIGHEST)
    return (jnp.exp(final_log), state_part.reshape(STATE, -1), adjoint_part.reshape(STATE, -1))


def span_full(
    b_vals,
    c_vals,
    x_vals,
    dy_round,
    rate_vals,
    skip_vals,
    state_in,
    adjoint_out,
    dout_vals,
    gate_vals,
):
    block_len = x_vals.shape[0]
    head_count = x_vals.shape[1]
    group_count = b_vals.shape[1]
    per_group = head_count // group_count
    cumlog = jnp.cumsum(rate_vals, axis=1)
    final_log = cumlog[:, -1]
    to_end = jnp.exp(final_log[:, None] - cumlog)
    from_start = jnp.exp(cumlog)
    causal = jnp.arange(block_len)[:, None] >= jnp.arange(block_len)[None, :]
    log_gaps = cumlog[:, :, None] - cumlog[:, None, :]
    decays = jnp.where(causal[None], jnp.exp(jnp.where(causal[None], log_gaps, 0.0)), 0.0)
    b_wide = b_vals.astype(jnp.float32)
    c_wide = c_vals.astype(jnp.float32)
    cb_dots = jnp.einsum("tgn,sgn->gts", c_vals, b_vals, preferred_element_type=jnp.float32)
    mixer_bf = (decays * jnp.repeat(cb_dots, per_group, axis=0)).astype(jnp.bfloat16)
    state_four = state_in.reshape(STATE, group_count, per_group, HEAD_DIM)
    adjoint_four = adjoint_out.reshape(STATE, group_count, per_group, HEAD_DIM)
    y_intra = jnp.einsum("hts,shp->thp", mixer_bf, x_vals, preferred_element_type=jnp.float32)
    y_inter = jnp.einsum(
        "tgn,ngkp->tgkp", c_wide, state_four, precision=lax.Precision.HIGHEST
    ).reshape(block_len, head_count, HEAD_DIM)
    x_wide = x_vals.astype(jnp.float32)
    output_pre = y_intra + y_inter * from_start.T[:, :, None] + skip_vals[None, :, None] * x_wide
    gate_wide = gate_vals.astype(jnp.float32)
    gate_sig = jax.nn.sigmoid(gate_wide)
    grad_gate = (
        dout_vals.astype(jnp.float32) * output_pre * gate_sig * (1.0 + gate_wide * (1.0 - gate_sig))
    ).astype(jnp.bfloat16)
    dy_wide = dy_round.astype(jnp.float32)
    x_inter = jnp.einsum(
        "sgn,ngkp->sgkp", b_wide, adjoint_four, precision=lax.Precision.HIGHEST
    ).reshape(block_len, head_count, HEAD_DIM)
    grad_vals = (
        jnp.einsum("hts,thp->shp", mixer_bf, dy_round, preferred_element_type=jnp.float32)
        + x_inter * to_end.T[:, :, None]
        + skip_vals[None, :, None] * dy_wide
    )
    mix_grad = (
        jnp.einsum("thp,shp->hts", dy_round, x_vals, preferred_element_type=jnp.float32) * decays
    )
    dots_grad = (
        mix_grad.reshape(group_count, per_group, block_len, block_len)
        .sum(axis=1)
        .astype(jnp.bfloat16)
    )
    dy_scaled = (dy_wide * from_start.T[:, :, None]).reshape(
        block_len, group_count, per_group, HEAD_DIM
    )
    x_scaled = (x_wide * to_end.T[:, :, None]).reshape(block_len, group_count, per_group, HEAD_DIM)
    c_grad = jnp.einsum(
        "gts,sgn->tgn", dots_grad, b_vals, preferred_element_type=jnp.float32
    ) + jnp.einsum("tgkp,ngkp->tgn", dy_scaled, state_four, precision=lax.Precision.HIGHEST)
    b_grad = jnp.einsum(
        "gts,tgn->sgn", dots_grad, c_vals, preferred_element_type=jnp.float32
    ) + jnp.einsum("sgkp,ngkp->sgn", x_scaled, adjoint_four, precision=lax.Precision.HIGHEST)
    return (grad_vals.astype(jnp.bfloat16), grad_gate, jnp.stack([b_grad, c_grad], axis=1))


def chain(earlier, later):
    return (earlier[0] * later[0], earlier[1] * jnp.repeat(later[0], HEAD_DIM)[None, :] + later[1])


def body(hidden_in, proj_weight, values_in, gate_in, log_decay, skip_gain, grad_out):
    tokens = hidden_in[0]
    tok_rows = tokens.shape[0]
    weight_local = proj_weight.reshape(proj_weight.shape[0], -1)
    col_count = weight_local.shape[1]
    inner_count = lax.axis_size(INNER)
    outer_count = lax.axis_size(OUTER)
    weight_inner = lax.all_to_all(
        jnp.broadcast_to(weight_local[None], (inner_count,) + weight_local.shape),
        INNER,
        0,
        0,
        tiled=True,
    )
    weight_full = lax.all_to_all(
        jnp.broadcast_to(weight_inner[None], (outer_count,) + weight_inner.shape),
        OUTER,
        0,
        0,
        tiled=True,
    ).reshape(-1, col_count)
    bc_sums = jnp.dot(tokens, weight_full, preferred_element_type=jnp.float32)
    group_count = col_count // (2 * STATE)
    head_count = values_in.shape[2] // HEAD_DIM
    nblocks = tok_rows // SPAN
    bc_vals = bc_sums.astype(jnp.bfloat16).reshape(nblocks, SPAN, 2, group_count, STATE)
    x_vals = values_in[0].reshape(nblocks, SPAN, head_count, HEAD_DIM)
    gate_vals = gate_in[0].reshape(nblocks, SPAN, head_count, HEAD_DIM)
    dout_vals = grad_out[0].reshape(nblocks, SPAN, head_count, HEAD_DIM)
    dy_round = (dout_vals.astype(jnp.float32) * jax.nn.silu(gate_vals.astype(jnp.float32))).astype(
        jnp.bfloat16
    )
    rate_vals = log_decay[0].reshape(head_count, nblocks, SPAN)
    summaries = [
        span_summary(bc_vals[0, :, 0], bc_vals[0, :, 1], x_vals[0], dy_round[0], rate_vals[:, 0])
    ]
    dev_decay = jnp.ones((head_count,), jnp.float32)
    dev_state = jnp.zeros((STATE, head_count * HEAD_DIM), jnp.float32)
    dev_adjoint = jnp.zeros((STATE, head_count * HEAD_DIM), jnp.float32)
    block_id = 0
    dev_state = (
        dev_state * jnp.repeat(summaries[block_id][0], HEAD_DIM)[None, :] + summaries[block_id][1]
    )
    dev_decay = dev_decay * summaries[block_id][0]
    dev_log = jnp.sum(jnp.cumsum(rate_vals, axis=2)[:, :, -1], axis=1)
    for block_id in reversed(range(nblocks)):
        dev_adjoint = (
            dev_adjoint * jnp.repeat(summaries[block_id][0], HEAD_DIM)[None, :]
            + summaries[block_id][2]
        )
    state_start, adjoint_end = carried_both(dev_log, dev_state, dev_adjoint, CTX)
    running = state_start
    block_id = 0
    states_in = running
    adjoints_out = [None] * nblocks
    running = adjoint_end
    for block_id in reversed(range(nblocks)):
        adjoints_out[block_id] = running
        running = (
            running * jnp.repeat(summaries[block_id][0], HEAD_DIM)[None, :] + summaries[block_id][2]
        )
    results = [
        span_full(
            bc_vals[0, :, 0],
            bc_vals[0, :, 1],
            x_vals[0],
            dy_round[0],
            rate_vals[:, 0],
            skip_gain,
            states_in,
            adjoints_out[0],
            dout_vals[0],
            gate_vals[0],
        )
    ]
    grad_values = jnp.concatenate([entry[0] for entry in results], axis=0).reshape(
        1, tok_rows, head_count * HEAD_DIM
    )
    grad_gate = jnp.concatenate([entry[1] for entry in results], axis=0).reshape(
        1, tok_rows, head_count * HEAD_DIM
    )
    grad_flat = (
        jnp.concatenate([entry[2] for entry in results], axis=0)
        .reshape(tok_rows, col_count)
        .astype(jnp.bfloat16)
    )
    input_terms = jnp.einsum(
        "tc,dc->td", grad_flat, weight_full, preferred_element_type=jnp.float32
    )
    grad_input = lax.psum_scatter(
        input_terms.astype(jnp.bfloat16), "head", scatter_dimension=1, tiled=True
    )[None]
    scale = 1.0 / (lax.axis_size(ROWS) * tok_rows)
    proj_terms = jnp.einsum("td,tc->dc", tokens, grad_flat, preferred_element_type=jnp.float32)
    proj_parts = lax.all_to_all(
        proj_terms.reshape(outer_count, inner_count, -1, col_count), OUTER, 0, 0, tiled=True
    ).sum(axis=0)
    proj_parts = lax.all_to_all(proj_parts, INNER, 0, 0, tiled=True)
    grad_proj = proj_parts.sum(axis=0) * scale
    grad_proj = grad_proj.reshape(-1, 2, col_count // 2)
    return (grad_input, grad_values, grad_gate, grad_proj)


def solution(mesh):
    sizes = tuple(size for _, size in CTX_PARTS)
    fine = jax.sharding.Mesh(
        mesh.devices.reshape(mesh.shape["dp"], *sizes, mesh.shape["head"]),
        ("dp",) + CTX + ("head",),
    )
    return jax.shard_map(
        body,
        mesh=fine,
        in_specs=(
            P("dp", CTX, None),
            P(ROWS, None, "head"),
            P("dp", CTX, "head"),
            P("dp", CTX, "head"),
            P("dp", "head", CTX),
            P("head"),
            P("dp", CTX, "head"),
        ),
        out_specs=(
            P("dp", CTX, "head"),
            P("dp", CTX, "head"),
            P("dp", CTX, "head"),
            P(ROWS, None, "head"),
        ),
        check_vma=False,
    )
```

```python
import jax
import jax.numpy as jnp
from jax import lax
from jax.sharding import PartitionSpec as P

HEAD_DIM = 64
STATE = 64
SPAN = 128
CTX_PARTS = (("ylo", 2), ("x", 4), ("z", 8))
CTX = tuple(name for name, _ in CTX_PARTS)
ROWS = ("dp",) + CTX
OUTER = ROWS[:-1]
INNER = ROWS[-1]


def carried_both(log_total, state, adjoint, axis):
    count = lax.axis_size(axis)
    rows, cols = state.shape
    chunk = cols // count
    assert HEAD_DIM % chunk == 0
    lanes = 128
    slabs = jnp.stack([state, adjoint]).reshape(2, rows, count, chunk).transpose(2, 0, 1, 3)
    slabs = slabs.reshape(count, -1, lanes)
    chunk_logs = jnp.repeat(log_total, cols // log_total.shape[0]).reshape(count, chunk)[:, :1]
    packed = jnp.concatenate(
        [slabs, jnp.broadcast_to(chunk_logs[:, :, None], (count, 1, lanes))], 1
    )
    got = lax.all_to_all(packed, axis, 0, 0, tiled=True)
    logs = got[:, -1, 0]
    parts = got[:, :-1].reshape(count, 2, rows, chunk)
    place = jnp.arange(count)
    before = place[None, :] < place[:, None]
    gaps = jnp.dot(
        jnp.where(before, logs[None, :], 0.0),
        before.astype(jnp.float32),
        precision=lax.Precision.HIGHEST,
    )
    carry = jnp.where(before, jnp.exp(jnp.where(before, gaps, 0.0)), 0.0)
    fwd = jnp.einsum("ik,knc->inc", carry, parts[:, 0], precision=lax.Precision.HIGHEST)
    bwd = jnp.einsum("ki,knc->inc", carry, parts[:, 1], precision=lax.Precision.HIGHEST)
    back = lax.all_to_all(
        jnp.stack([fwd, bwd], 1).reshape(count, -1, lanes), axis, 0, 0, tiled=True
    )
    back = back.reshape(count, 2, rows, chunk)
    back = back.transpose(1, 2, 0, 3).reshape(2, rows, cols)
    return back[0], back[1]


def span_summary(b_vals, c_vals, x_vals, dy_round, rate_vals):
    block_len = x_vals.shape[0]
    head_count = x_vals.shape[1]
    group_count = b_vals.shape[1]
    per_group = head_count // group_count
    cumlog = jnp.cumsum(rate_vals, axis=1)
    final_log = cumlog[:, -1]
    to_end = jnp.exp(final_log[:, None] - cumlog)
    from_start = jnp.exp(cumlog)
    b_wide = b_vals.astype(jnp.float32)
    c_wide = c_vals.astype(jnp.float32)
    x_scaled = (x_vals.astype(jnp.float32) * to_end.T[:, :, None]).reshape(
        block_len, group_count, per_group, HEAD_DIM
    )
    dy_scaled = (dy_round.astype(jnp.float32) * from_start.T[:, :, None]).reshape(
        block_len, group_count, per_group, HEAD_DIM
    )
    state_part = jnp.einsum("qgn,qgkp->ngkp", b_wide, x_scaled, precision=lax.Precision.HIGHEST)
    adjoint_part = jnp.einsum("qgn,qgkp->ngkp", c_wide, dy_scaled, precision=lax.Precision.HIGHEST)
    return (jnp.exp(final_log), state_part.reshape(STATE, -1), adjoint_part.reshape(STATE, -1))


def span_full(
    b_vals,
    c_vals,
    x_vals,
    dy_round,
    rate_vals,
    skip_vals,
    state_in,
    adjoint_out,
    dout_vals,
    gate_vals,
):
    block_len = x_vals.shape[0]
    head_count = x_vals.shape[1]
    group_count = b_vals.shape[1]
    per_group = head_count // group_count
    cumlog = jnp.cumsum(rate_vals, axis=1)
    final_log = cumlog[:, -1]
    to_end = jnp.exp(final_log[:, None] - cumlog)
    from_start = jnp.exp(cumlog)
    causal = jnp.arange(block_len)[:, None] >= jnp.arange(block_len)[None, :]
    log_gaps = cumlog[:, :, None] - cumlog[:, None, :]
    decays = jnp.where(causal[None], jnp.exp(jnp.where(causal[None], log_gaps, 0.0)), 0.0)
    b_wide = b_vals.astype(jnp.float32)
    c_wide = c_vals.astype(jnp.float32)
    cb_dots = jnp.einsum("tgn,sgn->gts", c_vals, b_vals, preferred_element_type=jnp.float32)
    mixer_bf = (decays * jnp.repeat(cb_dots, per_group, axis=0)).astype(jnp.bfloat16)
    state_four = state_in.reshape(STATE, group_count, per_group, HEAD_DIM)
    adjoint_four = adjoint_out.reshape(STATE, group_count, per_group, HEAD_DIM)
    y_intra = jnp.einsum("hts,shp->thp", mixer_bf, x_vals, preferred_element_type=jnp.float32)
    y_inter = jnp.einsum(
        "tgn,ngkp->tgkp", c_wide, state_four, precision=lax.Precision.HIGHEST
    ).reshape(block_len, head_count, HEAD_DIM)
    x_wide = x_vals.astype(jnp.float32)
    output_pre = y_intra + y_inter * from_start.T[:, :, None] + skip_vals[None, :, None] * x_wide
    gate_wide = gate_vals.astype(jnp.float32)
    gate_sig = jax.nn.sigmoid(gate_wide)
    grad_gate = (
        dout_vals.astype(jnp.float32) * output_pre * gate_sig * (1.0 + gate_wide * (1.0 - gate_sig))
    ).astype(jnp.bfloat16)
    dy_wide = dy_round.astype(jnp.float32)
    x_inter = jnp.einsum(
        "sgn,ngkp->sgkp", b_wide, adjoint_four, precision=lax.Precision.HIGHEST
    ).reshape(block_len, head_count, HEAD_DIM)
    grad_vals = (
        jnp.einsum("hts,thp->shp", mixer_bf, dy_round, preferred_element_type=jnp.float32)
        + x_inter * to_end.T[:, :, None]
        + skip_vals[None, :, None] * dy_wide
    )
    mix_grad = (
        jnp.einsum("thp,shp->hts", dy_round, x_vals, preferred_element_type=jnp.float32) * decays
    )
    dots_grad = (
        mix_grad.reshape(group_count, per_group, block_len, block_len)
        .sum(axis=1)
        .astype(jnp.bfloat16)
    )
    dy_scaled = (dy_wide * from_start.T[:, :, None]).reshape(
        block_len, group_count, per_group, HEAD_DIM
    )
    x_scaled = (x_wide * to_end.T[:, :, None]).reshape(block_len, group_count, per_group, HEAD_DIM)
    c_grad = jnp.einsum(
        "gts,sgn->tgn", dots_grad, b_vals, preferred_element_type=jnp.float32
    ) + jnp.einsum("tgkp,ngkp->tgn", dy_scaled, state_four, precision=lax.Precision.HIGHEST)
    b_grad = jnp.einsum(
        "gts,tgn->sgn", dots_grad, c_vals, preferred_element_type=jnp.float32
    ) + jnp.einsum("sgkp,ngkp->sgn", x_scaled, adjoint_four, precision=lax.Precision.HIGHEST)
    return (grad_vals.astype(jnp.bfloat16), grad_gate, jnp.stack([b_grad, c_grad], axis=1))


def chain(earlier, later):
    return (earlier[0] * later[0], earlier[1] * jnp.repeat(later[0], HEAD_DIM)[None, :] + later[1])


def body(hidden_in, proj_weight, values_in, gate_in, log_decay, skip_gain, grad_out):
    tokens = hidden_in[0]
    tok_rows = tokens.shape[0]
    weight_local = proj_weight.reshape(proj_weight.shape[0], -1)
    col_count = weight_local.shape[1]
    inner_count = lax.axis_size(INNER)
    outer_count = lax.axis_size(OUTER)
    weight_inner = lax.all_to_all(
        jnp.broadcast_to(weight_local[None], (inner_count,) + weight_local.shape),
        INNER,
        0,
        0,
        tiled=True,
    )
    weight_full = lax.all_to_all(
        jnp.broadcast_to(weight_inner[None], (outer_count,) + weight_inner.shape),
        OUTER,
        0,
        0,
        tiled=True,
    ).reshape(-1, col_count)
    bc_sums = jnp.dot(tokens, weight_full, preferred_element_type=jnp.float32)
    group_count = col_count // (2 * STATE)
    head_count = values_in.shape[2] // HEAD_DIM
    nblocks = tok_rows // SPAN
    bc_vals = bc_sums.astype(jnp.bfloat16).reshape(nblocks, SPAN, 2, group_count, STATE)
    x_vals = values_in[0].reshape(nblocks, SPAN, head_count, HEAD_DIM)
    gate_vals = gate_in[0].reshape(nblocks, SPAN, head_count, HEAD_DIM)
    dout_vals = grad_out[0].reshape(nblocks, SPAN, head_count, HEAD_DIM)
    dy_round = (dout_vals.astype(jnp.float32) * jax.nn.silu(gate_vals.astype(jnp.float32))).astype(
        jnp.bfloat16
    )
    rate_vals = log_decay[0].reshape(head_count, nblocks, SPAN)
    summaries = [
        span_summary(bc_vals[0, :, 0], bc_vals[0, :, 1], x_vals[0], dy_round[0], rate_vals[:, 0])
    ]
    dev_decay = jnp.ones((head_count,), jnp.float32)
    dev_state = jnp.zeros((STATE, head_count * HEAD_DIM), jnp.float32)
    dev_adjoint = jnp.zeros((STATE, head_count * HEAD_DIM), jnp.float32)
    block_id = 0
    dev_state = (
        dev_state * jnp.repeat(summaries[block_id][0], HEAD_DIM)[None, :] + summaries[block_id][1]
    )
    dev_decay = dev_decay * summaries[block_id][0]
    dev_log = jnp.sum(jnp.cumsum(rate_vals, axis=2)[:, :, -1], axis=1)
    for block_id in reversed(range(nblocks)):
        dev_adjoint = (
            dev_adjoint * jnp.repeat(summaries[block_id][0], HEAD_DIM)[None, :]
            + summaries[block_id][2]
        )
    state_start, adjoint_end = carried_both(dev_log, dev_state, dev_adjoint, CTX)
    running = state_start
    block_id = 0
    states_in = running
    adjoints_out = [None] * nblocks
    running = adjoint_end
    for block_id in reversed(range(nblocks)):
        adjoints_out[block_id] = running
        running = (
            running * jnp.repeat(summaries[block_id][0], HEAD_DIM)[None, :] + summaries[block_id][2]
        )
    results = [
        span_full(
            bc_vals[0, :, 0],
            bc_vals[0, :, 1],
            x_vals[0],
            dy_round[0],
            rate_vals[:, 0],
            skip_gain,
            states_in,
            adjoints_out[0],
            dout_vals[0],
            gate_vals[0],
        )
    ]
    grad_values = jnp.concatenate([entry[0] for entry in results], axis=0).reshape(
        1, tok_rows, head_count * HEAD_DIM
    )
    grad_gate = jnp.concatenate([entry[1] for entry in results], axis=0).reshape(
        1, tok_rows, head_count * HEAD_DIM
    )
    grad_flat = (
        jnp.concatenate([entry[2] for entry in results], axis=0)
        .reshape(tok_rows, col_count)
        .astype(jnp.bfloat16)
    )
    input_terms = jnp.einsum(
        "tc,dc->td", grad_flat, weight_full, preferred_element_type=jnp.float32
    )
    grad_input = lax.psum_scatter(
        input_terms.astype(jnp.bfloat16), "head", scatter_dimension=1, tiled=True
    )[None]
    scale = 1.0 / (lax.axis_size(ROWS) * tok_rows)
    proj_terms = jnp.einsum("td,tc->dc", tokens, grad_flat, preferred_element_type=jnp.float32)
    proj_parts = lax.all_to_all(
        proj_terms.reshape(outer_count, inner_count, -1, col_count), OUTER, 0, 0, tiled=True
    ).sum(axis=0)
    proj_parts = lax.all_to_all(proj_parts, INNER, 0, 0, tiled=True)
    grad_proj = proj_parts.sum(axis=0) * scale
    grad_proj = grad_proj.reshape(-1, 2, col_count // 2)
    return (grad_input, grad_values, grad_gate, grad_proj)


def solution(mesh):
    sizes = tuple(size for _, size in CTX_PARTS)
    fine = jax.sharding.Mesh(
        mesh.devices.reshape(mesh.shape["dp"], *sizes, mesh.shape["head"]),
        ("dp",) + CTX + ("head",),
    )
    return jax.shard_map(
        body,
        mesh=fine,
        in_specs=(
            P("dp", CTX, None),
            P(ROWS, None, "head"),
            P("dp", CTX, "head"),
            P("dp", CTX, "head"),
            P("dp", "head", CTX),
            P("head"),
            P("dp", CTX, "head"),
        ),
        out_specs=(
            P("dp", CTX, "head"),
            P("dp", CTX, "head"),
            P("dp", CTX, "head"),
            P(ROWS, None, "head"),
        ),
        check_vma=False,
    )
```

```python
import jax
import jax.numpy as jnp
from jax import lax
from jax.sharding import PartitionSpec as P

HEAD_DIM = 64
STATE = 64
SPAN = 128
CTX_PARTS = (("ylo", 2), ("x", 4), ("z", 8))
CTX = tuple(name for name, _ in CTX_PARTS)
ROWS = ("dp",) + CTX
OUTER = ROWS[:-1]
INNER = ROWS[-1]


def carried_both(log_total, state, adjoint, axis):
    count = lax.axis_size(axis)
    rows, cols = state.shape
    chunk = cols // count
    assert HEAD_DIM % chunk == 0
    log_row = jnp.repeat(log_total, cols // log_total.shape[0])[None, :]
    packed = jnp.concatenate(
        [jnp.concatenate([state, log_row], 0)[None], jnp.pad(adjoint, ((0, 1), (0, 0)))[None]], 0
    )
    packed = packed.reshape(2, rows + 1, count, chunk).transpose(2, 0, 1, 3)
    got = lax.all_to_all(packed, axis, 0, 0, tiled=True)
    logs = got[:, 0, rows, 0]
    place = jnp.arange(count)
    before = place[None, :] < place[:, None]
    gaps = jnp.dot(
        jnp.where(before, logs[None, :], 0.0),
        before.astype(jnp.float32),
        precision=lax.Precision.HIGHEST,
    )
    carry = jnp.where(before, jnp.exp(jnp.where(before, gaps, 0.0)), 0.0)
    fwd = jnp.einsum(
        "ik,knc->inc", carry, got[:, 0, :rows], precision=lax.Precision.HIGHEST
    )
    bwd = jnp.einsum(
        "ki,knc->inc", carry, got[:, 1, :rows], precision=lax.Precision.HIGHEST
    )
    back = lax.all_to_all(jnp.stack([fwd, bwd], 1), axis, 0, 0, tiled=True)
    back = back.transpose(1, 2, 0, 3).reshape(2, rows, cols)
    return back[0], back[1]


def span_summary(b_vals, c_vals, x_vals, dy_round, rate_vals):
    block_len = x_vals.shape[0]
    head_count = x_vals.shape[1]
    group_count = b_vals.shape[1]
    per_group = head_count // group_count
    cumlog = jnp.cumsum(rate_vals, axis=1)
    final_log = cumlog[:, -1]
    to_end = jnp.exp(final_log[:, None] - cumlog)
    from_start = jnp.exp(cumlog)
    b_wide = b_vals.astype(jnp.float32)
    c_wide = c_vals.astype(jnp.float32)
    x_scaled = (x_vals.astype(jnp.float32) * to_end.T[:, :, None]).reshape(
        block_len, group_count, per_group, HEAD_DIM
    )
    dy_scaled = (dy_round.astype(jnp.float32) * from_start.T[:, :, None]).reshape(
        block_len, group_count, per_group, HEAD_DIM
    )
    state_part = jnp.einsum("qgn,qgkp->ngkp", b_wide, x_scaled, precision=lax.Precision.HIGHEST)
    adjoint_part = jnp.einsum("qgn,qgkp->ngkp", c_wide, dy_scaled, precision=lax.Precision.HIGHEST)
    return (jnp.exp(final_log), state_part.reshape(STATE, -1), adjoint_part.reshape(STATE, -1))


def span_full(
    b_vals,
    c_vals,
    x_vals,
    dy_round,
    rate_vals,
    skip_vals,
    state_in,
    adjoint_out,
    dout_vals,
    gate_vals,
):
    block_len = x_vals.shape[0]
    head_count = x_vals.shape[1]
    group_count = b_vals.shape[1]
    per_group = head_count // group_count
    cumlog = jnp.cumsum(rate_vals, axis=1)
    final_log = cumlog[:, -1]
    to_end = jnp.exp(final_log[:, None] - cumlog)
    from_start = jnp.exp(cumlog)
    causal = jnp.arange(block_len)[:, None] >= jnp.arange(block_len)[None, :]
    log_gaps = cumlog[:, :, None] - cumlog[:, None, :]
    decays = jnp.where(causal[None], jnp.exp(jnp.where(causal[None], log_gaps, 0.0)), 0.0)
    b_wide = b_vals.astype(jnp.float32)
    c_wide = c_vals.astype(jnp.float32)
    cb_dots = jnp.einsum("tgn,sgn->gts", c_vals, b_vals, preferred_element_type=jnp.float32)
    mixer_bf = (decays * jnp.repeat(cb_dots, per_group, axis=0)).astype(jnp.bfloat16)
    x_wide = x_vals.astype(jnp.float32)
    dy_wide = dy_round.astype(jnp.float32)
    y_local = (
        jnp.einsum("hts,shp->thp", mixer_bf, x_vals, preferred_element_type=jnp.float32)
        + skip_vals[None, :, None] * x_wide
    )
    vals_local = (
        jnp.einsum("hts,thp->shp", mixer_bf, dy_round, preferred_element_type=jnp.float32)
        + skip_vals[None, :, None] * dy_wide
    )
    mix_grad = (
        jnp.einsum("thp,shp->hts", dy_round, x_vals, preferred_element_type=jnp.float32) * decays
    )
    dots_grad = (
        mix_grad.reshape(group_count, per_group, block_len, block_len)
        .sum(axis=1)
        .astype(jnp.bfloat16)
    )
    c_local = jnp.einsum("gts,sgn->tgn", dots_grad, b_vals, preferred_element_type=jnp.float32)
    b_local = jnp.einsum("gts,tgn->sgn", dots_grad, c_vals, preferred_element_type=jnp.float32)
    (y_local, vals_local, c_local, b_local), state_in, adjoint_out = lax.optimization_barrier(
        ((y_local, vals_local, c_local, b_local), state_in, adjoint_out)
    )
    state_four = state_in.reshape(STATE, group_count, per_group, HEAD_DIM)
    adjoint_four = adjoint_out.reshape(STATE, group_count, per_group, HEAD_DIM)
    y_inter = jnp.einsum(
        "tgn,ngkp->tgkp", c_wide, state_four, precision=lax.Precision.HIGHEST
    ).reshape(block_len, head_count, HEAD_DIM)
    output_pre = y_local + y_inter * from_start.T[:, :, None]
    gate_wide = gate_vals.astype(jnp.float32)
    gate_sig = jax.nn.sigmoid(gate_wide)
    grad_gate = (
        dout_vals.astype(jnp.float32) * output_pre * gate_sig * (1.0 + gate_wide * (1.0 - gate_sig))
    ).astype(jnp.bfloat16)
    x_inter = jnp.einsum(
        "sgn,ngkp->sgkp", b_wide, adjoint_four, precision=lax.Precision.HIGHEST
    ).reshape(block_len, head_count, HEAD_DIM)
    grad_vals = vals_local + x_inter * to_end.T[:, :, None]
    dy_scaled = (dy_wide * from_start.T[:, :, None]).reshape(
        block_len, group_count, per_group, HEAD_DIM
    )
    x_scaled = (x_wide * to_end.T[:, :, None]).reshape(block_len, group_count, per_group, HEAD_DIM)
    c_grad = c_local + jnp.einsum(
        "tgkp,ngkp->tgn", dy_scaled, state_four, precision=lax.Precision.HIGHEST
    )
    b_grad = b_local + jnp.einsum(
        "sgkp,ngkp->sgn", x_scaled, adjoint_four, precision=lax.Precision.HIGHEST
    )
    return (grad_vals.astype(jnp.bfloat16), grad_gate, jnp.stack([b_grad, c_grad], axis=1))


def chain(earlier, later):
    return (earlier[0] * later[0], earlier[1] * jnp.repeat(later[0], HEAD_DIM)[None, :] + later[1])


def body(hidden_in, proj_weight, values_in, gate_in, log_decay, skip_gain, grad_out):
    tokens = hidden_in[0]
    tok_rows = tokens.shape[0]
    weight_local = proj_weight.reshape(proj_weight.shape[0], -1)
    col_count = weight_local.shape[1]
    inner_count = lax.axis_size(INNER)
    outer_count = lax.axis_size(OUTER)
    weight_inner = lax.all_to_all(
        jnp.broadcast_to(weight_local[None], (inner_count,) + weight_local.shape),
        INNER,
        0,
        0,
        tiled=True,
    )
    weight_full = lax.all_to_all(
        jnp.broadcast_to(weight_inner[None], (outer_count,) + weight_inner.shape),
        OUTER,
        0,
        0,
        tiled=True,
    ).reshape(-1, col_count)
    bc_sums = jnp.dot(tokens, weight_full, preferred_element_type=jnp.float32)
    group_count = col_count // (2 * STATE)
    head_count = values_in.shape[2] // HEAD_DIM
    nblocks = tok_rows // SPAN
    bc_vals = bc_sums.astype(jnp.bfloat16).reshape(nblocks, SPAN, 2, group_count, STATE)
    x_vals = values_in[0].reshape(nblocks, SPAN, head_count, HEAD_DIM)
    gate_vals = gate_in[0].reshape(nblocks, SPAN, head_count, HEAD_DIM)
    dout_vals = grad_out[0].reshape(nblocks, SPAN, head_count, HEAD_DIM)
    dy_round = (dout_vals.astype(jnp.float32) * jax.nn.silu(gate_vals.astype(jnp.float32))).astype(
        jnp.bfloat16
    )
    rate_vals = log_decay[0].reshape(head_count, nblocks, SPAN)
    summaries = [
        span_summary(bc_vals[0, :, 0], bc_vals[0, :, 1], x_vals[0], dy_round[0], rate_vals[:, 0])
    ]
    dev_decay = jnp.ones((head_count,), jnp.float32)
    dev_state = jnp.zeros((STATE, head_count * HEAD_DIM), jnp.float32)
    dev_adjoint = jnp.zeros((STATE, head_count * HEAD_DIM), jnp.float32)
    block_id = 0
    dev_state = (
        dev_state * jnp.repeat(summaries[block_id][0], HEAD_DIM)[None, :] + summaries[block_id][1]
    )
    dev_decay = dev_decay * summaries[block_id][0]
    dev_log = jnp.sum(jnp.cumsum(rate_vals, axis=2)[:, :, -1], axis=1)
    for block_id in reversed(range(nblocks)):
        dev_adjoint = (
            dev_adjoint * jnp.repeat(summaries[block_id][0], HEAD_DIM)[None, :]
            + summaries[block_id][2]
        )
    state_start, adjoint_end = carried_both(dev_log, dev_state, dev_adjoint, CTX)
    running = state_start
    block_id = 0
    states_in = running
    adjoints_out = [None] * nblocks
    running = adjoint_end
    for block_id in reversed(range(nblocks)):
        adjoints_out[block_id] = running
        running = (
            running * jnp.repeat(summaries[block_id][0], HEAD_DIM)[None, :] + summaries[block_id][2]
        )
    results = [
        span_full(
            bc_vals[0, :, 0],
            bc_vals[0, :, 1],
            x_vals[0],
            dy_round[0],
            rate_vals[:, 0],
            skip_gain,
            states_in,
            adjoints_out[0],
            dout_vals[0],
            gate_vals[0],
        )
    ]
    grad_values = jnp.concatenate([entry[0] for entry in results], axis=0).reshape(
        1, tok_rows, head_count * HEAD_DIM
    )
    grad_gate = jnp.concatenate([entry[1] for entry in results], axis=0).reshape(
        1, tok_rows, head_count * HEAD_DIM
    )
    grad_flat = (
        jnp.concatenate([entry[2] for entry in results], axis=0)
        .reshape(tok_rows, col_count)
        .astype(jnp.bfloat16)
    )
    input_terms = jnp.einsum(
        "tc,dc->td", grad_flat, weight_full, preferred_element_type=jnp.float32
    )
    grad_input = lax.psum_scatter(
        input_terms.astype(jnp.bfloat16), "head", scatter_dimension=1, tiled=True
    )[None]
    scale = 1.0 / (lax.axis_size(ROWS) * tok_rows)
    proj_terms = jnp.einsum("td,tc->dc", tokens, grad_flat, preferred_element_type=jnp.float32)
    proj_parts = lax.all_to_all(
        proj_terms.reshape(outer_count, inner_count, -1, col_count), OUTER, 0, 0, tiled=True
    ).sum(axis=0)
    proj_parts = lax.all_to_all(proj_parts, INNER, 0, 0, tiled=True)
    grad_proj = proj_parts.sum(axis=0) * scale
    grad_proj = grad_proj.reshape(-1, 2, col_count // 2)
    return (grad_input, grad_values, grad_gate, grad_proj)


def solution(mesh):
    sizes = tuple(size for _, size in CTX_PARTS)
    fine = jax.sharding.Mesh(
        mesh.devices.reshape(mesh.shape["dp"], *sizes, mesh.shape["head"]),
        ("dp",) + CTX + ("head",),
    )
    return jax.shard_map(
        body,
        mesh=fine,
        in_specs=(
            P("dp", CTX, None),
            P(ROWS, None, "head"),
            P("dp", CTX, "head"),
            P("dp", CTX, "head"),
            P("dp", "head", CTX),
            P("head"),
            P("dp", CTX, "head"),
        ),
        out_specs=(
            P("dp", CTX, "head"),
            P("dp", CTX, "head"),
            P("dp", CTX, "head"),
            P(ROWS, None, "head"),
        ),
        check_vma=False,
    )
```

```python
import jax
import jax.numpy as jnp
from jax import lax
from jax.sharding import PartitionSpec as P

HEAD_DIM = 64
STATE = 64
SPAN = 128
CTX_PARTS = (("ylo", 2), ("x", 4), ("z", 8))
CTX = tuple(name for name, _ in CTX_PARTS)
ROWS = ("dp",) + CTX
OUTER = ROWS[:-1]
INNER = ROWS[-1]


def carried_both(log_total, state, adjoint, axis):
    count = lax.axis_size(axis)
    rows, cols = state.shape
    share = rows // count
    heads = log_total.shape[0]
    log_row = jnp.repeat(log_total, cols // heads)[None, None, :]
    packed = jnp.concatenate(
        [
            state.reshape(count, share, cols),
            adjoint.reshape(count, share, cols),
            jnp.broadcast_to(log_row, (count, 1, cols)),
        ],
        1,
    )
    got = lax.all_to_all(packed, axis, 0, 0, tiled=True)
    logs = got[:, 2 * share, :: cols // heads]
    place = jnp.arange(count)
    before = place[None, :] < place[:, None]
    gaps = jnp.einsum(
        "him,mk->hik",
        jnp.where(before[None], logs.T[:, None, :], 0.0),
        before.astype(jnp.float32),
        precision=lax.Precision.HIGHEST,
    )
    carry = jnp.where(before[None], jnp.exp(jnp.where(before[None], gaps, 0.0)), 0.0)
    parts = got[:, : 2 * share].reshape(count, 2, share, heads, cols // heads)
    fwd = jnp.einsum("hik,krhp->irhp", carry, parts[:, 0], precision=lax.Precision.HIGHEST)
    bwd = jnp.einsum("hki,krhp->irhp", carry, parts[:, 1], precision=lax.Precision.HIGHEST)
    back = lax.all_to_all(
        jnp.stack([fwd, bwd], 1).reshape(count, 2, share, cols), axis, 0, 0, tiled=True
    )
    return back[:, 0].reshape(rows, cols), back[:, 1].reshape(rows, cols)


def span_summary(b_vals, c_vals, x_vals, dy_round, rate_vals):
    block_len = x_vals.shape[0]
    head_count = x_vals.shape[1]
    group_count = b_vals.shape[1]
    per_group = head_count // group_count
    cumlog = jnp.cumsum(rate_vals, axis=1)
    final_log = cumlog[:, -1]
    to_end = jnp.exp(final_log[:, None] - cumlog)
    from_start = jnp.exp(cumlog)
    b_wide = b_vals.astype(jnp.float32)
    c_wide = c_vals.astype(jnp.float32)
    x_scaled = (x_vals.astype(jnp.float32) * to_end.T[:, :, None]).reshape(
        block_len, group_count, per_group, HEAD_DIM
    )
    dy_scaled = (dy_round.astype(jnp.float32) * from_start.T[:, :, None]).reshape(
        block_len, group_count, per_group, HEAD_DIM
    )
    state_part = jnp.einsum("qgn,qgkp->ngkp", b_wide, x_scaled, precision=lax.Precision.HIGHEST)
    adjoint_part = jnp.einsum("qgn,qgkp->ngkp", c_wide, dy_scaled, precision=lax.Precision.HIGHEST)
    return (jnp.exp(final_log), state_part.reshape(STATE, -1), adjoint_part.reshape(STATE, -1))


def span_full(
    b_vals,
    c_vals,
    x_vals,
    dy_round,
    rate_vals,
    skip_vals,
    state_in,
    adjoint_out,
    dout_vals,
    gate_vals,
):
    block_len = x_vals.shape[0]
    head_count = x_vals.shape[1]
    group_count = b_vals.shape[1]
    per_group = head_count // group_count
    cumlog = jnp.cumsum(rate_vals, axis=1)
    final_log = cumlog[:, -1]
    to_end = jnp.exp(final_log[:, None] - cumlog)
    from_start = jnp.exp(cumlog)
    causal = jnp.arange(block_len)[:, None] >= jnp.arange(block_len)[None, :]
    log_gaps = cumlog[:, :, None] - cumlog[:, None, :]
    decays = jnp.where(causal[None], jnp.exp(jnp.where(causal[None], log_gaps, 0.0)), 0.0)
    b_wide = b_vals.astype(jnp.float32)
    c_wide = c_vals.astype(jnp.float32)
    cb_dots = jnp.einsum("tgn,sgn->gts", c_vals, b_vals, preferred_element_type=jnp.float32)
    mixer_bf = (decays * jnp.repeat(cb_dots, per_group, axis=0)).astype(jnp.bfloat16)
    x_wide = x_vals.astype(jnp.float32)
    dy_wide = dy_round.astype(jnp.float32)
    y_local = (
        jnp.einsum("hts,shp->thp", mixer_bf, x_vals, preferred_element_type=jnp.float32)
        + skip_vals[None, :, None] * x_wide
    )
    vals_local = (
        jnp.einsum("hts,thp->shp", mixer_bf, dy_round, preferred_element_type=jnp.float32)
        + skip_vals[None, :, None] * dy_wide
    )
    mix_grad = (
        jnp.einsum("thp,shp->hts", dy_round, x_vals, preferred_element_type=jnp.float32) * decays
    )
    dots_grad = (
        mix_grad.reshape(group_count, per_group, block_len, block_len)
        .sum(axis=1)
        .astype(jnp.bfloat16)
    )
    c_local = jnp.einsum("gts,sgn->tgn", dots_grad, b_vals, preferred_element_type=jnp.float32)
    b_local = jnp.einsum("gts,tgn->sgn", dots_grad, c_vals, preferred_element_type=jnp.float32)
    (y_local, vals_local, c_local, b_local), state_in, adjoint_out = lax.optimization_barrier(
        ((y_local, vals_local, c_local, b_local), state_in, adjoint_out)
    )
    state_four = state_in.reshape(STATE, group_count, per_group, HEAD_DIM)
    adjoint_four = adjoint_out.reshape(STATE, group_count, per_group, HEAD_DIM)
    y_inter = jnp.einsum(
        "tgn,ngkp->tgkp", c_wide, state_four, precision=lax.Precision.HIGHEST
    ).reshape(block_len, head_count, HEAD_DIM)
    output_pre = y_local + y_inter * from_start.T[:, :, None]
    gate_wide = gate_vals.astype(jnp.float32)
    gate_sig = jax.nn.sigmoid(gate_wide)
    grad_gate = (
        dout_vals.astype(jnp.float32) * output_pre * gate_sig * (1.0 + gate_wide * (1.0 - gate_sig))
    ).astype(jnp.bfloat16)
    x_inter = jnp.einsum(
        "sgn,ngkp->sgkp", b_wide, adjoint_four, precision=lax.Precision.HIGHEST
    ).reshape(block_len, head_count, HEAD_DIM)
    grad_vals = vals_local + x_inter * to_end.T[:, :, None]
    dy_scaled = (dy_wide * from_start.T[:, :, None]).reshape(
        block_len, group_count, per_group, HEAD_DIM
    )
    x_scaled = (x_wide * to_end.T[:, :, None]).reshape(block_len, group_count, per_group, HEAD_DIM)
    c_grad = c_local + jnp.einsum(
        "tgkp,ngkp->tgn", dy_scaled, state_four, precision=lax.Precision.HIGHEST
    )
    b_grad = b_local + jnp.einsum(
        "sgkp,ngkp->sgn", x_scaled, adjoint_four, precision=lax.Precision.HIGHEST
    )
    return (grad_vals.astype(jnp.bfloat16), grad_gate, jnp.stack([b_grad, c_grad], axis=1))


def chain(earlier, later):
    return (earlier[0] * later[0], earlier[1] * jnp.repeat(later[0], HEAD_DIM)[None, :] + later[1])


def body(hidden_in, proj_weight, values_in, gate_in, log_decay, skip_gain, grad_out):
    tokens = hidden_in[0]
    tok_rows = tokens.shape[0]
    weight_local = proj_weight.reshape(proj_weight.shape[0], -1)
    col_count = weight_local.shape[1]
    inner_count = lax.axis_size(INNER)
    outer_count = lax.axis_size(OUTER)
    weight_inner = lax.all_to_all(
        jnp.broadcast_to(weight_local[None], (inner_count,) + weight_local.shape),
        INNER,
        0,
        0,
        tiled=True,
    )
    weight_full = lax.all_to_all(
        jnp.broadcast_to(weight_inner[None], (outer_count,) + weight_inner.shape),
        OUTER,
        0,
        0,
        tiled=True,
    ).reshape(-1, col_count)
    bc_sums = jnp.dot(tokens, weight_full, preferred_element_type=jnp.float32)
    group_count = col_count // (2 * STATE)
    head_count = values_in.shape[2] // HEAD_DIM
    nblocks = tok_rows // SPAN
    bc_vals = bc_sums.astype(jnp.bfloat16).reshape(nblocks, SPAN, 2, group_count, STATE)
    x_vals = values_in[0].reshape(nblocks, SPAN, head_count, HEAD_DIM)
    gate_vals = gate_in[0].reshape(nblocks, SPAN, head_count, HEAD_DIM)
    dout_vals = grad_out[0].reshape(nblocks, SPAN, head_count, HEAD_DIM)
    dy_round = (dout_vals.astype(jnp.float32) * jax.nn.silu(gate_vals.astype(jnp.float32))).astype(
        jnp.bfloat16
    )
    rate_vals = log_decay[0].reshape(head_count, nblocks, SPAN)
    summaries = [
        span_summary(bc_vals[0, :, 0], bc_vals[0, :, 1], x_vals[0], dy_round[0], rate_vals[:, 0])
    ]
    dev_decay = jnp.ones((head_count,), jnp.float32)
    dev_state = jnp.zeros((STATE, head_count * HEAD_DIM), jnp.float32)
    dev_adjoint = jnp.zeros((STATE, head_count * HEAD_DIM), jnp.float32)
    block_id = 0
    dev_state = (
        dev_state * jnp.repeat(summaries[block_id][0], HEAD_DIM)[None, :] + summaries[block_id][1]
    )
    dev_decay = dev_decay * summaries[block_id][0]
    dev_log = jnp.sum(jnp.cumsum(rate_vals, axis=2)[:, :, -1], axis=1)
    for block_id in reversed(range(nblocks)):
        dev_adjoint = (
            dev_adjoint * jnp.repeat(summaries[block_id][0], HEAD_DIM)[None, :]
            + summaries[block_id][2]
        )
    state_start, adjoint_end = carried_both(dev_log, dev_state, dev_adjoint, CTX)
    running = state_start
    block_id = 0
    states_in = running
    adjoints_out = [None] * nblocks
    running = adjoint_end
    for block_id in reversed(range(nblocks)):
        adjoints_out[block_id] = running
        running = (
            running * jnp.repeat(summaries[block_id][0], HEAD_DIM)[None, :] + summaries[block_id][2]
        )
    results = [
        span_full(
            bc_vals[0, :, 0],
            bc_vals[0, :, 1],
            x_vals[0],
            dy_round[0],
            rate_vals[:, 0],
            skip_gain,
            states_in,
            adjoints_out[0],
            dout_vals[0],
            gate_vals[0],
        )
    ]
    grad_values = jnp.concatenate([entry[0] for entry in results], axis=0).reshape(
        1, tok_rows, head_count * HEAD_DIM
    )
    grad_gate = jnp.concatenate([entry[1] for entry in results], axis=0).reshape(
        1, tok_rows, head_count * HEAD_DIM
    )
    grad_flat = (
        jnp.concatenate([entry[2] for entry in results], axis=0)
        .reshape(tok_rows, col_count)
        .astype(jnp.bfloat16)
    )
    input_terms = jnp.einsum(
        "tc,dc->td", grad_flat, weight_full, preferred_element_type=jnp.float32
    )
    grad_input = lax.psum_scatter(
        input_terms.astype(jnp.bfloat16), "head", scatter_dimension=1, tiled=True
    )[None]
    scale = 1.0 / (lax.axis_size(ROWS) * tok_rows)
    proj_terms = jnp.einsum("td,tc->dc", tokens, grad_flat, preferred_element_type=jnp.float32)
    proj_parts = lax.all_to_all(
        proj_terms.reshape(outer_count, inner_count, -1, col_count), OUTER, 0, 0, tiled=True
    ).sum(axis=0)
    proj_parts = lax.all_to_all(proj_parts, INNER, 0, 0, tiled=True)
    grad_proj = proj_parts.sum(axis=0) * scale
    grad_proj = grad_proj.reshape(-1, 2, col_count // 2)
    return (grad_input, grad_values, grad_gate, grad_proj)


def solution(mesh):
    sizes = tuple(size for _, size in CTX_PARTS)
    fine = jax.sharding.Mesh(
        mesh.devices.reshape(mesh.shape["dp"], *sizes, mesh.shape["head"]),
        ("dp",) + CTX + ("head",),
    )
    return jax.shard_map(
        body,
        mesh=fine,
        in_specs=(
            P("dp", CTX, None),
            P(ROWS, None, "head"),
            P("dp", CTX, "head"),
            P("dp", CTX, "head"),
            P("dp", "head", CTX),
            P("head"),
            P("dp", CTX, "head"),
        ),
        out_specs=(
            P("dp", CTX, "head"),
            P("dp", CTX, "head"),
            P("dp", CTX, "head"),
            P(ROWS, None, "head"),
        ),
        check_vma=False,
    )
```

```python
import jax
import jax.numpy as jnp
from jax import lax
from jax.sharding import PartitionSpec as P

HEAD_DIM = 64
STATE = 64
SPAN = 128
CTX_PARTS = (("ylo", 2), ("x", 4), ("z", 8))
CTX = tuple(name for name, _ in CTX_PARTS)
ROWS = ("dp",) + CTX
OUTER = ROWS[:-1]
INNER = ROWS[-1]


def carried_both(log_total, state, adjoint, axis):
    count = lax.axis_size(axis)
    rows, cols = state.shape
    chunk = cols // count
    assert HEAD_DIM % chunk == 0
    log_row = jnp.repeat(log_total, cols // log_total.shape[0])[None, :]
    packed = jnp.concatenate(
        [jnp.concatenate([state, log_row], 0)[None], jnp.pad(adjoint, ((0, 1), (0, 0)))[None]], 0
    )
    packed = packed.reshape(2, rows + 1, count, chunk).transpose(2, 0, 1, 3)
    got = lax.all_to_all(packed, axis, 0, 0, tiled=True)
    logs = got[:, 0, rows, 0]
    place = jnp.arange(count)
    before = place[None, :] < place[:, None]
    gaps = jnp.dot(
        jnp.where(before, logs[None, :], 0.0),
        before.astype(jnp.float32),
        precision=lax.Precision.HIGHEST,
    )
    carry = jnp.where(before, jnp.exp(jnp.where(before, gaps, 0.0)), 0.0)
    fwd = jnp.einsum(
        "ik,knc->inc", carry, got[:, 0, :rows], precision=lax.Precision.HIGHEST
    )
    bwd = jnp.einsum(
        "ki,knc->inc", carry, got[:, 1, :rows], precision=lax.Precision.HIGHEST
    )
    back = lax.all_to_all(jnp.stack([fwd, bwd], 1), axis, 0, 0, tiled=True)
    back = back.transpose(1, 2, 0, 3).reshape(2, rows, cols)
    return back[0], back[1]


def span_summary(b_vals, c_vals, x_vals, dy_round, rate_vals):
    block_len = x_vals.shape[0]
    head_count = x_vals.shape[1]
    group_count = b_vals.shape[1]
    per_group = head_count // group_count
    cumlog = jnp.cumsum(rate_vals, axis=1)
    final_log = cumlog[:, -1]
    to_end = jnp.exp(final_log[:, None] - cumlog)
    from_start = jnp.exp(cumlog)
    b_wide = b_vals.astype(jnp.float32)
    c_wide = c_vals.astype(jnp.float32)
    x_scaled = (x_vals.astype(jnp.float32) * to_end.T[:, :, None]).reshape(
        block_len, group_count, per_group, HEAD_DIM
    )
    dy_scaled = (dy_round.astype(jnp.float32) * from_start.T[:, :, None]).reshape(
        block_len, group_count, per_group, HEAD_DIM
    )
    state_part = jnp.einsum("qgn,qgkp->ngkp", b_wide, x_scaled, precision=lax.Precision.HIGHEST)
    adjoint_part = jnp.einsum("qgn,qgkp->ngkp", c_wide, dy_scaled, precision=lax.Precision.HIGHEST)
    return (jnp.exp(final_log), state_part.reshape(STATE, -1), adjoint_part.reshape(STATE, -1))


def span_full(
    b_vals,
    c_vals,
    x_vals,
    dy_round,
    rate_vals,
    skip_vals,
    state_in,
    adjoint_out,
    dout_vals,
    gate_vals,
):
    block_len = x_vals.shape[0]
    head_count = x_vals.shape[1]
    group_count = b_vals.shape[1]
    per_group = head_count // group_count
    cumlog = jnp.cumsum(rate_vals, axis=1)
    final_log = cumlog[:, -1]
    to_end = jnp.exp(final_log[:, None] - cumlog)
    from_start = jnp.exp(cumlog)
    causal = jnp.arange(block_len)[:, None] >= jnp.arange(block_len)[None, :]
    log_gaps = cumlog[:, :, None] - cumlog[:, None, :]
    decays = jnp.where(causal[None], jnp.exp(jnp.where(causal[None], log_gaps, 0.0)), 0.0)
    b_wide = b_vals.astype(jnp.float32)
    c_wide = c_vals.astype(jnp.float32)
    cb_dots = jnp.einsum("tgn,sgn->gts", c_vals, b_vals, preferred_element_type=jnp.float32)
    mixer_bf = (decays * jnp.repeat(cb_dots, per_group, axis=0)).astype(jnp.bfloat16)
    x_wide = x_vals.astype(jnp.float32)
    dy_wide = dy_round.astype(jnp.float32)
    y_local = (
        jnp.einsum("hts,shp->thp", mixer_bf, x_vals, preferred_element_type=jnp.float32)
        + skip_vals[None, :, None] * x_wide
    )
    vals_local = (
        jnp.einsum("hts,thp->shp", mixer_bf, dy_round, preferred_element_type=jnp.float32)
        + skip_vals[None, :, None] * dy_wide
    )
    mix_grad = (
        jnp.einsum("thp,shp->hts", dy_round, x_vals, preferred_element_type=jnp.float32) * decays
    )
    dots_grad = (
        mix_grad.reshape(group_count, per_group, block_len, block_len)
        .sum(axis=1)
        .astype(jnp.bfloat16)
    )
    c_local = jnp.einsum("gts,sgn->tgn", dots_grad, b_vals, preferred_element_type=jnp.float32)
    b_local = jnp.einsum("gts,tgn->sgn", dots_grad, c_vals, preferred_element_type=jnp.float32)
    (y_local, vals_local, c_local, b_local), state_in, adjoint_out = lax.optimization_barrier(
        ((y_local, vals_local, c_local, b_local), state_in, adjoint_out)
    )
    state_four = state_in.reshape(STATE, group_count, per_group, HEAD_DIM)
    adjoint_four = adjoint_out.reshape(STATE, group_count, per_group, HEAD_DIM)
    y_inter = jnp.einsum(
        "tgn,ngkp->tgkp", c_wide, state_four, precision=lax.Precision.HIGHEST
    ).reshape(block_len, head_count, HEAD_DIM)
    output_pre = y_local + y_inter * from_start.T[:, :, None]
    gate_wide = gate_vals.astype(jnp.float32)
    gate_sig = jax.nn.sigmoid(gate_wide)
    grad_gate = (
        dout_vals.astype(jnp.float32) * output_pre * gate_sig * (1.0 + gate_wide * (1.0 - gate_sig))
    ).astype(jnp.bfloat16)
    x_inter = jnp.einsum(
        "sgn,ngkp->sgkp", b_wide, adjoint_four, precision=lax.Precision.HIGHEST
    ).reshape(block_len, head_count, HEAD_DIM)
    grad_vals = vals_local + x_inter * to_end.T[:, :, None]
    dy_scaled = (dy_wide * from_start.T[:, :, None]).reshape(
        block_len, group_count, per_group, HEAD_DIM
    )
    x_scaled = (x_wide * to_end.T[:, :, None]).reshape(block_len, group_count, per_group, HEAD_DIM)
    c_grad = c_local + jnp.einsum(
        "tgkp,ngkp->tgn", dy_scaled, state_four, precision=lax.Precision.HIGHEST
    )
    b_grad = b_local + jnp.einsum(
        "sgkp,ngkp->sgn", x_scaled, adjoint_four, precision=lax.Precision.HIGHEST
    )
    return (grad_vals.astype(jnp.bfloat16), grad_gate, jnp.stack([b_grad, c_grad], axis=1))


def chain(earlier, later):
    return (earlier[0] * later[0], earlier[1] * jnp.repeat(later[0], HEAD_DIM)[None, :] + later[1])


def body(hidden_in, proj_weight, values_in, gate_in, log_decay, skip_gain, grad_out):
    tokens = hidden_in[0]
    tok_rows = tokens.shape[0]
    weight_local = proj_weight.reshape(proj_weight.shape[0], -1)
    col_count = weight_local.shape[1]
    inner_count = lax.axis_size(INNER)
    outer_count = lax.axis_size(OUTER)
    weight_inner = lax.all_to_all(
        jnp.broadcast_to(weight_local[None], (inner_count,) + weight_local.shape),
        INNER,
        0,
        0,
        tiled=True,
    )
    weight_full = lax.all_to_all(
        jnp.broadcast_to(weight_inner[None], (outer_count,) + weight_inner.shape),
        OUTER,
        0,
        0,
        tiled=True,
    ).reshape(-1, col_count)
    bc_sums = jnp.dot(tokens, weight_full, preferred_element_type=jnp.float32)
    group_count = col_count // (2 * STATE)
    head_count = values_in.shape[2] // HEAD_DIM
    nblocks = tok_rows // SPAN
    bc_vals = bc_sums.astype(jnp.bfloat16).reshape(nblocks, SPAN, 2, group_count, STATE)
    x_vals = values_in[0].reshape(nblocks, SPAN, head_count, HEAD_DIM)
    gate_vals = gate_in[0].reshape(nblocks, SPAN, head_count, HEAD_DIM)
    dout_vals = grad_out[0].reshape(nblocks, SPAN, head_count, HEAD_DIM)
    dy_round = (dout_vals.astype(jnp.float32) * jax.nn.silu(gate_vals.astype(jnp.float32))).astype(
        jnp.bfloat16
    )
    rate_vals = log_decay[0].reshape(head_count, nblocks, SPAN)
    summaries = [
        span_summary(bc_vals[0, :, 0], bc_vals[0, :, 1], x_vals[0], dy_round[0], rate_vals[:, 0])
    ]
    dev_decay = jnp.ones((head_count,), jnp.float32)
    dev_state = jnp.zeros((STATE, head_count * HEAD_DIM), jnp.float32)
    dev_adjoint = jnp.zeros((STATE, head_count * HEAD_DIM), jnp.float32)
    block_id = 0
    dev_state = (
        dev_state * jnp.repeat(summaries[block_id][0], HEAD_DIM)[None, :] + summaries[block_id][1]
    )
    dev_decay = dev_decay * summaries[block_id][0]
    dev_log = jnp.sum(jnp.cumsum(rate_vals, axis=2)[:, :, -1], axis=1)
    for block_id in reversed(range(nblocks)):
        dev_adjoint = (
            dev_adjoint * jnp.repeat(summaries[block_id][0], HEAD_DIM)[None, :]
            + summaries[block_id][2]
        )
    state_start, adjoint_end = carried_both(dev_log, dev_state, dev_adjoint, CTX)
    running = state_start
    block_id = 0
    states_in = running
    adjoints_out = [None] * nblocks
    running = adjoint_end
    for block_id in reversed(range(nblocks)):
        adjoints_out[block_id] = running
        running = (
            running * jnp.repeat(summaries[block_id][0], HEAD_DIM)[None, :] + summaries[block_id][2]
        )
    results = [
        span_full(
            bc_vals[0, :, 0],
            bc_vals[0, :, 1],
            x_vals[0],
            dy_round[0],
            rate_vals[:, 0],
            skip_gain,
            states_in,
            adjoints_out[0],
            dout_vals[0],
            gate_vals[0],
        )
    ]
    grad_values = jnp.concatenate([entry[0] for entry in results], axis=0).reshape(
        1, tok_rows, head_count * HEAD_DIM
    )
    grad_gate = jnp.concatenate([entry[1] for entry in results], axis=0).reshape(
        1, tok_rows, head_count * HEAD_DIM
    )
    grad_flat = (
        jnp.concatenate([entry[2] for entry in results], axis=0)
        .reshape(tok_rows, col_count)
        .astype(jnp.bfloat16)
    )
    input_terms = jnp.einsum(
        "tc,dc->td", grad_flat, weight_full, preferred_element_type=jnp.float32
    )
    grad_input = lax.psum_scatter(
        input_terms.astype(jnp.bfloat16), "head", scatter_dimension=1, tiled=True
    )[None]
    scale = 1.0 / (lax.axis_size(ROWS) * tok_rows)
    proj_terms = jnp.einsum("tc,td->cd", grad_flat, tokens, preferred_element_type=jnp.float32)
    proj_parts = lax.all_to_all(
        proj_terms.reshape(col_count, outer_count, -1), OUTER, 1, 1, tiled=True
    ).sum(axis=1)
    proj_parts = lax.all_to_all(
        proj_parts.reshape(col_count, inner_count, -1), INNER, 1, 1, tiled=True
    )
    proj_parts = proj_parts.sum(axis=1).T[None]
    grad_proj = proj_parts.sum(axis=0) * scale
    grad_proj = grad_proj.reshape(-1, 2, col_count // 2)
    return (grad_input, grad_values, grad_gate, grad_proj)


def solution(mesh):
    sizes = tuple(size for _, size in CTX_PARTS)
    fine = jax.sharding.Mesh(
        mesh.devices.reshape(mesh.shape["dp"], *sizes, mesh.shape["head"]),
        ("dp",) + CTX + ("head",),
    )
    return jax.shard_map(
        body,
        mesh=fine,
        in_specs=(
            P("dp", CTX, None),
            P(ROWS, None, "head"),
            P("dp", CTX, "head"),
            P("dp", CTX, "head"),
            P("dp", "head", CTX),
            P("head"),
            P("dp", CTX, "head"),
        ),
        out_specs=(
            P("dp", CTX, "head"),
            P("dp", CTX, "head"),
            P("dp", CTX, "head"),
            P(ROWS, None, "head"),
        ),
        check_vma=False,
    )
```

```python
import jax
import jax.numpy as jnp
from jax import lax
from jax.sharding import PartitionSpec as P

HEAD_DIM = 64
STATE = 64
SPAN = 128
CTX_PARTS = (("ylo", 2), ("x", 4), ("z", 8))
CTX = tuple(name for name, _ in CTX_PARTS)
ROWS = ("dp",) + CTX
OUTER = ROWS[:-1]
INNER = ROWS[-1]


def carried_both(log_total, state, adjoint, axis):
    count = lax.axis_size(axis)
    rows, cols = state.shape
    chunk = cols // count
    assert HEAD_DIM % chunk == 0
    log_row = jnp.repeat(log_total, cols // log_total.shape[0])[None, :]
    packed = jnp.concatenate(
        [jnp.concatenate([state, log_row], 0)[None], jnp.pad(adjoint, ((0, 1), (0, 0)))[None]], 0
    )
    packed = packed.reshape(2, rows + 1, count, chunk).transpose(2, 0, 1, 3)
    got = lax.all_to_all(packed, axis, 0, 0, tiled=True)
    logs = got[:, 0, rows, 0]
    place = jnp.arange(count)
    before = place[None, :] < place[:, None]
    gaps = jnp.dot(
        jnp.where(before, logs[None, :], 0.0),
        before.astype(jnp.float32),
        precision=lax.Precision.HIGHEST,
    )
    carry = jnp.where(before, jnp.exp(jnp.where(before, gaps, 0.0)), 0.0)
    fwd = jnp.einsum(
        "ik,knc->inc", carry, got[:, 0, :rows], precision=lax.Precision.HIGHEST
    )
    bwd = jnp.einsum(
        "ki,knc->inc", carry, got[:, 1, :rows], precision=lax.Precision.HIGHEST
    )
    back = lax.all_to_all(jnp.stack([fwd, bwd], 1), axis, 0, 0, tiled=True)
    return back[:, 0], back[:, 1]


def span_summary(b_vals, c_vals, x_vals, dy_round, rate_vals):
    block_len = x_vals.shape[0]
    head_count = x_vals.shape[1]
    group_count = b_vals.shape[1]
    per_group = head_count // group_count
    cumlog = jnp.cumsum(rate_vals, axis=1)
    final_log = cumlog[:, -1]
    to_end = jnp.exp(final_log[:, None] - cumlog)
    from_start = jnp.exp(cumlog)
    b_wide = b_vals.astype(jnp.float32)
    c_wide = c_vals.astype(jnp.float32)
    x_scaled = (x_vals.astype(jnp.float32) * to_end.T[:, :, None]).reshape(
        block_len, group_count, per_group, HEAD_DIM
    )
    dy_scaled = (dy_round.astype(jnp.float32) * from_start.T[:, :, None]).reshape(
        block_len, group_count, per_group, HEAD_DIM
    )
    state_part = jnp.einsum("qgn,qgkp->ngkp", b_wide, x_scaled, precision=lax.Precision.HIGHEST)
    adjoint_part = jnp.einsum("qgn,qgkp->ngkp", c_wide, dy_scaled, precision=lax.Precision.HIGHEST)
    return (jnp.exp(final_log), state_part.reshape(STATE, -1), adjoint_part.reshape(STATE, -1))


def span_full(
    b_vals,
    c_vals,
    x_vals,
    dy_round,
    rate_vals,
    skip_vals,
    state_in,
    adjoint_out,
    dout_vals,
    gate_vals,
):
    block_len = x_vals.shape[0]
    head_count = x_vals.shape[1]
    group_count = b_vals.shape[1]
    per_group = head_count // group_count
    cumlog = jnp.cumsum(rate_vals, axis=1)
    final_log = cumlog[:, -1]
    to_end = jnp.exp(final_log[:, None] - cumlog)
    from_start = jnp.exp(cumlog)
    causal = jnp.arange(block_len)[:, None] >= jnp.arange(block_len)[None, :]
    log_gaps = cumlog[:, :, None] - cumlog[:, None, :]
    decays = jnp.where(causal[None], jnp.exp(jnp.where(causal[None], log_gaps, 0.0)), 0.0)
    b_wide = b_vals.astype(jnp.float32)
    c_wide = c_vals.astype(jnp.float32)
    cb_dots = jnp.einsum("tgn,sgn->gts", c_vals, b_vals, preferred_element_type=jnp.float32)
    mixer_bf = (decays * jnp.repeat(cb_dots, per_group, axis=0)).astype(jnp.bfloat16)
    x_wide = x_vals.astype(jnp.float32)
    dy_wide = dy_round.astype(jnp.float32)
    y_local = (
        jnp.einsum("hts,shp->thp", mixer_bf, x_vals, preferred_element_type=jnp.float32)
        + skip_vals[None, :, None] * x_wide
    )
    vals_local = (
        jnp.einsum("hts,thp->shp", mixer_bf, dy_round, preferred_element_type=jnp.float32)
        + skip_vals[None, :, None] * dy_wide
    )
    mix_grad = (
        jnp.einsum("thp,shp->hts", dy_round, x_vals, preferred_element_type=jnp.float32) * decays
    )
    dots_grad = (
        mix_grad.reshape(group_count, per_group, block_len, block_len)
        .sum(axis=1)
        .astype(jnp.bfloat16)
    )
    c_local = jnp.einsum("gts,sgn->tgn", dots_grad, b_vals, preferred_element_type=jnp.float32)
    b_local = jnp.einsum("gts,tgn->sgn", dots_grad, c_vals, preferred_element_type=jnp.float32)
    (y_local, vals_local, c_local, b_local), state_in, adjoint_out = lax.optimization_barrier(
        ((y_local, vals_local, c_local, b_local), state_in, adjoint_out)
    )
    width = state_in.shape[-1]
    state_five = state_in.reshape(group_count, per_group, HEAD_DIM // width, STATE, width)
    adjoint_five = adjoint_out.reshape(group_count, per_group, HEAD_DIM // width, STATE, width)
    y_inter = jnp.einsum(
        "tgn,gkhnc->tgkhc", c_wide, state_five, precision=lax.Precision.HIGHEST
    ).reshape(block_len, head_count, HEAD_DIM)
    output_pre = y_local + y_inter * from_start.T[:, :, None]
    gate_wide = gate_vals.astype(jnp.float32)
    gate_sig = jax.nn.sigmoid(gate_wide)
    grad_gate = (
        dout_vals.astype(jnp.float32) * output_pre * gate_sig * (1.0 + gate_wide * (1.0 - gate_sig))
    ).astype(jnp.bfloat16)
    x_inter = jnp.einsum(
        "sgn,gkhnc->sgkhc", b_wide, adjoint_five, precision=lax.Precision.HIGHEST
    ).reshape(block_len, head_count, HEAD_DIM)
    grad_vals = vals_local + x_inter * to_end.T[:, :, None]
    dy_scaled = (dy_wide * from_start.T[:, :, None]).reshape(
        block_len, group_count, per_group, HEAD_DIM // width, width
    )
    x_scaled = (x_wide * to_end.T[:, :, None]).reshape(
        block_len, group_count, per_group, HEAD_DIM // width, width
    )
    c_grad = c_local + jnp.einsum(
        "tgkhc,gkhnc->tgn", dy_scaled, state_five, precision=lax.Precision.HIGHEST
    )
    b_grad = b_local + jnp.einsum(
        "sgkhc,gkhnc->sgn", x_scaled, adjoint_five, precision=lax.Precision.HIGHEST
    )
    return (grad_vals.astype(jnp.bfloat16), grad_gate, jnp.stack([b_grad, c_grad], axis=1))


def chain(earlier, later):
    return (earlier[0] * later[0], earlier[1] * jnp.repeat(later[0], HEAD_DIM)[None, :] + later[1])


def body(hidden_in, proj_weight, values_in, gate_in, log_decay, skip_gain, grad_out):
    tokens = hidden_in[0]
    tok_rows = tokens.shape[0]
    weight_local = proj_weight.reshape(proj_weight.shape[0], -1)
    col_count = weight_local.shape[1]
    inner_count = lax.axis_size(INNER)
    outer_count = lax.axis_size(OUTER)
    weight_inner = lax.all_to_all(
        jnp.broadcast_to(weight_local[None], (inner_count,) + weight_local.shape),
        INNER,
        0,
        0,
        tiled=True,
    )
    weight_full = lax.all_to_all(
        jnp.broadcast_to(weight_inner[None], (outer_count,) + weight_inner.shape),
        OUTER,
        0,
        0,
        tiled=True,
    ).reshape(-1, col_count)
    bc_sums = jnp.dot(tokens, weight_full, preferred_element_type=jnp.float32)
    group_count = col_count // (2 * STATE)
    head_count = values_in.shape[2] // HEAD_DIM
    nblocks = tok_rows // SPAN
    bc_vals = bc_sums.astype(jnp.bfloat16).reshape(nblocks, SPAN, 2, group_count, STATE)
    x_vals = values_in[0].reshape(nblocks, SPAN, head_count, HEAD_DIM)
    gate_vals = gate_in[0].reshape(nblocks, SPAN, head_count, HEAD_DIM)
    dout_vals = grad_out[0].reshape(nblocks, SPAN, head_count, HEAD_DIM)
    dy_round = (dout_vals.astype(jnp.float32) * jax.nn.silu(gate_vals.astype(jnp.float32))).astype(
        jnp.bfloat16
    )
    rate_vals = log_decay[0].reshape(head_count, nblocks, SPAN)
    summaries = [
        span_summary(bc_vals[0, :, 0], bc_vals[0, :, 1], x_vals[0], dy_round[0], rate_vals[:, 0])
    ]
    dev_decay = jnp.ones((head_count,), jnp.float32)
    dev_state = jnp.zeros((STATE, head_count * HEAD_DIM), jnp.float32)
    dev_adjoint = jnp.zeros((STATE, head_count * HEAD_DIM), jnp.float32)
    block_id = 0
    dev_state = (
        dev_state * jnp.repeat(summaries[block_id][0], HEAD_DIM)[None, :] + summaries[block_id][1]
    )
    dev_decay = dev_decay * summaries[block_id][0]
    dev_log = jnp.sum(jnp.cumsum(rate_vals, axis=2)[:, :, -1], axis=1)
    for block_id in reversed(range(nblocks)):
        dev_adjoint = (
            dev_adjoint * jnp.repeat(summaries[block_id][0], HEAD_DIM)[None, :]
            + summaries[block_id][2]
        )
    state_start, adjoint_end = carried_both(dev_log, dev_state, dev_adjoint, CTX)
    assert nblocks == 1
    states_in = state_start
    adjoints_out = [adjoint_end]
    results = [
        span_full(
            bc_vals[0, :, 0],
            bc_vals[0, :, 1],
            x_vals[0],
            dy_round[0],
            rate_vals[:, 0],
            skip_gain,
            states_in,
            adjoints_out[0],
            dout_vals[0],
            gate_vals[0],
        )
    ]
    grad_values = jnp.concatenate([entry[0] for entry in results], axis=0).reshape(
        1, tok_rows, head_count * HEAD_DIM
    )
    grad_gate = jnp.concatenate([entry[1] for entry in results], axis=0).reshape(
        1, tok_rows, head_count * HEAD_DIM
    )
    grad_flat = (
        jnp.concatenate([entry[2] for entry in results], axis=0)
        .reshape(tok_rows, col_count)
        .astype(jnp.bfloat16)
    )
    input_terms = jnp.einsum(
        "tc,dc->td", grad_flat, weight_full, preferred_element_type=jnp.float32
    )
    grad_input = lax.psum_scatter(
        input_terms.astype(jnp.bfloat16), "head", scatter_dimension=1, tiled=True
    )[None]
    scale = 1.0 / (lax.axis_size(ROWS) * tok_rows)
    proj_terms = jnp.einsum("tc,td->cd", grad_flat, tokens, preferred_element_type=jnp.float32)
    proj_parts = lax.all_to_all(
        proj_terms.reshape(col_count, outer_count, -1), OUTER, 1, 1, tiled=True
    ).sum(axis=1)
    proj_parts = lax.all_to_all(
        proj_parts.reshape(col_count, inner_count, -1), INNER, 1, 1, tiled=True
    )
    proj_parts = proj_parts.sum(axis=1).T[None]
    grad_proj = proj_parts.sum(axis=0) * scale
    grad_proj = grad_proj.reshape(-1, 2, col_count // 2)
    return (grad_input, grad_values, grad_gate, grad_proj)


def solution(mesh):
    sizes = tuple(size for _, size in CTX_PARTS)
    fine = jax.sharding.Mesh(
        mesh.devices.reshape(mesh.shape["dp"], *sizes, mesh.shape["head"]),
        ("dp",) + CTX + ("head",),
    )
    return jax.shard_map(
        body,
        mesh=fine,
        in_specs=(
            P("dp", CTX, None),
            P(ROWS, None, "head"),
            P("dp", CTX, "head"),
            P("dp", CTX, "head"),
            P("dp", "head", CTX),
            P("head"),
            P("dp", CTX, "head"),
        ),
        out_specs=(
            P("dp", CTX, "head"),
            P("dp", CTX, "head"),
            P("dp", CTX, "head"),
            P(ROWS, None, "head"),
        ),
        check_vma=False,
    )
```

```python
import jax
import jax.numpy as jnp
from jax import lax
from jax.sharding import PartitionSpec as P

HEAD_DIM = 64
STATE = 64
SPAN = 128
CTX_PARTS = (("ylo", 2), ("x", 4), ("z", 8))
CTX = tuple(name for name, _ in CTX_PARTS)
ROWS = ("dp",) + CTX
OUTER = ROWS[:-1]
INNER = ROWS[-1]


def carried_both(log_total, state, adjoint, axis):
    count = lax.axis_size(axis)
    rows, cols = state.shape
    chunk = cols // count
    assert HEAD_DIM % chunk == 0
    log_row = jnp.repeat(log_total, cols // log_total.shape[0])[None, :]
    packed = jnp.concatenate(
        [jnp.concatenate([state, log_row], 0)[None], jnp.pad(adjoint, ((0, 1), (0, 0)))[None]], 0
    )
    packed = packed.reshape(2, rows + 1, count, chunk).transpose(2, 0, 1, 3)
    got = lax.all_to_all(packed.reshape(count, 1, -1), axis, 0, 0, tiled=True)
    got = got.reshape(count, 2, rows + 1, chunk)
    logs = got[:, 0, rows, 0]
    place = jnp.arange(count)
    before = place[None, :] < place[:, None]
    gaps = jnp.dot(
        jnp.where(before, logs[None, :], 0.0),
        before.astype(jnp.float32),
        precision=lax.Precision.HIGHEST,
    )
    carry = jnp.where(before, jnp.exp(jnp.where(before, gaps, 0.0)), 0.0)
    fwd = jnp.einsum(
        "ik,knc->inc", carry, got[:, 0, :rows], precision=lax.Precision.HIGHEST
    )
    bwd = jnp.einsum(
        "ki,knc->inc", carry, got[:, 1, :rows], precision=lax.Precision.HIGHEST
    )
    back = lax.all_to_all(jnp.stack([fwd, bwd], 1), axis, 0, 0, tiled=True)
    back = back.transpose(1, 2, 0, 3).reshape(2, rows, cols)
    return back[0], back[1]


def span_summary(b_vals, c_vals, x_vals, dy_round, rate_vals):
    block_len = x_vals.shape[0]
    head_count = x_vals.shape[1]
    group_count = b_vals.shape[1]
    per_group = head_count // group_count
    cumlog = jnp.cumsum(rate_vals, axis=1)
    final_log = cumlog[:, -1]
    to_end = jnp.exp(final_log[:, None] - cumlog)
    from_start = jnp.exp(cumlog)
    b_wide = b_vals.astype(jnp.float32)
    c_wide = c_vals.astype(jnp.float32)
    x_scaled = (x_vals.astype(jnp.float32) * to_end.T[:, :, None]).reshape(
        block_len, group_count, per_group, HEAD_DIM
    )
    dy_scaled = (dy_round.astype(jnp.float32) * from_start.T[:, :, None]).reshape(
        block_len, group_count, per_group, HEAD_DIM
    )
    state_part = jnp.einsum("qgn,qgkp->ngkp", b_wide, x_scaled, precision=lax.Precision.HIGHEST)
    adjoint_part = jnp.einsum("qgn,qgkp->ngkp", c_wide, dy_scaled, precision=lax.Precision.HIGHEST)
    return (jnp.exp(final_log), state_part.reshape(STATE, -1), adjoint_part.reshape(STATE, -1))


def span_full(
    b_vals,
    c_vals,
    x_vals,
    dy_round,
    rate_vals,
    skip_vals,
    state_in,
    adjoint_out,
    dout_vals,
    gate_vals,
):
    block_len = x_vals.shape[0]
    head_count = x_vals.shape[1]
    group_count = b_vals.shape[1]
    per_group = head_count // group_count
    cumlog = jnp.cumsum(rate_vals, axis=1)
    final_log = cumlog[:, -1]
    to_end = jnp.exp(final_log[:, None] - cumlog)
    from_start = jnp.exp(cumlog)
    causal = jnp.arange(block_len)[:, None] >= jnp.arange(block_len)[None, :]
    log_gaps = cumlog[:, :, None] - cumlog[:, None, :]
    decays = jnp.where(causal[None], jnp.exp(jnp.where(causal[None], log_gaps, 0.0)), 0.0)
    b_wide = b_vals.astype(jnp.float32)
    c_wide = c_vals.astype(jnp.float32)
    cb_dots = jnp.einsum("tgn,sgn->gts", c_vals, b_vals, preferred_element_type=jnp.float32)
    mixer_bf = (decays * jnp.repeat(cb_dots, per_group, axis=0)).astype(jnp.bfloat16)
    x_wide = x_vals.astype(jnp.float32)
    dy_wide = dy_round.astype(jnp.float32)
    y_local = (
        jnp.einsum("hts,shp->thp", mixer_bf, x_vals, preferred_element_type=jnp.float32)
        + skip_vals[None, :, None] * x_wide
    )
    vals_local = (
        jnp.einsum("hts,thp->shp", mixer_bf, dy_round, preferred_element_type=jnp.float32)
        + skip_vals[None, :, None] * dy_wide
    )
    mix_grad = (
        jnp.einsum("thp,shp->hts", dy_round, x_vals, preferred_element_type=jnp.float32) * decays
    )
    dots_grad = (
        mix_grad.reshape(group_count, per_group, block_len, block_len)
        .sum(axis=1)
        .astype(jnp.bfloat16)
    )
    c_local = jnp.einsum("gts,sgn->tgn", dots_grad, b_vals, preferred_element_type=jnp.float32)
    b_local = jnp.einsum("gts,tgn->sgn", dots_grad, c_vals, preferred_element_type=jnp.float32)
    (y_local, vals_local, c_local, b_local), state_in, adjoint_out = lax.optimization_barrier(
        ((y_local, vals_local, c_local, b_local), state_in, adjoint_out)
    )
    state_four = state_in.reshape(STATE, group_count, per_group, HEAD_DIM)
    adjoint_four = adjoint_out.reshape(STATE, group_count, per_group, HEAD_DIM)
    y_inter = jnp.einsum(
        "tgn,ngkp->tgkp", c_wide, state_four, precision=lax.Precision.HIGHEST
    ).reshape(block_len, head_count, HEAD_DIM)
    output_pre = y_local + y_inter * from_start.T[:, :, None]
    gate_wide = gate_vals.astype(jnp.float32)
    gate_sig = jax.nn.sigmoid(gate_wide)
    grad_gate = (
        dout_vals.astype(jnp.float32) * output_pre * gate_sig * (1.0 + gate_wide * (1.0 - gate_sig))
    ).astype(jnp.bfloat16)
    x_inter = jnp.einsum(
        "sgn,ngkp->sgkp", b_wide, adjoint_four, precision=lax.Precision.HIGHEST
    ).reshape(block_len, head_count, HEAD_DIM)
    grad_vals = vals_local + x_inter * to_end.T[:, :, None]
    dy_scaled = (dy_wide * from_start.T[:, :, None]).reshape(
        block_len, group_count, per_group, HEAD_DIM
    )
    x_scaled = (x_wide * to_end.T[:, :, None]).reshape(block_len, group_count, per_group, HEAD_DIM)
    c_grad = c_local + jnp.einsum(
        "tgkp,ngkp->tgn", dy_scaled, state_four, precision=lax.Precision.HIGHEST
    )
    b_grad = b_local + jnp.einsum(
        "sgkp,ngkp->sgn", x_scaled, adjoint_four, precision=lax.Precision.HIGHEST
    )
    return (grad_vals.astype(jnp.bfloat16), grad_gate, jnp.stack([b_grad, c_grad], axis=1))


def chain(earlier, later):
    return (earlier[0] * later[0], earlier[1] * jnp.repeat(later[0], HEAD_DIM)[None, :] + later[1])


def body(hidden_in, proj_weight, values_in, gate_in, log_decay, skip_gain, grad_out):
    tokens = hidden_in[0]
    tok_rows = tokens.shape[0]
    weight_local = proj_weight.reshape(proj_weight.shape[0], -1)
    col_count = weight_local.shape[1]
    inner_count = lax.axis_size(INNER)
    outer_count = lax.axis_size(OUTER)
    weight_inner = lax.all_to_all(
        jnp.broadcast_to(weight_local[None], (inner_count,) + weight_local.shape),
        INNER,
        0,
        0,
        tiled=True,
    )
    weight_full = lax.all_to_all(
        jnp.broadcast_to(weight_inner[None], (outer_count,) + weight_inner.shape),
        OUTER,
        0,
        0,
        tiled=True,
    ).reshape(-1, col_count)
    bc_sums = jnp.dot(tokens, weight_full, preferred_element_type=jnp.float32)
    group_count = col_count // (2 * STATE)
    head_count = values_in.shape[2] // HEAD_DIM
    nblocks = tok_rows // SPAN
    bc_vals = bc_sums.astype(jnp.bfloat16).reshape(nblocks, SPAN, 2, group_count, STATE)
    x_vals = values_in[0].reshape(nblocks, SPAN, head_count, HEAD_DIM)
    gate_vals = gate_in[0].reshape(nblocks, SPAN, head_count, HEAD_DIM)
    dout_vals = grad_out[0].reshape(nblocks, SPAN, head_count, HEAD_DIM)
    dy_round = (dout_vals.astype(jnp.float32) * jax.nn.silu(gate_vals.astype(jnp.float32))).astype(
        jnp.bfloat16
    )
    rate_vals = log_decay[0].reshape(head_count, nblocks, SPAN)
    summaries = [
        span_summary(bc_vals[0, :, 0], bc_vals[0, :, 1], x_vals[0], dy_round[0], rate_vals[:, 0])
    ]
    dev_decay = jnp.ones((head_count,), jnp.float32)
    dev_state = jnp.zeros((STATE, head_count * HEAD_DIM), jnp.float32)
    dev_adjoint = jnp.zeros((STATE, head_count * HEAD_DIM), jnp.float32)
    block_id = 0
    dev_state = (
        dev_state * jnp.repeat(summaries[block_id][0], HEAD_DIM)[None, :] + summaries[block_id][1]
    )
    dev_decay = dev_decay * summaries[block_id][0]
    dev_log = jnp.sum(jnp.cumsum(rate_vals, axis=2)[:, :, -1], axis=1)
    for block_id in reversed(range(nblocks)):
        dev_adjoint = (
            dev_adjoint * jnp.repeat(summaries[block_id][0], HEAD_DIM)[None, :]
            + summaries[block_id][2]
        )
    state_start, adjoint_end = carried_both(dev_log, dev_state, dev_adjoint, CTX)
    running = state_start
    block_id = 0
    states_in = running
    adjoints_out = [None] * nblocks
    running = adjoint_end
    for block_id in reversed(range(nblocks)):
        adjoints_out[block_id] = running
        running = (
            running * jnp.repeat(summaries[block_id][0], HEAD_DIM)[None, :] + summaries[block_id][2]
        )
    results = [
        span_full(
            bc_vals[0, :, 0],
            bc_vals[0, :, 1],
            x_vals[0],
            dy_round[0],
            rate_vals[:, 0],
            skip_gain,
            states_in,
            adjoints_out[0],
            dout_vals[0],
            gate_vals[0],
        )
    ]
    grad_values = jnp.concatenate([entry[0] for entry in results], axis=0).reshape(
        1, tok_rows, head_count * HEAD_DIM
    )
    grad_gate = jnp.concatenate([entry[1] for entry in results], axis=0).reshape(
        1, tok_rows, head_count * HEAD_DIM
    )
    grad_flat = (
        jnp.concatenate([entry[2] for entry in results], axis=0)
        .reshape(tok_rows, col_count)
        .astype(jnp.bfloat16)
    )
    input_terms = jnp.einsum(
        "tc,dc->td", grad_flat, weight_full, preferred_element_type=jnp.float32
    )
    grad_input = lax.psum_scatter(
        input_terms.astype(jnp.bfloat16), "head", scatter_dimension=1, tiled=True
    )[None]
    scale = 1.0 / (lax.axis_size(ROWS) * tok_rows)
    proj_terms = jnp.einsum("tc,td->cd", grad_flat, tokens, preferred_element_type=jnp.float32)
    proj_parts = lax.all_to_all(
        proj_terms.reshape(col_count, outer_count, -1), OUTER, 1, 1, tiled=True
    ).sum(axis=1)
    proj_parts = lax.all_to_all(
        proj_parts.reshape(col_count, inner_count, -1), INNER, 1, 1, tiled=True
    )
    proj_parts = proj_parts.sum(axis=1).T[None]
    grad_proj = proj_parts.sum(axis=0) * scale
    grad_proj = grad_proj.reshape(-1, 2, col_count // 2)
    return (grad_input, grad_values, grad_gate, grad_proj)


def solution(mesh):
    sizes = tuple(size for _, size in CTX_PARTS)
    fine = jax.sharding.Mesh(
        mesh.devices.reshape(mesh.shape["dp"], *sizes, mesh.shape["head"]),
        ("dp",) + CTX + ("head",),
    )
    return jax.shard_map(
        body,
        mesh=fine,
        in_specs=(
            P("dp", CTX, None),
            P(ROWS, None, "head"),
            P("dp", CTX, "head"),
            P("dp", CTX, "head"),
            P("dp", "head", CTX),
            P("head"),
            P("dp", CTX, "head"),
        ),
        out_specs=(
            P("dp", CTX, "head"),
            P("dp", CTX, "head"),
            P("dp", CTX, "head"),
            P(ROWS, None, "head"),
        ),
        check_vma=False,
    )
```

```python
import jax
import jax.numpy as jnp
from jax import lax
from jax.sharding import PartitionSpec as P

HEAD_DIM = 64
STATE = 64
SPAN = 128
CTX_PARTS = (("ylo", 2), ("x", 4), ("z", 8))
CTX = tuple(name for name, _ in CTX_PARTS)
ROWS = ("dp",) + CTX
OUTER = ROWS[:-1]
INNER = ROWS[-1]


def carried_both(log_total, state, adjoint, axis):
    count = lax.axis_size(axis)
    rows, cols = state.shape
    chunk = cols // count
    assert HEAD_DIM % chunk == 0
    flat = rows * chunk

    def rows_of(a):
        return a.reshape(rows, count, chunk).transpose(1, 0, 2).reshape(count, flat)

    chunk_logs = jnp.repeat(log_total, cols // log_total.shape[0]).reshape(count, chunk)
    packed = jnp.concatenate(
        [rows_of(state), rows_of(adjoint), chunk_logs, jnp.zeros_like(chunk_logs)], 1
    )
    got = lax.all_to_all(packed[:, None], axis, 0, 0, tiled=True)[:, 0]
    logs = got[:, 2 * flat]
    place = jnp.arange(count)
    before = place[None, :] < place[:, None]
    gaps = jnp.dot(
        jnp.where(before, logs[None, :], 0.0),
        before.astype(jnp.float32),
        precision=lax.Precision.HIGHEST,
    )
    carry = jnp.where(before, jnp.exp(jnp.where(before, gaps, 0.0)), 0.0)
    fwd = jnp.dot(carry, got[:, :flat], precision=lax.Precision.HIGHEST)
    bwd = jnp.dot(carry.T, got[:, flat : 2 * flat], precision=lax.Precision.HIGHEST)
    back = lax.all_to_all(jnp.concatenate([fwd, bwd], 1)[:, None], axis, 0, 0, tiled=True)
    back = back.reshape(count, 2, rows, chunk).transpose(1, 2, 0, 3).reshape(2, rows, cols)
    return back[0], back[1]


def span_summary(b_vals, c_vals, x_vals, dy_round, rate_vals):
    block_len = x_vals.shape[0]
    head_count = x_vals.shape[1]
    group_count = b_vals.shape[1]
    per_group = head_count // group_count
    cumlog = jnp.cumsum(rate_vals, axis=1)
    final_log = cumlog[:, -1]
    to_end = jnp.exp(final_log[:, None] - cumlog)
    from_start = jnp.exp(cumlog)
    b_wide = b_vals.astype(jnp.float32)
    c_wide = c_vals.astype(jnp.float32)
    x_scaled = (x_vals.astype(jnp.float32) * to_end.T[:, :, None]).reshape(
        block_len, group_count, per_group, HEAD_DIM
    )
    dy_scaled = (dy_round.astype(jnp.float32) * from_start.T[:, :, None]).reshape(
        block_len, group_count, per_group, HEAD_DIM
    )
    state_part = jnp.einsum("qgn,qgkp->ngkp", b_wide, x_scaled, precision=lax.Precision.HIGHEST)
    adjoint_part = jnp.einsum("qgn,qgkp->ngkp", c_wide, dy_scaled, precision=lax.Precision.HIGHEST)
    return (jnp.exp(final_log), state_part.reshape(STATE, -1), adjoint_part.reshape(STATE, -1))


def span_full(
    b_vals,
    c_vals,
    x_vals,
    dy_round,
    rate_vals,
    skip_vals,
    state_in,
    adjoint_out,
    dout_vals,
    gate_vals,
):
    block_len = x_vals.shape[0]
    head_count = x_vals.shape[1]
    group_count = b_vals.shape[1]
    per_group = head_count // group_count
    cumlog = jnp.cumsum(rate_vals, axis=1)
    final_log = cumlog[:, -1]
    to_end = jnp.exp(final_log[:, None] - cumlog)
    from_start = jnp.exp(cumlog)
    causal = jnp.arange(block_len)[:, None] >= jnp.arange(block_len)[None, :]
    log_gaps = cumlog[:, :, None] - cumlog[:, None, :]
    decays = jnp.where(causal[None], jnp.exp(jnp.where(causal[None], log_gaps, 0.0)), 0.0)
    b_wide = b_vals.astype(jnp.float32)
    c_wide = c_vals.astype(jnp.float32)
    cb_dots = jnp.einsum("tgn,sgn->gts", c_vals, b_vals, preferred_element_type=jnp.float32)
    mixer_bf = (decays * jnp.repeat(cb_dots, per_group, axis=0)).astype(jnp.bfloat16)
    x_wide = x_vals.astype(jnp.float32)
    dy_wide = dy_round.astype(jnp.float32)
    y_local = (
        jnp.einsum("hts,shp->thp", mixer_bf, x_vals, preferred_element_type=jnp.float32)
        + skip_vals[None, :, None] * x_wide
    )
    vals_local = (
        jnp.einsum("hts,thp->shp", mixer_bf, dy_round, preferred_element_type=jnp.float32)
        + skip_vals[None, :, None] * dy_wide
    )
    mix_grad = (
        jnp.einsum("thp,shp->hts", dy_round, x_vals, preferred_element_type=jnp.float32) * decays
    )
    dots_grad = (
        mix_grad.reshape(group_count, per_group, block_len, block_len)
        .sum(axis=1)
        .astype(jnp.bfloat16)
    )
    c_local = jnp.einsum("gts,sgn->tgn", dots_grad, b_vals, preferred_element_type=jnp.float32)
    b_local = jnp.einsum("gts,tgn->sgn", dots_grad, c_vals, preferred_element_type=jnp.float32)
    (y_local, vals_local, c_local, b_local), state_in, adjoint_out = lax.optimization_barrier(
        ((y_local, vals_local, c_local, b_local), state_in, adjoint_out)
    )
    state_four = state_in.reshape(STATE, group_count, per_group, HEAD_DIM)
    adjoint_four = adjoint_out.reshape(STATE, group_count, per_group, HEAD_DIM)
    y_inter = jnp.einsum(
        "tgn,ngkp->tgkp", c_wide, state_four, precision=lax.Precision.HIGHEST
    ).reshape(block_len, head_count, HEAD_DIM)
    output_pre = y_local + y_inter * from_start.T[:, :, None]
    gate_wide = gate_vals.astype(jnp.float32)
    gate_sig = jax.nn.sigmoid(gate_wide)
    grad_gate = (
        dout_vals.astype(jnp.float32) * output_pre * gate_sig * (1.0 + gate_wide * (1.0 - gate_sig))
    ).astype(jnp.bfloat16)
    x_inter = jnp.einsum(
        "sgn,ngkp->sgkp", b_wide, adjoint_four, precision=lax.Precision.HIGHEST
    ).reshape(block_len, head_count, HEAD_DIM)
    grad_vals = vals_local + x_inter * to_end.T[:, :, None]
    dy_scaled = (dy_wide * from_start.T[:, :, None]).reshape(
        block_len, group_count, per_group, HEAD_DIM
    )
    x_scaled = (x_wide * to_end.T[:, :, None]).reshape(block_len, group_count, per_group, HEAD_DIM)
    c_grad = c_local + jnp.einsum(
        "tgkp,ngkp->tgn", dy_scaled, state_four, precision=lax.Precision.HIGHEST
    )
    b_grad = b_local + jnp.einsum(
        "sgkp,ngkp->sgn", x_scaled, adjoint_four, precision=lax.Precision.HIGHEST
    )
    return (grad_vals.astype(jnp.bfloat16), grad_gate, jnp.stack([b_grad, c_grad], axis=1))


def chain(earlier, later):
    return (earlier[0] * later[0], earlier[1] * jnp.repeat(later[0], HEAD_DIM)[None, :] + later[1])


def body(hidden_in, proj_weight, values_in, gate_in, log_decay, skip_gain, grad_out):
    tokens = hidden_in[0]
    tok_rows = tokens.shape[0]
    weight_local = proj_weight.reshape(proj_weight.shape[0], -1)
    col_count = weight_local.shape[1]
    inner_count = lax.axis_size(INNER)
    outer_count = lax.axis_size(OUTER)
    weight_inner = lax.all_to_all(
        jnp.broadcast_to(weight_local[None], (inner_count,) + weight_local.shape),
        INNER,
        0,
        0,
        tiled=True,
    )
    weight_full = lax.all_to_all(
        jnp.broadcast_to(weight_inner[None], (outer_count,) + weight_inner.shape),
        OUTER,
        0,
        0,
        tiled=True,
    ).reshape(-1, col_count)
    bc_sums = jnp.dot(tokens, weight_full, preferred_element_type=jnp.float32)
    group_count = col_count // (2 * STATE)
    head_count = values_in.shape[2] // HEAD_DIM
    nblocks = tok_rows // SPAN
    bc_vals = bc_sums.astype(jnp.bfloat16).reshape(nblocks, SPAN, 2, group_count, STATE)
    x_vals = values_in[0].reshape(nblocks, SPAN, head_count, HEAD_DIM)
    gate_vals = gate_in[0].reshape(nblocks, SPAN, head_count, HEAD_DIM)
    dout_vals = grad_out[0].reshape(nblocks, SPAN, head_count, HEAD_DIM)
    dy_round = (dout_vals.astype(jnp.float32) * jax.nn.silu(gate_vals.astype(jnp.float32))).astype(
        jnp.bfloat16
    )
    rate_vals = log_decay[0].reshape(head_count, nblocks, SPAN)
    summaries = [
        span_summary(bc_vals[0, :, 0], bc_vals[0, :, 1], x_vals[0], dy_round[0], rate_vals[:, 0])
    ]
    dev_decay = jnp.ones((head_count,), jnp.float32)
    dev_state = jnp.zeros((STATE, head_count * HEAD_DIM), jnp.float32)
    dev_adjoint = jnp.zeros((STATE, head_count * HEAD_DIM), jnp.float32)
    block_id = 0
    dev_state = (
        dev_state * jnp.repeat(summaries[block_id][0], HEAD_DIM)[None, :] + summaries[block_id][1]
    )
    dev_decay = dev_decay * summaries[block_id][0]
    dev_log = jnp.sum(jnp.cumsum(rate_vals, axis=2)[:, :, -1], axis=1)
    for block_id in reversed(range(nblocks)):
        dev_adjoint = (
            dev_adjoint * jnp.repeat(summaries[block_id][0], HEAD_DIM)[None, :]
            + summaries[block_id][2]
        )
    state_start, adjoint_end = carried_both(dev_log, dev_state, dev_adjoint, CTX)
    running = state_start
    block_id = 0
    states_in = running
    adjoints_out = [None] * nblocks
    running = adjoint_end
    for block_id in reversed(range(nblocks)):
        adjoints_out[block_id] = running
        running = (
            running * jnp.repeat(summaries[block_id][0], HEAD_DIM)[None, :] + summaries[block_id][2]
        )
    results = [
        span_full(
            bc_vals[0, :, 0],
            bc_vals[0, :, 1],
            x_vals[0],
            dy_round[0],
            rate_vals[:, 0],
            skip_gain,
            states_in,
            adjoints_out[0],
            dout_vals[0],
            gate_vals[0],
        )
    ]
    grad_values = jnp.concatenate([entry[0] for entry in results], axis=0).reshape(
        1, tok_rows, head_count * HEAD_DIM
    )
    grad_gate = jnp.concatenate([entry[1] for entry in results], axis=0).reshape(
        1, tok_rows, head_count * HEAD_DIM
    )
    grad_flat = (
        jnp.concatenate([entry[2] for entry in results], axis=0)
        .reshape(tok_rows, col_count)
        .astype(jnp.bfloat16)
    )
    input_terms = jnp.einsum(
        "tc,dc->td", grad_flat, weight_full, preferred_element_type=jnp.float32
    )
    grad_input = lax.psum_scatter(
        input_terms.astype(jnp.bfloat16), "head", scatter_dimension=1, tiled=True
    )[None]
    scale = 1.0 / (lax.axis_size(ROWS) * tok_rows)
    proj_terms = jnp.einsum("tc,td->cd", grad_flat, tokens, preferred_element_type=jnp.float32)
    proj_parts = lax.all_to_all(
        proj_terms.reshape(col_count, outer_count, -1), OUTER, 1, 1, tiled=True
    ).sum(axis=1)
    proj_parts = lax.all_to_all(
        proj_parts.reshape(col_count, inner_count, -1), INNER, 1, 1, tiled=True
    )
    proj_parts = proj_parts.sum(axis=1).T[None]
    grad_proj = proj_parts.sum(axis=0) * scale
    grad_proj = grad_proj.reshape(-1, 2, col_count // 2)
    return (grad_input, grad_values, grad_gate, grad_proj)


def solution(mesh):
    sizes = tuple(size for _, size in CTX_PARTS)
    fine = jax.sharding.Mesh(
        mesh.devices.reshape(mesh.shape["dp"], *sizes, mesh.shape["head"]),
        ("dp",) + CTX + ("head",),
    )
    return jax.shard_map(
        body,
        mesh=fine,
        in_specs=(
            P("dp", CTX, None),
            P(ROWS, None, "head"),
            P("dp", CTX, "head"),
            P("dp", CTX, "head"),
            P("dp", "head", CTX),
            P("head"),
            P("dp", CTX, "head"),
        ),
        out_specs=(
            P("dp", CTX, "head"),
            P("dp", CTX, "head"),
            P("dp", CTX, "head"),
            P(ROWS, None, "head"),
        ),
        check_vma=False,
    )
```

```python
import jax
import jax.numpy as jnp
from jax import lax
from jax.sharding import PartitionSpec as P

HEAD_DIM = 64
STATE = 64
SPAN = 128
CTX_PARTS = (("ylo", 2), ("x", 4), ("z", 8))
CTX = tuple(name for name, _ in CTX_PARTS)
ROWS = ("dp",) + CTX
OUTER = ROWS[:-1]
INNER = ROWS[-1]


def carried_both(log_total, state_rows, adjoint_rows, axis, rows, cols):
    count = lax.axis_size(axis)
    chunk = cols // count
    assert HEAD_DIM % chunk == 0

    chunk_logs = jnp.repeat(log_total, cols // log_total.shape[0]).reshape(count, chunk)
    packed = jnp.concatenate(
        [state_rows, adjoint_rows, chunk_logs, jnp.zeros_like(chunk_logs)], 1
    )
    got = lax.all_to_all(packed[:, None], axis, 0, 0, tiled=True)[:, 0]
    logs = got[:, 2 * rows * chunk]
    place = jnp.arange(count)
    before = place[None, :] < place[:, None]
    gaps = jnp.dot(
        jnp.where(before, logs[None, :], 0.0),
        before.astype(jnp.float32),
        precision=lax.Precision.HIGHEST,
    )
    carry = jnp.where(before, jnp.exp(jnp.where(before, gaps, 0.0)), 0.0)
    flat = rows * chunk
    fwd = jnp.dot(carry, got[:, :flat], precision=lax.Precision.HIGHEST)
    bwd = jnp.dot(carry.T, got[:, flat : 2 * flat], precision=lax.Precision.HIGHEST)
    back = lax.all_to_all(jnp.concatenate([fwd, bwd], 1)[:, None], axis, 0, 0, tiled=True)
    back = back.reshape(count, 2, rows, chunk).transpose(1, 2, 0, 3).reshape(2, rows, cols)
    return back[0], back[1]


def summary_rows(b_vals, c_vals, x_vals, dy_round, rate_vals, count):
    block_len = x_vals.shape[0]
    head_count = x_vals.shape[1]
    group_count = b_vals.shape[1]
    per_group = head_count // group_count
    chunk = head_count * HEAD_DIM // count
    cumlog = jnp.cumsum(rate_vals, axis=1)
    final_log = cumlog[:, -1]
    to_end = jnp.exp(final_log[:, None] - cumlog)
    from_start = jnp.exp(cumlog)
    shape = (block_len, group_count, per_group, HEAD_DIM // chunk, chunk)
    x_scaled = (x_vals.astype(jnp.float32) * to_end.T[:, :, None]).reshape(shape)
    dy_scaled = (dy_round.astype(jnp.float32) * from_start.T[:, :, None]).reshape(shape)
    state_part = jnp.einsum(
        "qgn,qgkhc->gkhnc", b_vals.astype(jnp.float32), x_scaled, precision=lax.Precision.HIGHEST
    )
    adjoint_part = jnp.einsum(
        "qgn,qgkhc->gkhnc", c_vals.astype(jnp.float32), dy_scaled, precision=lax.Precision.HIGHEST
    )
    return state_part.reshape(count, -1), adjoint_part.reshape(count, -1)


def span_summary(b_vals, c_vals, x_vals, dy_round, rate_vals):
    block_len = x_vals.shape[0]
    head_count = x_vals.shape[1]
    group_count = b_vals.shape[1]
    per_group = head_count // group_count
    cumlog = jnp.cumsum(rate_vals, axis=1)
    final_log = cumlog[:, -1]
    to_end = jnp.exp(final_log[:, None] - cumlog)
    from_start = jnp.exp(cumlog)
    b_wide = b_vals.astype(jnp.float32)
    c_wide = c_vals.astype(jnp.float32)
    x_scaled = (x_vals.astype(jnp.float32) * to_end.T[:, :, None]).reshape(
        block_len, group_count, per_group, HEAD_DIM
    )
    dy_scaled = (dy_round.astype(jnp.float32) * from_start.T[:, :, None]).reshape(
        block_len, group_count, per_group, HEAD_DIM
    )
    state_part = jnp.einsum("qgn,qgkp->ngkp", b_wide, x_scaled, precision=lax.Precision.HIGHEST)
    adjoint_part = jnp.einsum("qgn,qgkp->ngkp", c_wide, dy_scaled, precision=lax.Precision.HIGHEST)
    return (jnp.exp(final_log), state_part.reshape(STATE, -1), adjoint_part.reshape(STATE, -1))


def span_full(
    b_vals,
    c_vals,
    x_vals,
    dy_round,
    rate_vals,
    skip_vals,
    state_in,
    adjoint_out,
    dout_vals,
    gate_vals,
):
    block_len = x_vals.shape[0]
    head_count = x_vals.shape[1]
    group_count = b_vals.shape[1]
    per_group = head_count // group_count
    cumlog = jnp.cumsum(rate_vals, axis=1)
    final_log = cumlog[:, -1]
    to_end = jnp.exp(final_log[:, None] - cumlog)
    from_start = jnp.exp(cumlog)
    causal = jnp.arange(block_len)[:, None] >= jnp.arange(block_len)[None, :]
    log_gaps = cumlog[:, :, None] - cumlog[:, None, :]
    decays = jnp.where(causal[None], jnp.exp(jnp.where(causal[None], log_gaps, 0.0)), 0.0)
    b_wide = b_vals.astype(jnp.float32)
    c_wide = c_vals.astype(jnp.float32)
    cb_dots = jnp.einsum("tgn,sgn->gts", c_vals, b_vals, preferred_element_type=jnp.float32)
    mixer_bf = (decays * jnp.repeat(cb_dots, per_group, axis=0)).astype(jnp.bfloat16)
    x_wide = x_vals.astype(jnp.float32)
    dy_wide = dy_round.astype(jnp.float32)
    y_local = (
        jnp.einsum("hts,shp->thp", mixer_bf, x_vals, preferred_element_type=jnp.float32)
        + skip_vals[None, :, None] * x_wide
    )
    vals_local = (
        jnp.einsum("hts,thp->shp", mixer_bf, dy_round, preferred_element_type=jnp.float32)
        + skip_vals[None, :, None] * dy_wide
    )
    mix_grad = (
        jnp.einsum("thp,shp->hts", dy_round, x_vals, preferred_element_type=jnp.float32) * decays
    )
    dots_grad = (
        mix_grad.reshape(group_count, per_group, block_len, block_len)
        .sum(axis=1)
        .astype(jnp.bfloat16)
    )
    c_local = jnp.einsum("gts,sgn->tgn", dots_grad, b_vals, preferred_element_type=jnp.float32)
    b_local = jnp.einsum("gts,tgn->sgn", dots_grad, c_vals, preferred_element_type=jnp.float32)
    (y_local, vals_local, c_local, b_local), state_in, adjoint_out = lax.optimization_barrier(
        ((y_local, vals_local, c_local, b_local), state_in, adjoint_out)
    )
    state_four = state_in.reshape(STATE, group_count, per_group, HEAD_DIM)
    adjoint_four = adjoint_out.reshape(STATE, group_count, per_group, HEAD_DIM)
    y_inter = jnp.einsum(
        "tgn,ngkp->tgkp", c_wide, state_four, precision=lax.Precision.HIGHEST
    ).reshape(block_len, head_count, HEAD_DIM)
    output_pre = y_local + y_inter * from_start.T[:, :, None]
    gate_wide = gate_vals.astype(jnp.float32)
    gate_sig = jax.nn.sigmoid(gate_wide)
    grad_gate = (
        dout_vals.astype(jnp.float32) * output_pre * gate_sig * (1.0 + gate_wide * (1.0 - gate_sig))
    ).astype(jnp.bfloat16)
    x_inter = jnp.einsum(
        "sgn,ngkp->sgkp", b_wide, adjoint_four, precision=lax.Precision.HIGHEST
    ).reshape(block_len, head_count, HEAD_DIM)
    grad_vals = vals_local + x_inter * to_end.T[:, :, None]
    dy_scaled = (dy_wide * from_start.T[:, :, None]).reshape(
        block_len, group_count, per_group, HEAD_DIM
    )
    x_scaled = (x_wide * to_end.T[:, :, None]).reshape(block_len, group_count, per_group, HEAD_DIM)
    c_grad = c_local + jnp.einsum(
        "tgkp,ngkp->tgn", dy_scaled, state_four, precision=lax.Precision.HIGHEST
    )
    b_grad = b_local + jnp.einsum(
        "sgkp,ngkp->sgn", x_scaled, adjoint_four, precision=lax.Precision.HIGHEST
    )
    return (grad_vals.astype(jnp.bfloat16), grad_gate, jnp.stack([b_grad, c_grad], axis=1))


def chain(earlier, later):
    return (earlier[0] * later[0], earlier[1] * jnp.repeat(later[0], HEAD_DIM)[None, :] + later[1])


def body(hidden_in, proj_weight, values_in, gate_in, log_decay, skip_gain, grad_out):
    tokens = hidden_in[0]
    tok_rows = tokens.shape[0]
    weight_local = proj_weight.reshape(proj_weight.shape[0], -1)
    col_count = weight_local.shape[1]
    inner_count = lax.axis_size(INNER)
    outer_count = lax.axis_size(OUTER)
    weight_inner = lax.all_to_all(
        jnp.broadcast_to(weight_local[None], (inner_count,) + weight_local.shape),
        INNER,
        0,
        0,
        tiled=True,
    )
    weight_full = lax.all_to_all(
        jnp.broadcast_to(weight_inner[None], (outer_count,) + weight_inner.shape),
        OUTER,
        0,
        0,
        tiled=True,
    ).reshape(-1, col_count)
    bc_sums = jnp.dot(tokens, weight_full, preferred_element_type=jnp.float32)
    group_count = col_count // (2 * STATE)
    head_count = values_in.shape[2] // HEAD_DIM
    nblocks = tok_rows // SPAN
    bc_vals = bc_sums.astype(jnp.bfloat16).reshape(nblocks, SPAN, 2, group_count, STATE)
    x_vals = values_in[0].reshape(nblocks, SPAN, head_count, HEAD_DIM)
    gate_vals = gate_in[0].reshape(nblocks, SPAN, head_count, HEAD_DIM)
    dout_vals = grad_out[0].reshape(nblocks, SPAN, head_count, HEAD_DIM)
    dy_round = (dout_vals.astype(jnp.float32) * jax.nn.silu(gate_vals.astype(jnp.float32))).astype(
        jnp.bfloat16
    )
    rate_vals = log_decay[0].reshape(head_count, nblocks, SPAN)
    assert nblocks == 1
    dev_log = jnp.sum(jnp.cumsum(rate_vals, axis=2)[:, :, -1], axis=1)
    ctx_count = lax.axis_size(CTX)
    state_rows, adjoint_rows = summary_rows(
        bc_vals[0, :, 0], bc_vals[0, :, 1], x_vals[0], dy_round[0], rate_vals[:, 0], ctx_count
    )
    state_start, adjoint_end = carried_both(
        dev_log, state_rows, adjoint_rows, CTX, STATE, head_count * HEAD_DIM
    )
    states_in = state_start
    adjoints_out = [adjoint_end]
    results = [
        span_full(
            bc_vals[0, :, 0],
            bc_vals[0, :, 1],
            x_vals[0],
            dy_round[0],
            rate_vals[:, 0],
            skip_gain,
            states_in,
            adjoints_out[0],
            dout_vals[0],
            gate_vals[0],
        )
    ]
    grad_values = jnp.concatenate([entry[0] for entry in results], axis=0).reshape(
        1, tok_rows, head_count * HEAD_DIM
    )
    grad_gate = jnp.concatenate([entry[1] for entry in results], axis=0).reshape(
        1, tok_rows, head_count * HEAD_DIM
    )
    grad_flat = (
        jnp.concatenate([entry[2] for entry in results], axis=0)
        .reshape(tok_rows, col_count)
        .astype(jnp.bfloat16)
    )
    input_terms = jnp.einsum(
        "tc,dc->td", grad_flat, weight_full, preferred_element_type=jnp.float32
    )
    grad_input = lax.psum_scatter(
        input_terms.astype(jnp.bfloat16), "head", scatter_dimension=1, tiled=True
    )[None]
    scale = 1.0 / (lax.axis_size(ROWS) * tok_rows)
    proj_terms = jnp.einsum("tc,td->cd", grad_flat, tokens, preferred_element_type=jnp.float32)
    proj_parts = lax.all_to_all(
        proj_terms.reshape(col_count, outer_count, -1), OUTER, 1, 1, tiled=True
    ).sum(axis=1)
    proj_parts = lax.all_to_all(
        proj_parts.reshape(col_count, inner_count, -1), INNER, 1, 1, tiled=True
    )
    proj_parts = proj_parts.sum(axis=1).T[None]
    grad_proj = proj_parts.sum(axis=0) * scale
    grad_proj = grad_proj.reshape(-1, 2, col_count // 2)
    return (grad_input, grad_values, grad_gate, grad_proj)


def solution(mesh):
    sizes = tuple(size for _, size in CTX_PARTS)
    fine = jax.sharding.Mesh(
        mesh.devices.reshape(mesh.shape["dp"], *sizes, mesh.shape["head"]),
        ("dp",) + CTX + ("head",),
    )
    return jax.shard_map(
        body,
        mesh=fine,
        in_specs=(
            P("dp", CTX, None),
            P(ROWS, None, "head"),
            P("dp", CTX, "head"),
            P("dp", CTX, "head"),
            P("dp", "head", CTX),
            P("head"),
            P("dp", CTX, "head"),
        ),
        out_specs=(
            P("dp", CTX, "head"),
            P("dp", CTX, "head"),
            P("dp", CTX, "head"),
            P(ROWS, None, "head"),
        ),
        check_vma=False,
    )
```

```python
import jax
import jax.numpy as jnp
from jax import lax
from jax.sharding import PartitionSpec as P

HEAD_DIM = 64
STATE = 64
SPAN = 128
CTX_PARTS = (("ylo", 2), ("x", 4), ("z", 8))
CTX = tuple(name for name, _ in CTX_PARTS)
ROWS = ("dp",) + CTX
OUTER = ROWS[:-1]
INNER = ROWS[-1]


def carried_both(log_total, state_rows, adjoint_rows, axis, rows, cols):
    count = lax.axis_size(axis)
    chunk = cols // count
    assert HEAD_DIM % chunk == 0

    chunk_logs = jnp.repeat(log_total, cols // log_total.shape[0]).reshape(count, chunk)
    packed = jnp.concatenate(
        [state_rows, adjoint_rows, chunk_logs, jnp.zeros_like(chunk_logs)], 1
    )
    got = lax.all_to_all(packed[:, None], axis, 0, 0, tiled=True)[:, 0]
    logs = got[:, 2 * rows * chunk]
    place = jnp.arange(count)
    before = place[None, :] < place[:, None]
    gaps = jnp.dot(
        jnp.where(before, logs[None, :], 0.0),
        before.astype(jnp.float32),
        precision=lax.Precision.HIGHEST,
    )
    carry = jnp.where(before, jnp.exp(jnp.where(before, gaps, 0.0)), 0.0)
    flat = rows * chunk
    fwd = jnp.dot(carry, got[:, :flat], precision=lax.Precision.HIGHEST)
    bwd = jnp.dot(carry.T, got[:, flat : 2 * flat], precision=lax.Precision.HIGHEST)
    back = lax.all_to_all(jnp.concatenate([fwd, bwd], 1)[:, None], axis, 0, 0, tiled=True)
    back = back.reshape(count, 2, rows, chunk)
    return back[:, 0], back[:, 1]


def summary_rows(b_vals, c_vals, x_vals, dy_round, rate_vals, count):
    block_len = x_vals.shape[0]
    head_count = x_vals.shape[1]
    group_count = b_vals.shape[1]
    per_group = head_count // group_count
    chunk = head_count * HEAD_DIM // count
    cumlog = jnp.cumsum(rate_vals, axis=1)
    final_log = cumlog[:, -1]
    to_end = jnp.exp(final_log[:, None] - cumlog)
    from_start = jnp.exp(cumlog)
    shape = (block_len, group_count, per_group, HEAD_DIM // chunk, chunk)
    x_scaled = (x_vals.astype(jnp.float32) * to_end.T[:, :, None]).reshape(shape)
    dy_scaled = (dy_round.astype(jnp.float32) * from_start.T[:, :, None]).reshape(shape)
    state_part = jnp.einsum(
        "qgn,qgkhc->gkhnc", b_vals.astype(jnp.float32), x_scaled, precision=lax.Precision.HIGHEST
    )
    adjoint_part = jnp.einsum(
        "qgn,qgkhc->gkhnc", c_vals.astype(jnp.float32), dy_scaled, precision=lax.Precision.HIGHEST
    )
    return state_part.reshape(count, -1), adjoint_part.reshape(count, -1)


def span_summary(b_vals, c_vals, x_vals, dy_round, rate_vals):
    block_len = x_vals.shape[0]
    head_count = x_vals.shape[1]
    group_count = b_vals.shape[1]
    per_group = head_count // group_count
    cumlog = jnp.cumsum(rate_vals, axis=1)
    final_log = cumlog[:, -1]
    to_end = jnp.exp(final_log[:, None] - cumlog)
    from_start = jnp.exp(cumlog)
    b_wide = b_vals.astype(jnp.float32)
    c_wide = c_vals.astype(jnp.float32)
    x_scaled = (x_vals.astype(jnp.float32) * to_end.T[:, :, None]).reshape(
        block_len, group_count, per_group, HEAD_DIM
    )
    dy_scaled = (dy_round.astype(jnp.float32) * from_start.T[:, :, None]).reshape(
        block_len, group_count, per_group, HEAD_DIM
    )
    state_part = jnp.einsum("qgn,qgkp->ngkp", b_wide, x_scaled, precision=lax.Precision.HIGHEST)
    adjoint_part = jnp.einsum("qgn,qgkp->ngkp", c_wide, dy_scaled, precision=lax.Precision.HIGHEST)
    return (jnp.exp(final_log), state_part.reshape(STATE, -1), adjoint_part.reshape(STATE, -1))


def span_full(
    b_vals,
    c_vals,
    x_vals,
    dy_round,
    rate_vals,
    skip_vals,
    state_in,
    adjoint_out,
    dout_vals,
    gate_vals,
):
    block_len = x_vals.shape[0]
    head_count = x_vals.shape[1]
    group_count = b_vals.shape[1]
    per_group = head_count // group_count
    cumlog = jnp.cumsum(rate_vals, axis=1)
    final_log = cumlog[:, -1]
    to_end = jnp.exp(final_log[:, None] - cumlog)
    from_start = jnp.exp(cumlog)
    causal = jnp.arange(block_len)[:, None] >= jnp.arange(block_len)[None, :]
    log_gaps = cumlog[:, :, None] - cumlog[:, None, :]
    decays = jnp.where(causal[None], jnp.exp(jnp.where(causal[None], log_gaps, 0.0)), 0.0)
    b_wide = b_vals.astype(jnp.float32)
    c_wide = c_vals.astype(jnp.float32)
    cb_dots = jnp.einsum("tgn,sgn->gts", c_vals, b_vals, preferred_element_type=jnp.float32)
    mixer_bf = (decays * jnp.repeat(cb_dots, per_group, axis=0)).astype(jnp.bfloat16)
    x_wide = x_vals.astype(jnp.float32)
    dy_wide = dy_round.astype(jnp.float32)
    y_local = (
        jnp.einsum("hts,shp->thp", mixer_bf, x_vals, preferred_element_type=jnp.float32)
        + skip_vals[None, :, None] * x_wide
    )
    vals_local = (
        jnp.einsum("hts,thp->shp", mixer_bf, dy_round, preferred_element_type=jnp.float32)
        + skip_vals[None, :, None] * dy_wide
    )
    mix_grad = (
        jnp.einsum("thp,shp->hts", dy_round, x_vals, preferred_element_type=jnp.float32) * decays
    )
    dots_grad = (
        mix_grad.reshape(group_count, per_group, block_len, block_len)
        .sum(axis=1)
        .astype(jnp.bfloat16)
    )
    c_local = jnp.einsum("gts,sgn->tgn", dots_grad, b_vals, preferred_element_type=jnp.float32)
    b_local = jnp.einsum("gts,tgn->sgn", dots_grad, c_vals, preferred_element_type=jnp.float32)
    (y_local, vals_local, c_local, b_local), state_in, adjoint_out = lax.optimization_barrier(
        ((y_local, vals_local, c_local, b_local), state_in, adjoint_out)
    )
    width = state_in.shape[-1]
    state_five = state_in.reshape(group_count, per_group, HEAD_DIM // width, STATE, width)
    adjoint_five = adjoint_out.reshape(group_count, per_group, HEAD_DIM // width, STATE, width)
    y_inter = jnp.einsum(
        "tgn,gkhnc->tgkhc", c_wide, state_five, precision=lax.Precision.HIGHEST
    ).reshape(block_len, head_count, HEAD_DIM)
    output_pre = y_local + y_inter * from_start.T[:, :, None]
    gate_wide = gate_vals.astype(jnp.float32)
    gate_sig = jax.nn.sigmoid(gate_wide)
    grad_gate = (
        dout_vals.astype(jnp.float32) * output_pre * gate_sig * (1.0 + gate_wide * (1.0 - gate_sig))
    ).astype(jnp.bfloat16)
    x_inter = jnp.einsum(
        "sgn,gkhnc->sgkhc", b_wide, adjoint_five, precision=lax.Precision.HIGHEST
    ).reshape(block_len, head_count, HEAD_DIM)
    grad_vals = vals_local + x_inter * to_end.T[:, :, None]
    dy_scaled = (dy_wide * from_start.T[:, :, None]).reshape(
        block_len, group_count, per_group, HEAD_DIM // width, width
    )
    x_scaled = (x_wide * to_end.T[:, :, None]).reshape(
        block_len, group_count, per_group, HEAD_DIM // width, width
    )
    c_grad = c_local + jnp.einsum(
        "tgkhc,gkhnc->tgn", dy_scaled, state_five, precision=lax.Precision.HIGHEST
    )
    b_grad = b_local + jnp.einsum(
        "sgkhc,gkhnc->sgn", x_scaled, adjoint_five, precision=lax.Precision.HIGHEST
    )
    return (grad_vals.astype(jnp.bfloat16), grad_gate, jnp.stack([b_grad, c_grad], axis=1))


def chain(earlier, later):
    return (earlier[0] * later[0], earlier[1] * jnp.repeat(later[0], HEAD_DIM)[None, :] + later[1])


def body(hidden_in, proj_weight, values_in, gate_in, log_decay, skip_gain, grad_out):
    tokens = hidden_in[0]
    tok_rows = tokens.shape[0]
    weight_local = proj_weight.reshape(proj_weight.shape[0], -1)
    col_count = weight_local.shape[1]
    inner_count = lax.axis_size(INNER)
    outer_count = lax.axis_size(OUTER)
    weight_inner = lax.all_to_all(
        jnp.broadcast_to(weight_local[None], (inner_count,) + weight_local.shape),
        INNER,
        0,
        0,
        tiled=True,
    )
    weight_full = lax.all_to_all(
        jnp.broadcast_to(weight_inner[None], (outer_count,) + weight_inner.shape),
        OUTER,
        0,
        0,
        tiled=True,
    ).reshape(-1, col_count)
    bc_sums = jnp.dot(tokens, weight_full, preferred_element_type=jnp.float32)
    group_count = col_count // (2 * STATE)
    head_count = values_in.shape[2] // HEAD_DIM
    nblocks = tok_rows // SPAN
    bc_vals = bc_sums.astype(jnp.bfloat16).reshape(nblocks, SPAN, 2, group_count, STATE)
    x_vals = values_in[0].reshape(nblocks, SPAN, head_count, HEAD_DIM)
    gate_vals = gate_in[0].reshape(nblocks, SPAN, head_count, HEAD_DIM)
    dout_vals = grad_out[0].reshape(nblocks, SPAN, head_count, HEAD_DIM)
    dy_round = (dout_vals.astype(jnp.float32) * jax.nn.silu(gate_vals.astype(jnp.float32))).astype(
        jnp.bfloat16
    )
    rate_vals = log_decay[0].reshape(head_count, nblocks, SPAN)
    assert nblocks == 1
    dev_log = jnp.sum(jnp.cumsum(rate_vals, axis=2)[:, :, -1], axis=1)
    ctx_count = lax.axis_size(CTX)
    state_rows, adjoint_rows = summary_rows(
        bc_vals[0, :, 0], bc_vals[0, :, 1], x_vals[0], dy_round[0], rate_vals[:, 0], ctx_count
    )
    state_start, adjoint_end = carried_both(
        dev_log, state_rows, adjoint_rows, CTX, STATE, head_count * HEAD_DIM
    )
    states_in = state_start
    adjoints_out = [adjoint_end]
    results = [
        span_full(
            bc_vals[0, :, 0],
            bc_vals[0, :, 1],
            x_vals[0],
            dy_round[0],
            rate_vals[:, 0],
            skip_gain,
            states_in,
            adjoints_out[0],
            dout_vals[0],
            gate_vals[0],
        )
    ]
    grad_values = jnp.concatenate([entry[0] for entry in results], axis=0).reshape(
        1, tok_rows, head_count * HEAD_DIM
    )
    grad_gate = jnp.concatenate([entry[1] for entry in results], axis=0).reshape(
        1, tok_rows, head_count * HEAD_DIM
    )
    grad_flat = (
        jnp.concatenate([entry[2] for entry in results], axis=0)
        .reshape(tok_rows, col_count)
        .astype(jnp.bfloat16)
    )
    input_terms = jnp.einsum(
        "tc,dc->td", grad_flat, weight_full, preferred_element_type=jnp.float32
    )
    grad_input = lax.psum_scatter(
        input_terms.astype(jnp.bfloat16), "head", scatter_dimension=1, tiled=True
    )[None]
    scale = 1.0 / (lax.axis_size(ROWS) * tok_rows)
    proj_terms = jnp.einsum("tc,td->cd", grad_flat, tokens, preferred_element_type=jnp.float32)
    proj_parts = lax.all_to_all(
        proj_terms.reshape(col_count, outer_count, -1), OUTER, 1, 1, tiled=True
    ).sum(axis=1)
    proj_parts = lax.all_to_all(
        proj_parts.reshape(col_count, inner_count, -1), INNER, 1, 1, tiled=True
    )
    proj_parts = proj_parts.sum(axis=1).T[None]
    grad_proj = proj_parts.sum(axis=0) * scale
    grad_proj = grad_proj.reshape(-1, 2, col_count // 2)
    return (grad_input, grad_values, grad_gate, grad_proj)


def solution(mesh):
    sizes = tuple(size for _, size in CTX_PARTS)
    fine = jax.sharding.Mesh(
        mesh.devices.reshape(mesh.shape["dp"], *sizes, mesh.shape["head"]),
        ("dp",) + CTX + ("head",),
    )
    return jax.shard_map(
        body,
        mesh=fine,
        in_specs=(
            P("dp", CTX, None),
            P(ROWS, None, "head"),
            P("dp", CTX, "head"),
            P("dp", CTX, "head"),
            P("dp", "head", CTX),
            P("head"),
            P("dp", CTX, "head"),
        ),
        out_specs=(
            P("dp", CTX, "head"),
            P("dp", CTX, "head"),
            P("dp", CTX, "head"),
            P(ROWS, None, "head"),
        ),
        check_vma=False,
    )
```

```python
import jax
import jax.numpy as jnp
from jax import lax
from jax.sharding import PartitionSpec as P

HEAD_DIM = 64
STATE = 64
SPAN = 128
CTX_PARTS = (("ylo", 2), ("x", 4), ("z", 8))
CTX = tuple(name for name, _ in CTX_PARTS)
ROWS = ("dp",) + CTX
OUTER = ROWS[:-1]
INNER = ROWS[-1]


def carried_both(log_total, state_rows, adjoint_rows, axis, rows, cols):
    count = lax.axis_size(axis)
    chunk = cols // count
    assert HEAD_DIM % chunk == 0

    chunk_logs = jnp.repeat(log_total, cols // log_total.shape[0]).reshape(count, chunk)
    packed = jnp.concatenate(
        [state_rows, adjoint_rows, chunk_logs, jnp.zeros_like(chunk_logs)], 1
    )
    got = lax.all_to_all(packed[:, None], axis, 0, 0, tiled=True)[:, 0]
    logs = got[:, 2 * rows * chunk]
    place = jnp.arange(count)
    before = place[None, :] < place[:, None]
    gaps = jnp.dot(
        jnp.where(before, logs[None, :], 0.0),
        before.astype(jnp.float32),
        precision=lax.Precision.HIGHEST,
    )
    carry = jnp.where(before, jnp.exp(jnp.where(before, gaps, 0.0)), 0.0)
    flat = rows * chunk
    fwd = jnp.dot(carry, got[:, :flat], precision=lax.Precision.HIGHEST)
    bwd = jnp.dot(carry.T, got[:, flat : 2 * flat], precision=lax.Precision.HIGHEST)
    back = lax.all_to_all(jnp.concatenate([fwd, bwd], 1)[:, None], axis, 0, 0, tiled=True)
    back = back.reshape(count, 2, rows, chunk)
    return back[:, 0], back[:, 1]


def summary_rows(b_vals, c_vals, x_vals, dy_round, rate_vals, count):
    block_len = x_vals.shape[0]
    head_count = x_vals.shape[1]
    group_count = b_vals.shape[1]
    per_group = head_count // group_count
    chunk = head_count * HEAD_DIM // count
    cumlog = jnp.cumsum(rate_vals, axis=1)
    final_log = cumlog[:, -1]
    to_end = jnp.exp(final_log[:, None] - cumlog)
    from_start = jnp.exp(cumlog)
    shape = (block_len, group_count, per_group, HEAD_DIM // chunk, chunk)
    x_scaled = (x_vals.astype(jnp.float32) * to_end.T[:, :, None]).reshape(shape)
    dy_scaled = (dy_round.astype(jnp.float32) * from_start.T[:, :, None]).reshape(shape)
    state_part = jnp.einsum(
        "qgn,qgkhc->gkhnc", b_vals.astype(jnp.float32), x_scaled, precision=lax.Precision.HIGHEST
    )
    adjoint_part = jnp.einsum(
        "qgn,qgkhc->gkhnc", c_vals.astype(jnp.float32), dy_scaled, precision=lax.Precision.HIGHEST
    )
    return state_part.reshape(count, -1), adjoint_part.reshape(count, -1)


def span_summary(b_vals, c_vals, x_vals, dy_round, rate_vals):
    block_len = x_vals.shape[0]
    head_count = x_vals.shape[1]
    group_count = b_vals.shape[1]
    per_group = head_count // group_count
    cumlog = jnp.cumsum(rate_vals, axis=1)
    final_log = cumlog[:, -1]
    to_end = jnp.exp(final_log[:, None] - cumlog)
    from_start = jnp.exp(cumlog)
    b_wide = b_vals.astype(jnp.float32)
    c_wide = c_vals.astype(jnp.float32)
    x_scaled = (x_vals.astype(jnp.float32) * to_end.T[:, :, None]).reshape(
        block_len, group_count, per_group, HEAD_DIM
    )
    dy_scaled = (dy_round.astype(jnp.float32) * from_start.T[:, :, None]).reshape(
        block_len, group_count, per_group, HEAD_DIM
    )
    state_part = jnp.einsum("qgn,qgkp->ngkp", b_wide, x_scaled, precision=lax.Precision.HIGHEST)
    adjoint_part = jnp.einsum("qgn,qgkp->ngkp", c_wide, dy_scaled, precision=lax.Precision.HIGHEST)
    return (jnp.exp(final_log), state_part.reshape(STATE, -1), adjoint_part.reshape(STATE, -1))


def span_full(
    b_vals,
    c_vals,
    x_vals,
    dy_round,
    rate_vals,
    skip_vals,
    state_in,
    adjoint_out,
    dout_vals,
    gate_vals,
):
    block_len = x_vals.shape[0]
    head_count = x_vals.shape[1]
    group_count = b_vals.shape[1]
    per_group = head_count // group_count
    cumlog = jnp.cumsum(rate_vals, axis=1)
    final_log = cumlog[:, -1]
    to_end = jnp.exp(final_log[:, None] - cumlog)
    from_start = jnp.exp(cumlog)
    causal = jnp.arange(block_len)[:, None] >= jnp.arange(block_len)[None, :]
    log_gaps = cumlog[:, :, None] - cumlog[:, None, :]
    decays = jnp.where(causal[None], jnp.exp(jnp.where(causal[None], log_gaps, 0.0)), 0.0)
    b_wide = b_vals.astype(jnp.float32)
    c_wide = c_vals.astype(jnp.float32)
    cb_dots = jnp.einsum("tgn,sgn->gts", c_vals, b_vals, preferred_element_type=jnp.float32)
    mixer_bf = (decays * jnp.repeat(cb_dots, per_group, axis=0)).astype(jnp.bfloat16)
    x_wide = x_vals.astype(jnp.float32)
    dy_wide = dy_round.astype(jnp.float32)
    y_local = (
        jnp.einsum("hts,shp->thp", mixer_bf, x_vals, preferred_element_type=jnp.float32)
        + skip_vals[None, :, None] * x_wide
    )
    vals_local = (
        jnp.einsum("hts,thp->shp", mixer_bf, dy_round, preferred_element_type=jnp.float32)
        + skip_vals[None, :, None] * dy_wide
    )
    mix_grad = (
        jnp.einsum("thp,shp->hts", dy_round, x_vals, preferred_element_type=jnp.float32) * decays
    )
    dots_grad = (
        mix_grad.reshape(group_count, per_group, block_len, block_len)
        .sum(axis=1)
        .astype(jnp.bfloat16)
    )
    c_local = jnp.einsum("gts,sgn->tgn", dots_grad, b_vals, preferred_element_type=jnp.float32)
    b_local = jnp.einsum("gts,tgn->sgn", dots_grad, c_vals, preferred_element_type=jnp.float32)
    (y_local, vals_local, c_local, b_local), state_in, adjoint_out = lax.optimization_barrier(
        ((y_local, vals_local, c_local, b_local), state_in, adjoint_out)
    )
    width = state_in.shape[-1]
    state_five = state_in.reshape(group_count, per_group, HEAD_DIM // width, STATE, width)
    adjoint_five = adjoint_out.reshape(group_count, per_group, HEAD_DIM // width, STATE, width)
    y_inter = jnp.einsum(
        "tgn,gkhnc->tgkhc", c_wide, state_five, precision=lax.Precision.HIGHEST
    ).reshape(block_len, head_count, HEAD_DIM)
    output_pre = y_local + y_inter * from_start.T[:, :, None]
    gate_wide = gate_vals.astype(jnp.float32)
    gate_sig = jax.nn.sigmoid(gate_wide)
    grad_gate = (
        dout_vals.astype(jnp.float32) * output_pre * gate_sig * (1.0 + gate_wide * (1.0 - gate_sig))
    ).astype(jnp.bfloat16)
    x_inter = jnp.einsum(
        "sgn,gkhnc->sgkhc", b_wide, adjoint_five, precision=lax.Precision.HIGHEST
    ).reshape(block_len, head_count, HEAD_DIM)
    grad_vals = vals_local + x_inter * to_end.T[:, :, None]
    dy_scaled = (dy_wide * from_start.T[:, :, None]).reshape(
        block_len, group_count, per_group, HEAD_DIM // width, width
    )
    x_scaled = (x_wide * to_end.T[:, :, None]).reshape(
        block_len, group_count, per_group, HEAD_DIM // width, width
    )
    c_grad = c_local + jnp.einsum(
        "tgkhc,gkhnc->tgn", dy_scaled, state_five, precision=lax.Precision.HIGHEST
    )
    b_grad = b_local + jnp.einsum(
        "sgkhc,gkhnc->sgn", x_scaled, adjoint_five, precision=lax.Precision.HIGHEST
    )
    return (grad_vals.astype(jnp.bfloat16), grad_gate, jnp.stack([b_grad, c_grad], axis=1))


def chain(earlier, later):
    return (earlier[0] * later[0], earlier[1] * jnp.repeat(later[0], HEAD_DIM)[None, :] + later[1])


def body(hidden_in, proj_weight, values_in, gate_in, log_decay, skip_gain, grad_out):
    tokens = hidden_in[0]
    tok_rows = tokens.shape[0]
    weight_local = proj_weight.reshape(proj_weight.shape[0], -1)
    col_count = weight_local.shape[1]
    inner_count = lax.axis_size(INNER)
    outer_count = lax.axis_size(OUTER)
    weight_inner = lax.all_to_all(
        jnp.broadcast_to(weight_local[None], (inner_count,) + weight_local.shape),
        INNER,
        0,
        0,
        tiled=True,
    )
    weight_full = lax.all_to_all(
        jnp.broadcast_to(weight_inner[None], (outer_count,) + weight_inner.shape),
        OUTER,
        0,
        0,
        tiled=True,
    ).reshape(-1, col_count)
    bc_sums = jnp.dot(tokens, weight_full, preferred_element_type=jnp.float32)
    group_count = col_count // (2 * STATE)
    head_count = values_in.shape[2] // HEAD_DIM
    nblocks = tok_rows // SPAN
    bc_vals = bc_sums.astype(jnp.bfloat16).reshape(nblocks, SPAN, 2, group_count, STATE)
    x_vals = values_in[0].reshape(nblocks, SPAN, head_count, HEAD_DIM)
    gate_vals = gate_in[0].reshape(nblocks, SPAN, head_count, HEAD_DIM)
    dout_vals = grad_out[0].reshape(nblocks, SPAN, head_count, HEAD_DIM)
    dy_round = (dout_vals.astype(jnp.float32) * jax.nn.silu(gate_vals.astype(jnp.float32))).astype(
        jnp.bfloat16
    )
    rate_vals = log_decay[0].reshape(head_count, nblocks, SPAN)
    assert nblocks == 1
    dev_log = jnp.sum(jnp.cumsum(rate_vals, axis=2)[:, :, -1], axis=1)
    ctx_count = lax.axis_size(CTX)
    state_rows, adjoint_rows = summary_rows(
        bc_vals[0, :, 0], bc_vals[0, :, 1], x_vals[0], dy_round[0], rate_vals[:, 0], ctx_count
    )
    state_start, adjoint_end = carried_both(
        dev_log, state_rows, adjoint_rows, CTX, STATE, head_count * HEAD_DIM
    )
    states_in = state_start
    adjoints_out = [adjoint_end]
    results = [
        span_full(
            bc_vals[0, :, 0],
            bc_vals[0, :, 1],
            x_vals[0],
            dy_round[0],
            rate_vals[:, 0],
            skip_gain,
            states_in,
            adjoints_out[0],
            dout_vals[0],
            gate_vals[0],
        )
    ]
    grad_values = jnp.concatenate([entry[0] for entry in results], axis=0).reshape(
        1, tok_rows, head_count * HEAD_DIM
    )
    grad_gate = jnp.concatenate([entry[1] for entry in results], axis=0).reshape(
        1, tok_rows, head_count * HEAD_DIM
    )
    grad_flat = (
        jnp.concatenate([entry[2] for entry in results], axis=0)
        .reshape(tok_rows, col_count)
        .astype(jnp.bfloat16)
    )
    input_terms = jnp.einsum(
        "tc,dc->td", grad_flat, weight_full, preferred_element_type=jnp.float32
    )
    grad_input = lax.psum_scatter(
        input_terms.astype(jnp.bfloat16), "head", scatter_dimension=1, tiled=True
    )[None]
    scale = 1.0 / (lax.axis_size(ROWS) * tok_rows)
    tokens_z = (
        tokens.reshape(tok_rows, outer_count, inner_count, -1)
        .transpose(0, 2, 1, 3)
        .reshape(tok_rows, -1)
    )
    proj_terms = jnp.einsum("tc,td->cd", grad_flat, tokens_z, preferred_element_type=jnp.float32)
    proj_parts = lax.all_to_all(
        proj_terms.reshape(col_count, inner_count, -1), INNER, 1, 1, tiled=True
    ).sum(axis=1)
    proj_parts = lax.all_to_all(
        proj_parts.T.reshape(outer_count, -1, col_count), OUTER, 0, 0, tiled=True
    )
    grad_proj = proj_parts.sum(axis=0) * scale
    grad_proj = grad_proj.reshape(-1, 2, col_count // 2)
    return (grad_input, grad_values, grad_gate, grad_proj)


def solution(mesh):
    sizes = tuple(size for _, size in CTX_PARTS)
    fine = jax.sharding.Mesh(
        mesh.devices.reshape(mesh.shape["dp"], *sizes, mesh.shape["head"]),
        ("dp",) + CTX + ("head",),
    )
    return jax.shard_map(
        body,
        mesh=fine,
        in_specs=(
            P("dp", CTX, None),
            P(ROWS, None, "head"),
            P("dp", CTX, "head"),
            P("dp", CTX, "head"),
            P("dp", "head", CTX),
            P("head"),
            P("dp", CTX, "head"),
        ),
        out_specs=(
            P("dp", CTX, "head"),
            P("dp", CTX, "head"),
            P("dp", CTX, "head"),
            P(ROWS, None, "head"),
        ),
        check_vma=False,
    )
```

```python
import jax
import jax.numpy as jnp
from jax import lax
from jax.sharding import PartitionSpec as P

HEAD_DIM = 64
STATE = 64
SPAN = 128
CTX_PARTS = (("ylo", 2), ("x", 4), ("z", 8))
CTX = tuple(name for name, _ in CTX_PARTS)
ROWS = ("dp",) + CTX
OUTER = ROWS[:-1]
INNER = ROWS[-1]


def carried_both(log_total, state_rows, adjoint_rows, axis, rows, cols):
    count = lax.axis_size(axis)
    chunk = cols // count
    assert HEAD_DIM % chunk == 0

    chunk_logs = jnp.repeat(log_total, cols // log_total.shape[0]).reshape(count, chunk)
    packed = jnp.concatenate(
        [state_rows, adjoint_rows, chunk_logs, jnp.zeros_like(chunk_logs)], 1
    )
    got = lax.all_to_all(packed[:, None], axis, 0, 0, tiled=True)[:, 0]
    logs = got[:, 2 * rows * chunk]
    place = jnp.arange(count)
    before = place[None, :] < place[:, None]
    gaps = jnp.dot(
        jnp.where(before, logs[None, :], 0.0),
        before.astype(jnp.float32),
        precision=lax.Precision.HIGHEST,
    )
    carry = jnp.where(before, jnp.exp(jnp.where(before, gaps, 0.0)), 0.0)
    flat = rows * chunk
    fwd = jnp.dot(carry, got[:, :flat], precision=lax.Precision.HIGHEST)
    bwd = jnp.dot(carry.T, got[:, flat : 2 * flat], precision=lax.Precision.HIGHEST)
    back = lax.all_to_all(jnp.concatenate([fwd, bwd], 1)[:, None], axis, 0, 0, tiled=True)
    back = back.reshape(count, 2, rows, chunk)
    return back[:, 0], back[:, 1]


def summary_rows(b_vals, c_vals, x_vals, dy_round, rate_vals, count):
    block_len = x_vals.shape[0]
    head_count = x_vals.shape[1]
    group_count = b_vals.shape[1]
    per_group = head_count // group_count
    chunk = head_count * HEAD_DIM // count
    cumlog = jnp.cumsum(rate_vals, axis=1)
    final_log = cumlog[:, -1]
    to_end = jnp.exp(final_log[:, None] - cumlog)
    from_start = jnp.exp(cumlog)
    shape = (block_len, group_count, per_group, HEAD_DIM // chunk, chunk)
    x_scaled = (x_vals.astype(jnp.float32) * to_end.T[:, :, None]).reshape(shape)
    dy_scaled = (dy_round.astype(jnp.float32) * from_start.T[:, :, None]).reshape(shape)
    state_part = jnp.einsum(
        "qgn,qgkhc->gkhnc", b_vals.astype(jnp.float32), x_scaled, precision=lax.Precision.HIGHEST
    )
    adjoint_part = jnp.einsum(
        "qgn,qgkhc->gkhnc", c_vals.astype(jnp.float32), dy_scaled, precision=lax.Precision.HIGHEST
    )
    return state_part.reshape(count, -1), adjoint_part.reshape(count, -1)


def span_summary(b_vals, c_vals, x_vals, dy_round, rate_vals):
    block_len = x_vals.shape[0]
    head_count = x_vals.shape[1]
    group_count = b_vals.shape[1]
    per_group = head_count // group_count
    cumlog = jnp.cumsum(rate_vals, axis=1)
    final_log = cumlog[:, -1]
    to_end = jnp.exp(final_log[:, None] - cumlog)
    from_start = jnp.exp(cumlog)
    b_wide = b_vals.astype(jnp.float32)
    c_wide = c_vals.astype(jnp.float32)
    x_scaled = (x_vals.astype(jnp.float32) * to_end.T[:, :, None]).reshape(
        block_len, group_count, per_group, HEAD_DIM
    )
    dy_scaled = (dy_round.astype(jnp.float32) * from_start.T[:, :, None]).reshape(
        block_len, group_count, per_group, HEAD_DIM
    )
    state_part = jnp.einsum("qgn,qgkp->ngkp", b_wide, x_scaled, precision=lax.Precision.HIGHEST)
    adjoint_part = jnp.einsum("qgn,qgkp->ngkp", c_wide, dy_scaled, precision=lax.Precision.HIGHEST)
    return (jnp.exp(final_log), state_part.reshape(STATE, -1), adjoint_part.reshape(STATE, -1))


def span_full(
    b_vals,
    c_vals,
    x_vals,
    dy_round,
    rate_vals,
    skip_vals,
    state_in,
    adjoint_out,
    dout_vals,
    gate_vals,
):
    block_len = x_vals.shape[0]
    head_count = x_vals.shape[1]
    group_count = b_vals.shape[1]
    per_group = head_count // group_count
    cumlog = jnp.cumsum(rate_vals, axis=1)
    final_log = cumlog[:, -1]
    to_end = jnp.exp(final_log[:, None] - cumlog)
    from_start = jnp.exp(cumlog)
    causal = jnp.arange(block_len)[:, None] >= jnp.arange(block_len)[None, :]
    log_gaps = cumlog[:, :, None] - cumlog[:, None, :]
    decays = jnp.where(causal[None], jnp.exp(jnp.where(causal[None], log_gaps, 0.0)), 0.0)
    b_wide = b_vals.astype(jnp.float32)
    c_wide = c_vals.astype(jnp.float32)
    cb_dots = jnp.einsum("tgn,sgn->gts", c_vals, b_vals, preferred_element_type=jnp.float32)
    mixer_bf = (decays * jnp.repeat(cb_dots, per_group, axis=0)).astype(jnp.bfloat16)
    x_wide = x_vals.astype(jnp.float32)
    dy_wide = dy_round.astype(jnp.float32)
    y_local = (
        jnp.einsum("hts,shp->thp", mixer_bf, x_vals, preferred_element_type=jnp.float32)
        + skip_vals[None, :, None] * x_wide
    )
    vals_local = (
        jnp.einsum("hts,thp->shp", mixer_bf, dy_round, preferred_element_type=jnp.float32)
        + skip_vals[None, :, None] * dy_wide
    )
    mix_grad = (
        jnp.einsum("thp,shp->hts", dy_round, x_vals, preferred_element_type=jnp.float32) * decays
    )
    dots_grad = (
        mix_grad.reshape(group_count, per_group, block_len, block_len)
        .sum(axis=1)
        .astype(jnp.bfloat16)
    )
    c_local = jnp.einsum("gts,sgn->tgn", dots_grad, b_vals, preferred_element_type=jnp.float32)
    b_local = jnp.einsum("gts,tgn->sgn", dots_grad, c_vals, preferred_element_type=jnp.float32)
    (y_local, vals_local, c_local, b_local), state_in, adjoint_out = lax.optimization_barrier(
        ((y_local, vals_local, c_local, b_local), state_in, adjoint_out)
    )
    width = state_in.shape[-1]
    state_five = state_in.reshape(group_count, per_group, HEAD_DIM // width, STATE, width)
    adjoint_five = adjoint_out.reshape(group_count, per_group, HEAD_DIM // width, STATE, width)
    y_inter = jnp.einsum(
        "tgn,gkhnc->tgkhc", c_wide, state_five, precision=lax.Precision.HIGHEST
    ).reshape(block_len, head_count, HEAD_DIM)
    output_pre = y_local + y_inter * from_start.T[:, :, None]
    gate_wide = gate_vals.astype(jnp.float32)
    gate_sig = jax.nn.sigmoid(gate_wide)
    grad_gate = (
        dout_vals.astype(jnp.float32) * output_pre * gate_sig * (1.0 + gate_wide * (1.0 - gate_sig))
    ).astype(jnp.bfloat16)
    x_inter = jnp.einsum(
        "sgn,gkhnc->sgkhc", b_wide, adjoint_five, precision=lax.Precision.HIGHEST
    ).reshape(block_len, head_count, HEAD_DIM)
    grad_vals = vals_local + x_inter * to_end.T[:, :, None]
    dy_scaled = (dy_wide * from_start.T[:, :, None]).reshape(
        block_len, group_count, per_group, HEAD_DIM // width, width
    )
    x_scaled = (x_wide * to_end.T[:, :, None]).reshape(
        block_len, group_count, per_group, HEAD_DIM // width, width
    )
    c_grad = c_local + jnp.einsum(
        "tgkhc,gkhnc->tgn", dy_scaled, state_five, precision=lax.Precision.HIGHEST
    )
    b_grad = b_local + jnp.einsum(
        "sgkhc,gkhnc->sgn", x_scaled, adjoint_five, precision=lax.Precision.HIGHEST
    )
    return (grad_vals.astype(jnp.bfloat16), grad_gate, jnp.stack([b_grad, c_grad], axis=1))


def chain(earlier, later):
    return (earlier[0] * later[0], earlier[1] * jnp.repeat(later[0], HEAD_DIM)[None, :] + later[1])


def body(hidden_in, proj_weight, values_in, gate_in, log_decay, skip_gain, grad_out):
    tokens = hidden_in[0]
    tok_rows = tokens.shape[0]
    weight_local = proj_weight.reshape(proj_weight.shape[0], -1)
    col_count = weight_local.shape[1]
    inner_count = lax.axis_size(INNER)
    outer_count = lax.axis_size(OUTER)
    weight_inner = lax.all_gather(weight_local, INNER, axis=0)
    weight_full = lax.all_to_all(
        jnp.broadcast_to(weight_inner[None], (outer_count,) + weight_inner.shape),
        OUTER,
        0,
        0,
        tiled=True,
    ).reshape(-1, col_count)
    bc_sums = jnp.dot(tokens, weight_full, preferred_element_type=jnp.float32)
    group_count = col_count // (2 * STATE)
    head_count = values_in.shape[2] // HEAD_DIM
    nblocks = tok_rows // SPAN
    bc_vals = bc_sums.astype(jnp.bfloat16).reshape(nblocks, SPAN, 2, group_count, STATE)
    x_vals = values_in[0].reshape(nblocks, SPAN, head_count, HEAD_DIM)
    gate_vals = gate_in[0].reshape(nblocks, SPAN, head_count, HEAD_DIM)
    dout_vals = grad_out[0].reshape(nblocks, SPAN, head_count, HEAD_DIM)
    dy_round = (dout_vals.astype(jnp.float32) * jax.nn.silu(gate_vals.astype(jnp.float32))).astype(
        jnp.bfloat16
    )
    rate_vals = log_decay[0].reshape(head_count, nblocks, SPAN)
    assert nblocks == 1
    dev_log = jnp.sum(jnp.cumsum(rate_vals, axis=2)[:, :, -1], axis=1)
    ctx_count = lax.axis_size(CTX)
    state_rows, adjoint_rows = summary_rows(
        bc_vals[0, :, 0], bc_vals[0, :, 1], x_vals[0], dy_round[0], rate_vals[:, 0], ctx_count
    )
    state_start, adjoint_end = carried_both(
        dev_log, state_rows, adjoint_rows, CTX, STATE, head_count * HEAD_DIM
    )
    states_in = state_start
    adjoints_out = [adjoint_end]
    results = [
        span_full(
            bc_vals[0, :, 0],
            bc_vals[0, :, 1],
            x_vals[0],
            dy_round[0],
            rate_vals[:, 0],
            skip_gain,
            states_in,
            adjoints_out[0],
            dout_vals[0],
            gate_vals[0],
        )
    ]
    grad_values = jnp.concatenate([entry[0] for entry in results], axis=0).reshape(
        1, tok_rows, head_count * HEAD_DIM
    )
    grad_gate = jnp.concatenate([entry[1] for entry in results], axis=0).reshape(
        1, tok_rows, head_count * HEAD_DIM
    )
    grad_flat = (
        jnp.concatenate([entry[2] for entry in results], axis=0)
        .reshape(tok_rows, col_count)
        .astype(jnp.bfloat16)
    )
    input_terms = jnp.einsum(
        "tc,dc->td", grad_flat, weight_full, preferred_element_type=jnp.float32
    )
    grad_input = lax.psum_scatter(
        input_terms.astype(jnp.bfloat16), "head", scatter_dimension=1, tiled=True
    )[None]
    scale = 1.0 / (lax.axis_size(ROWS) * tok_rows)
    proj_terms = jnp.einsum("tc,td->cd", grad_flat, tokens, preferred_element_type=jnp.float32)
    proj_parts = lax.all_to_all(
        proj_terms.reshape(col_count, outer_count, -1), OUTER, 1, 1, tiled=True
    ).sum(axis=1)
    proj_parts = lax.all_to_all(
        proj_parts.reshape(col_count, inner_count, -1), INNER, 1, 1, tiled=True
    )
    proj_parts = proj_parts.sum(axis=1).T[None]
    grad_proj = proj_parts.sum(axis=0) * scale
    grad_proj = grad_proj.reshape(-1, 2, col_count // 2)
    return (grad_input, grad_values, grad_gate, grad_proj)


def solution(mesh):
    sizes = tuple(size for _, size in CTX_PARTS)
    fine = jax.sharding.Mesh(
        mesh.devices.reshape(mesh.shape["dp"], *sizes, mesh.shape["head"]),
        ("dp",) + CTX + ("head",),
    )
    return jax.shard_map(
        body,
        mesh=fine,
        in_specs=(
            P("dp", CTX, None),
            P(ROWS, None, "head"),
            P("dp", CTX, "head"),
            P("dp", CTX, "head"),
            P("dp", "head", CTX),
            P("head"),
            P("dp", CTX, "head"),
        ),
        out_specs=(
            P("dp", CTX, "head"),
            P("dp", CTX, "head"),
            P("dp", CTX, "head"),
            P(ROWS, None, "head"),
        ),
        check_vma=False,
    )
```

```python
import jax
import jax.numpy as jnp
from jax import lax
from jax.sharding import PartitionSpec as P

HEAD_DIM = 64
STATE = 64
SPAN = 128
CTX_PARTS = (("ylo", 2), ("x", 4), ("z", 8))
CTX = tuple(name for name, _ in CTX_PARTS)
ROWS = ("dp",) + CTX
OUTER = ROWS[:-1]
INNER = ROWS[-1]


def carried_both(log_total, state_rows, adjoint_rows, axis, rows, cols):
    count = lax.axis_size(axis)
    chunk = cols // count
    assert HEAD_DIM % chunk == 0

    chunk_logs = jnp.repeat(log_total, cols // log_total.shape[0]).reshape(count, chunk)
    packed = jnp.concatenate(
        [state_rows, adjoint_rows, chunk_logs, jnp.zeros_like(chunk_logs)], 1
    )
    got = lax.all_to_all(packed[:, None], axis, 0, 0, tiled=True)[:, 0]
    logs = got[:, 2 * rows * chunk]
    place = jnp.arange(count)
    before = place[None, :] < place[:, None]
    gaps = jnp.dot(
        jnp.where(before, logs[None, :], 0.0),
        before.astype(jnp.float32),
        precision=lax.Precision.HIGHEST,
    )
    carry = jnp.where(before, jnp.exp(jnp.where(before, gaps, 0.0)), 0.0)
    flat = rows * chunk
    fwd = jnp.dot(carry, got[:, :flat], precision=lax.Precision.HIGHEST)
    bwd = jnp.dot(carry.T, got[:, flat : 2 * flat], precision=lax.Precision.HIGHEST)
    back = lax.all_to_all(jnp.concatenate([fwd, bwd], 1)[:, None], axis, 0, 0, tiled=True)
    back = back.reshape(count, 2, rows, chunk)
    return back[:, 0], back[:, 1]


def summary_rows(b_vals, c_vals, x_vals, dy_round, rate_vals, count):
    block_len = x_vals.shape[0]
    head_count = x_vals.shape[1]
    group_count = b_vals.shape[1]
    per_group = head_count // group_count
    chunk = head_count * HEAD_DIM // count
    cumlog = jnp.cumsum(rate_vals, axis=1)
    final_log = cumlog[:, -1]
    to_end = jnp.exp(final_log[:, None] - cumlog)
    from_start = jnp.exp(cumlog)
    shape = (block_len, group_count, per_group, HEAD_DIM // chunk, chunk)
    x_scaled = (x_vals.astype(jnp.float32) * to_end.T[:, :, None]).reshape(shape)
    dy_scaled = (dy_round.astype(jnp.float32) * from_start.T[:, :, None]).reshape(shape)
    state_part = jnp.einsum(
        "qgn,qgkhc->gkhnc", b_vals.astype(jnp.float32), x_scaled, precision=lax.Precision.HIGHEST
    )
    adjoint_part = jnp.einsum(
        "qgn,qgkhc->gkhnc", c_vals.astype(jnp.float32), dy_scaled, precision=lax.Precision.HIGHEST
    )
    return state_part.reshape(count, -1), adjoint_part.reshape(count, -1)


def span_summary(b_vals, c_vals, x_vals, dy_round, rate_vals):
    block_len = x_vals.shape[0]
    head_count = x_vals.shape[1]
    group_count = b_vals.shape[1]
    per_group = head_count // group_count
    cumlog = jnp.cumsum(rate_vals, axis=1)
    final_log = cumlog[:, -1]
    to_end = jnp.exp(final_log[:, None] - cumlog)
    from_start = jnp.exp(cumlog)
    b_wide = b_vals.astype(jnp.float32)
    c_wide = c_vals.astype(jnp.float32)
    x_scaled = (x_vals.astype(jnp.float32) * to_end.T[:, :, None]).reshape(
        block_len, group_count, per_group, HEAD_DIM
    )
    dy_scaled = (dy_round.astype(jnp.float32) * from_start.T[:, :, None]).reshape(
        block_len, group_count, per_group, HEAD_DIM
    )
    state_part = jnp.einsum("qgn,qgkp->ngkp", b_wide, x_scaled, precision=lax.Precision.HIGHEST)
    adjoint_part = jnp.einsum("qgn,qgkp->ngkp", c_wide, dy_scaled, precision=lax.Precision.HIGHEST)
    return (jnp.exp(final_log), state_part.reshape(STATE, -1), adjoint_part.reshape(STATE, -1))


def span_full(
    b_vals,
    c_vals,
    x_vals,
    dy_round,
    rate_vals,
    skip_vals,
    state_in,
    adjoint_out,
    dout_vals,
    gate_vals,
):
    block_len = x_vals.shape[0]
    head_count = x_vals.shape[1]
    group_count = b_vals.shape[1]
    per_group = head_count // group_count
    cumlog = jnp.cumsum(rate_vals, axis=1)
    final_log = cumlog[:, -1]
    to_end = jnp.exp(final_log[:, None] - cumlog)
    from_start = jnp.exp(cumlog)
    causal = jnp.arange(block_len)[:, None] >= jnp.arange(block_len)[None, :]
    log_gaps = cumlog[:, :, None] - cumlog[:, None, :]
    decays = jnp.where(causal[None], jnp.exp(jnp.where(causal[None], log_gaps, 0.0)), 0.0)
    b_wide = b_vals.astype(jnp.float32)
    c_wide = c_vals.astype(jnp.float32)
    cb_dots = jnp.einsum("tgn,sgn->gts", c_vals, b_vals, preferred_element_type=jnp.float32)
    mixer_bf = (decays * jnp.repeat(cb_dots, per_group, axis=0)).astype(jnp.bfloat16)
    x_wide = x_vals.astype(jnp.float32)
    dy_wide = dy_round.astype(jnp.float32)
    y_local = (
        jnp.einsum("hts,shp->thp", mixer_bf, x_vals, preferred_element_type=jnp.float32)
        + skip_vals[None, :, None] * x_wide
    )
    vals_local = (
        jnp.einsum("hts,thp->shp", mixer_bf, dy_round, preferred_element_type=jnp.float32)
        + skip_vals[None, :, None] * dy_wide
    )
    mix_grad = (
        jnp.einsum("thp,shp->hts", dy_round, x_vals, preferred_element_type=jnp.float32) * decays
    )
    dots_grad = (
        mix_grad.reshape(group_count, per_group, block_len, block_len)
        .sum(axis=1)
        .astype(jnp.bfloat16)
    )
    c_local = jnp.einsum("gts,sgn->tgn", dots_grad, b_vals, preferred_element_type=jnp.float32)
    b_local = jnp.einsum("gts,tgn->sgn", dots_grad, c_vals, preferred_element_type=jnp.float32)
    (y_local, vals_local, c_local, b_local), state_in, adjoint_out = lax.optimization_barrier(
        ((y_local, vals_local, c_local, b_local), state_in, adjoint_out)
    )
    width = state_in.shape[-1]
    state_five = state_in.reshape(group_count, per_group, HEAD_DIM // width, STATE, width)
    adjoint_five = adjoint_out.reshape(group_count, per_group, HEAD_DIM // width, STATE, width)
    y_inter = jnp.einsum(
        "tgn,gkhnc->tgkhc", c_wide, state_five, precision=lax.Precision.HIGHEST
    ).reshape(block_len, head_count, HEAD_DIM)
    output_pre = y_local + y_inter * from_start.T[:, :, None]
    gate_wide = gate_vals.astype(jnp.float32)
    gate_sig = jax.nn.sigmoid(gate_wide)
    grad_gate = (
        dout_vals.astype(jnp.float32) * output_pre * gate_sig * (1.0 + gate_wide * (1.0 - gate_sig))
    ).astype(jnp.bfloat16)
    x_inter = jnp.einsum(
        "sgn,gkhnc->sgkhc", b_wide, adjoint_five, precision=lax.Precision.HIGHEST
    ).reshape(block_len, head_count, HEAD_DIM)
    grad_vals = vals_local + x_inter * to_end.T[:, :, None]
    dy_scaled = (dy_wide * from_start.T[:, :, None]).reshape(
        block_len, group_count, per_group, HEAD_DIM // width, width
    )
    x_scaled = (x_wide * to_end.T[:, :, None]).reshape(
        block_len, group_count, per_group, HEAD_DIM // width, width
    )
    c_grad = c_local + jnp.einsum(
        "tgkhc,gkhnc->tgn", dy_scaled, state_five, precision=lax.Precision.HIGHEST
    )
    b_grad = b_local + jnp.einsum(
        "sgkhc,gkhnc->sgn", x_scaled, adjoint_five, precision=lax.Precision.HIGHEST
    )
    return (grad_vals.astype(jnp.bfloat16), grad_gate, jnp.stack([b_grad, c_grad], axis=1))


def chain(earlier, later):
    return (earlier[0] * later[0], earlier[1] * jnp.repeat(later[0], HEAD_DIM)[None, :] + later[1])


def body(hidden_in, proj_weight, values_in, gate_in, log_decay, skip_gain, grad_out):
    tokens = hidden_in[0]
    tok_rows = tokens.shape[0]
    weight_local = proj_weight.reshape(proj_weight.shape[0], -1)
    col_count = weight_local.shape[1]
    inner_count = lax.axis_size(INNER)
    outer_count = lax.axis_size(OUTER)
    weight_inner = lax.all_gather(weight_local, INNER, axis=0)
    weight_full = lax.all_gather(weight_inner, OUTER, axis=0).reshape(-1, col_count)
    bc_sums = jnp.dot(tokens, weight_full, preferred_element_type=jnp.float32)
    group_count = col_count // (2 * STATE)
    head_count = values_in.shape[2] // HEAD_DIM
    nblocks = tok_rows // SPAN
    bc_vals = bc_sums.astype(jnp.bfloat16).reshape(nblocks, SPAN, 2, group_count, STATE)
    x_vals = values_in[0].reshape(nblocks, SPAN, head_count, HEAD_DIM)
    gate_vals = gate_in[0].reshape(nblocks, SPAN, head_count, HEAD_DIM)
    dout_vals = grad_out[0].reshape(nblocks, SPAN, head_count, HEAD_DIM)
    dy_round = (dout_vals.astype(jnp.float32) * jax.nn.silu(gate_vals.astype(jnp.float32))).astype(
        jnp.bfloat16
    )
    rate_vals = log_decay[0].reshape(head_count, nblocks, SPAN)
    assert nblocks == 1
    dev_log = jnp.sum(jnp.cumsum(rate_vals, axis=2)[:, :, -1], axis=1)
    ctx_count = lax.axis_size(CTX)
    state_rows, adjoint_rows = summary_rows(
        bc_vals[0, :, 0], bc_vals[0, :, 1], x_vals[0], dy_round[0], rate_vals[:, 0], ctx_count
    )
    state_start, adjoint_end = carried_both(
        dev_log, state_rows, adjoint_rows, CTX, STATE, head_count * HEAD_DIM
    )
    states_in = state_start
    adjoints_out = [adjoint_end]
    results = [
        span_full(
            bc_vals[0, :, 0],
            bc_vals[0, :, 1],
            x_vals[0],
            dy_round[0],
            rate_vals[:, 0],
            skip_gain,
            states_in,
            adjoints_out[0],
            dout_vals[0],
            gate_vals[0],
        )
    ]
    grad_values = jnp.concatenate([entry[0] for entry in results], axis=0).reshape(
        1, tok_rows, head_count * HEAD_DIM
    )
    grad_gate = jnp.concatenate([entry[1] for entry in results], axis=0).reshape(
        1, tok_rows, head_count * HEAD_DIM
    )
    grad_flat = (
        jnp.concatenate([entry[2] for entry in results], axis=0)
        .reshape(tok_rows, col_count)
        .astype(jnp.bfloat16)
    )
    input_terms = jnp.einsum(
        "tc,dc->td", grad_flat, weight_full, preferred_element_type=jnp.float32
    )
    grad_input = lax.psum_scatter(
        input_terms.astype(jnp.bfloat16), "head", scatter_dimension=1, tiled=True
    )[None]
    scale = 1.0 / (lax.axis_size(ROWS) * tok_rows)
    proj_terms = jnp.einsum("tc,td->cd", grad_flat, tokens, preferred_element_type=jnp.float32)
    proj_parts = lax.all_to_all(
        proj_terms.reshape(col_count, outer_count, -1), OUTER, 1, 1, tiled=True
    ).sum(axis=1)
    proj_parts = lax.all_to_all(
        proj_parts.reshape(col_count, inner_count, -1), INNER, 1, 1, tiled=True
    )
    proj_parts = proj_parts.sum(axis=1).T[None]
    grad_proj = proj_parts.sum(axis=0) * scale
    grad_proj = grad_proj.reshape(-1, 2, col_count // 2)
    return (grad_input, grad_values, grad_gate, grad_proj)


def solution(mesh):
    sizes = tuple(size for _, size in CTX_PARTS)
    fine = jax.sharding.Mesh(
        mesh.devices.reshape(mesh.shape["dp"], *sizes, mesh.shape["head"]),
        ("dp",) + CTX + ("head",),
    )
    return jax.shard_map(
        body,
        mesh=fine,
        in_specs=(
            P("dp", CTX, None),
            P(ROWS, None, "head"),
            P("dp", CTX, "head"),
            P("dp", CTX, "head"),
            P("dp", "head", CTX),
            P("head"),
            P("dp", CTX, "head"),
        ),
        out_specs=(
            P("dp", CTX, "head"),
            P("dp", CTX, "head"),
            P("dp", CTX, "head"),
            P(ROWS, None, "head"),
        ),
        check_vma=False,
    )
```
